768 devices in a mesh: ctx: 96 (over y, z), head: 8 (over x, core).
Axes of the slice: x: 4, y: 8, z: 12, core: 2. Of those that a mesh axis runs over, the one named last changes fastest.
Arguments:
- queries: bfloat16 [256, 12288], P('head', 'ctx'), may hold values from -6 to 6
- keys: bfloat16 [256, 12288], P('head', 'ctx'), may hold values from -6 to 6
- values: bfloat16 [12288, 2048], P('ctx', 'head'), may hold values from -6 to 6
- seg_ids: int32 [12288], P('ctx'), may hold values from 0 to 11, never falling along the last dimension, each value on 1 to 2048 neighbouring positions
- conv_weight: bfloat16 [3, 256], P(None, 'head'), may hold values from -3.5 to 3.5
- out_weight: bfloat16 [2048, 4096], P('head'), may hold values from -0.125 to 0.125
- out_grad: bfloat16 [12288, 4096], P('ctx', 'head'), may hold values from -6 to 6
Outputs:
- grad_queries: float32 [256, 12288], P('head', 'ctx')
- grad_keys: float32 [256, 12288], P('head', 'ctx')
- grad_values: float32 [12288, 2048], P('ctx', 'head')
The draws below stay inside these ranges and needn't reach their ends.
Inputs may be any that keep to these rules, and one draw needn't show every extreme that they name: `seg_ids`: document numbers never fall along the sequence; each document holds 1 to 2048 tokens, and one holds exactly 2048.
All inputs are finite; a program needn't handle non-finite values.
Results may differ from the reference program's by a relative error of at most 0.0005.
Values may be sent and summed in bfloat16 or wider, within the bound.
No kernel may reach another device: no remote copies, remote signals or barrier semaphores. Data moves between devices by JAX's collectives and lax.ppermute only.
A program may use at most 64 MiB of HBM per device.

```python
import math
import jax
import jax.numpy as jnp
import numpy as np
from jax import lax

D = 4096
HEADS = 16
HD = 128
FD = 16
TOK_DEV = 128
NF = 153
QK = 256
HV = 2048
SEQ = 12288
MOST = 2048
DOCS = 12


def steps_of(stream_key, extent, pieces, smallest, largest):
    factor_of = 1.0
    for position, blocks in pieces:
        steps = jax.random.uniform(jax.random.fold_in(jax.random.fold_in(stream_key, 6), position), (blocks,), jnp.float32, smallest / len(pieces), largest / len(pieces))
        factor_of = factor_of * jnp.repeat(jnp.exp(steps), extent[position] // blocks).reshape((-1,) + (1,) * (len(extent) - 1 - position))
    return factor_of


def split_up(amount, total, reach, slope):
    portions = [(1 << 20) // math.isqrt(grade ** slope) + 1 for grade in range(2, amount + 1)]
    surplus, given = total - reach - (amount - 1), [1] * (amount - 1)
    while surplus > 0:
        candidates = [i for i in range(amount - 1) if given[i] < reach]
        pool, left = sum([portions[i] for i in candidates]), surplus
        for i in candidates:
            addition = min(reach - given[i], max(1, left * portions[i] // pool), surplus)
            given[i] = given[i] + addition
            surplus = surplus - addition
    return np.array([reach] + given)


def uneven(stream_key, count, total, limit, slope):
    if count == 2:
        one = jax.random.randint(stream_key, (), max(1, total - limit), min(limit, total - 1) + 1)
        return jnp.stack([one, total - one])
    tallies = jnp.asarray(split_up(count, total, limit, slope), jnp.int32)
    twos = (count - 1) // 2
    donor, taker = tallies[1:1 + 2 * twos:2], tallies[2:2 + 2 * twos:2]
    slack = jnp.minimum(donor - 1, limit - taker)
    moved = jax.random.randint(jax.random.fold_in(stream_key, 1), (twos,), 0, 1 << 20) % (slack + 1)
    tallies = tallies.at[1:1 + 2 * twos:2].set(donor - moved).at[2:2 + 2 * twos:2].set(taker + moved)
    return tallies[jax.random.permutation(jax.random.fold_in(stream_key, 2), count)]


def scatter_about(rng, dims, deviation, bound, split=(), kind=jnp.bfloat16):
    values = jax.random.normal(rng, dims, jnp.float32) * deviation
    if len(split) > 0:
        values = steps_of(rng, dims, split, -0.22, 0.18) * values
    return jnp.clip(values, min=-bound, max=bound).astype(kind)


def setup_inputs(seed: int = 0) -> dict:
    seeds = jax.random.split(jax.random.key(seed), 8)
    queries = scatter_about(seeds[0], (QK, SEQ), 1.0, 6.0, ((0, 8), (1, 96)))
    keys = scatter_about(seeds[1], (QK, SEQ), 1.0, 6.0, ((0, 8), (1, 96)))
    values = scatter_about(seeds[2], (SEQ, HV), 1.0, 6.0, ((0, 96), (1, 8)))
    seg_ids = jnp.searchsorted(jnp.cumsum(uneven(seeds[3], DOCS, SEQ, MOST, 2)), jnp.arange(SEQ), side="right").astype(jnp.int32)
    conv_weight = scatter_about(seeds[4], (3, QK), 3 ** -0.5, 3.5, ((1, 8),))
    out_weight = scatter_about(seeds[5], (HV, D), HV ** -0.5, 0.125, ((0, 8),))
    out_grad = scatter_about(seeds[6], (SEQ, D), 1.0, 6.0, ((0, 96), (1, 8)))
    return dict(queries=queries, keys=keys, values=values, seg_ids=seg_ids, conv_weight=conv_weight, out_weight=out_weight, out_grad=out_grad)


half_root = 0.7071067811865476
exact_mode = lax.Precision.HIGHEST

def features(entries):
    scaled = entries * 0.5
    row_index, col_index = np.triu_indices(scaled.shape[-2], 1)
    cross = jnp.take(scaled, row_index, axis=-2) * jnp.take(scaled, col_index, axis=-2)
    return jnp.concatenate([jnp.ones_like(scaled[..., :1, :]), scaled, scaled * scaled * half_root, cross], axis=-2)

def block_output(q_feat, k_feat, head_values, doc_ids, carry_mask, state_in, normer_in):
    length = doc_ids.shape[0]
    causal = jnp.arange(length)[:, None] >= jnp.arange(length)[None, :]
    allowed = (causal & (doc_ids[:, None] == doc_ids[None, :])).astype(jnp.float32)
    scores = jnp.einsum('hft,hfs->hts', q_feat, k_feat, precision=exact_mode) * allowed[None, :, :]
    numerator = jnp.einsum('hts,shd->thd', scores, head_values, precision=exact_mode)
    numerator = numerator + carry_mask[:, None, None] * jnp.einsum('hft,hfd->thd', q_feat, state_in, precision=exact_mode)
    denominator = lax.optimization_barrier(jnp.sum(scores, axis=2)).T + carry_mask[:, None] * jnp.einsum('hft,hf->th', q_feat, normer_in, precision=exact_mode)
    return numerator / denominator[:, :, None]

def convolve(query_rows, taps, doc_ids):
    summed = taps[0][:, None] * query_rows
    for offset in (1, 2):
        shifted = jnp.pad(query_rows, ((0, 0), (offset, 0)))[:, :-offset]
        shifted_ids = jnp.pad(doc_ids, (offset, 0), constant_values=-1)[:-offset]
        same_doc = (shifted_ids == doc_ids).astype(jnp.float32)
        summed = summed + taps[offset][:, None] * shifted * same_doc[None, :]
    return summed

def attention(q_conv, key_rows, value_cols, doc_ids):
    blocks = SEQ // TOK_DEV
    q_blocks = q_conv.reshape(HEADS, FD, blocks, TOK_DEV).transpose(2, 0, 1, 3)
    k_blocks = key_rows.reshape(HEADS, FD, blocks, TOK_DEV).transpose(2, 0, 1, 3)
    v_blocks = value_cols.reshape(blocks, TOK_DEV, HEADS, HD)
    id_blocks = doc_ids.reshape(blocks, TOK_DEV)

    def advance(carry, block):
        state_in, normer_in, last_id = carry
        q_block, k_block, v_block, id_block = block
        q_feat = features(q_block)
        k_feat = features(k_block)
        carry_mask = (id_block == last_id).astype(jnp.float32)
        result = block_output(q_feat, k_feat, v_block, id_block, carry_mask, state_in, normer_in)
        block_last = id_block[TOK_DEV - 1]
        tail_mask = (id_block == block_last).astype(jnp.float32)
        keep_old = (last_id == block_last).astype(jnp.float32)
        tail_feat = k_feat * tail_mask[None, None, :]
        new_state = keep_old * state_in + jnp.einsum('hfs,shd->hfd', tail_feat, v_block, precision=exact_mode)
        new_normer = keep_old * normer_in + lax.optimization_barrier(jnp.sum(tail_feat, axis=2))
        return ((new_state, new_normer, block_last), result.reshape(TOK_DEV, HEADS * HD))
    start_carry = (jnp.zeros((HEADS, NF, HD), jnp.float32), jnp.zeros((HEADS, NF), jnp.float32), jnp.int32(-1))
    _, outputs = lax.scan(jax.checkpoint(advance), start_carry, (q_blocks, k_blocks, v_blocks, id_blocks))
    return outputs.reshape(SEQ, HEADS * HD)

def reference(queries, keys, values, seg_ids, conv_weight, out_weight, out_grad):
    grad_attn = jnp.dot(out_grad, out_weight.T, preferred_element_type=jnp.float32)
    taps = conv_weight.astype(jnp.float32)

    def forward(query_rows, key_rows, value_cols):
        q_conv = convolve(query_rows, taps, seg_ids)
        return attention(q_conv, key_rows, value_cols, seg_ids)
    _, pullback = jax.vjp(forward, queries.astype(jnp.float32), keys.astype(jnp.float32), values.astype(jnp.float32))
    grad_queries, grad_keys, grad_values = pullback(grad_attn)
    return (grad_queries, grad_keys, grad_values)
```

```python
import jax
import jax.numpy as jnp
import numpy as np
from jax import lax
from jax.sharding import PartitionSpec as P

FD = 16
MOST = 2048


half_root = 0.7071067811865476
split_mode = lax.Precision.HIGH


def shifted(piece, axis, step, reverse):
    size = lax.axis_size(axis)
    if reverse:
        pairs = [(source, source - step) for source in range(step, size)]
    else:
        pairs = [(source, source + step) for source in range(size - step)]
    return lax.ppermute(piece, axis, pairs)


def entering(shard, axis, combine, reverse, reach):
    size = lax.axis_size(axis)
    total = shifted(shard, axis, 1, reverse)
    step = 1
    while step < reach and step < size:
        total = combine(shifted(total, axis, step, reverse), total)
        step *= 2
    return total


def features(entries):
    scaled = entries * 0.5
    row_index, col_index = np.triu_indices(scaled.shape[-2], 1)
    cross = jnp.take(scaled, row_index, axis=-2) * jnp.take(scaled, col_index, axis=-2)
    return jnp.concatenate(
        [jnp.ones_like(scaled[..., :1, :]), scaled, scaled * scaled * half_root, cross], axis=-2
    )


def block_output(q_feat, k_feat, head_values, doc_ids, carry_mask, state_in, normer_in):
    length = doc_ids.shape[0]
    causal = jnp.arange(length)[:, None] >= jnp.arange(length)[None, :]
    allowed = (causal & (doc_ids[:, None] == doc_ids[None, :])).astype(jnp.float32)
    scores = jnp.einsum("hft,hfs->hts", q_feat, k_feat, precision=split_mode) * allowed[None, :, :]
    numerator = jnp.einsum("hts,shd->thd", scores, head_values, precision=split_mode)
    numerator = numerator + carry_mask[:, None, None] * jnp.einsum(
        "hft,hfd->thd", q_feat, state_in, precision=split_mode
    )
    denominator = jnp.sum(scores, axis=2).T + carry_mask[:, None] * jnp.einsum(
        "hft,hf->th", q_feat, normer_in, precision=split_mode
    )
    return numerator / denominator[:, :, None]


def join_forward(earlier, later):
    empty_later = later[0][1] == 0.0
    same_doc = earlier[0][1] == later[0][1]
    state_out = jnp.where(empty_later, earlier[2], later[2] + jnp.where(same_doc, earlier[2], 0.0))
    normer_out = jnp.where(empty_later, earlier[3], later[3] + jnp.where(same_doc, earlier[3], 0.0))
    return (
        jnp.where(empty_later, earlier[0], later[0]),
        jnp.where(empty_later, earlier[1], later[1]),
        state_out,
        normer_out,
    )


def join_backward(earlier, later):
    empty_later = later[0][0] == 0.0
    same_doc = earlier[0][0] == later[0][0]
    state_out = jnp.where(empty_later, earlier[2], later[2] + jnp.where(same_doc, earlier[2], 0.0))
    normer_out = jnp.where(empty_later, earlier[3], later[3] + jnp.where(same_doc, earlier[3], 0.0))
    return (
        jnp.where(empty_later, earlier[0], later[0]),
        jnp.where(empty_later, earlier[1], later[1]),
        state_out,
        normer_out,
    )


def body(queries, keys, values, seg_ids, conv_weight, out_weight, out_grad):
    local_heads = queries.shape[0] // FD
    length = queries.shape[1]
    head_width = values.shape[1] // local_heads
    reach = -(-(MOST - 1) // length)
    grad_attn = lax.dot_general(
        lax.all_gather(out_grad, "head", axis=1, tiled=True),
        out_weight,
        (((1,), (1,)), ((), ())),
        preferred_element_type=jnp.float32,
    )
    doc_ids = (seg_ids + 1).astype(jnp.float32)
    query_rows = queries.astype(jnp.float32)
    key_heads = keys.astype(jnp.float32).reshape(local_heads, FD, length)
    head_values = values.astype(jnp.float32).reshape(length, local_heads, head_width)
    taps = conv_weight.astype(jnp.float32)
    k_feat, feature_pullback = jax.vjp(features, key_heads)
    tail_mask = (doc_ids == doc_ids[length - 1]).astype(jnp.float32)
    tail_feat = k_feat * tail_mask[None, None, :]
    tail_state = jnp.einsum("hfs,shd->hfd", tail_feat, head_values, precision=split_mode)
    tail_normer = jnp.sum(tail_feat, axis=2)
    forward_piece = (doc_ids[length - 2 :], query_rows[:, length - 2 :], tail_state, tail_normer)
    before = entering(forward_piece, "ctx", join_forward, False, reach)
    query_ext = jnp.concatenate([before[1], query_rows], axis=1)
    ids_before = jnp.concatenate([before[0], doc_ids])
    q_conv = taps[0][:, None] * query_rows
    for offset in (1, 2):
        same_doc = (ids_before[2 - offset : 2 - offset + length] == doc_ids).astype(jnp.float32)
        q_conv = (
            q_conv
            + taps[offset][:, None]
            * query_ext[:, 2 - offset : 2 - offset + length]
            * same_doc[None, :]
        )
    carry_mask = (doc_ids == before[0][1]).astype(jnp.float32)

    def local_forward(q_conv_in, k_feat_in, values_in, state_in, normer_in):
        q_feat = features(q_conv_in.reshape(local_heads, FD, length))
        result = block_output(
            q_feat, k_feat_in, values_in, doc_ids, carry_mask, state_in, normer_in
        )
        return result.reshape(length, local_heads * head_width)

    _, local_pullback = jax.vjp(local_forward, q_conv, k_feat, head_values, before[2], before[3])
    grad_qconv, grad_kfeat, grad_heads, grad_state, grad_normer = local_pullback(grad_attn)
    backward_piece = (doc_ids[:2], grad_qconv[:, :2], grad_state, grad_normer)
    after = entering(backward_piece, "ctx", join_backward, True, reach)
    head_mask = (doc_ids == after[0][0]).astype(jnp.float32)
    flowing = (
        jnp.einsum("hfd,shd->hfs", after[2], head_values, precision=split_mode)
        + after[3][:, :, None]
    )
    grad_kfeat = grad_kfeat + flowing * head_mask[None, None, :]
    grad_heads = grad_heads + jnp.einsum(
        "hfs,hfd->shd", k_feat * head_mask[None, None, :], after[2], precision=split_mode
    )
    (grad_key_heads,) = feature_pullback(grad_kfeat)
    grad_ext = jnp.concatenate([grad_qconv, after[1]], axis=1)
    ids_after = jnp.concatenate([doc_ids, after[0]])
    grad_queries = taps[0][:, None] * grad_qconv
    for offset in (1, 2):
        same_doc = (ids_after[offset : offset + length] == doc_ids).astype(jnp.float32)
        grad_queries = (
            grad_queries
            + taps[offset][:, None] * grad_ext[:, offset : offset + length] * same_doc[None, :]
        )
    grad_keys = grad_key_heads.reshape(local_heads * FD, length)
    grad_values = grad_heads.reshape(length, local_heads * head_width)
    return (grad_queries, grad_keys, grad_values)


def solution(mesh):
    in_specs = (
        P("head", "ctx"),
        P("head", "ctx"),
        P("ctx", "head"),
        P("ctx"),
        P(None, "head"),
        P("head", None),
        P("ctx", "head"),
    )
    out_specs = (P("head", "ctx"), P("head", "ctx"), P("ctx", "head"))
    return jax.shard_map(body, mesh=mesh, in_specs=in_specs, out_specs=out_specs, check_vma=False)
```

```python
import jax
import jax.numpy as jnp
import numpy as np
from jax import lax
from jax.sharding import PartitionSpec as P

FD = 16
MOST = 2048


half_root = 0.7071067811865476
split_mode = lax.Precision.HIGH


def shifted(piece, axis, step, reverse):
    size = lax.axis_size(axis)
    if reverse:
        pairs = [(source, source - step) for source in range(step, size)]
    else:
        pairs = [(source, source + step) for source in range(size - step)]
    return lax.ppermute(piece, axis, pairs)


def entering(shard, axis, combine, reverse, reach):
    size = lax.axis_size(axis)
    total = shifted(shard, axis, 1, reverse)
    step = 1
    while step < reach and step < size:
        total = combine(shifted(total, axis, step, reverse), total)
        step *= 2
    return total


def features(entries):
    scaled = entries * 0.5
    width = scaled.shape[-2]
    cross = jnp.concatenate(
        [scaled[..., i : i + 1, :] * scaled[..., i + 1 :, :] for i in range(width - 1)], axis=-2
    )
    return jnp.concatenate(
        [jnp.ones_like(scaled[..., :1, :]), scaled, scaled * scaled * half_root, cross], axis=-2
    )


def block_output(q_feat, k_feat, head_values, doc_ids, carry_mask, state_in, normer_in):
    length = doc_ids.shape[0]
    causal = jnp.arange(length)[:, None] >= jnp.arange(length)[None, :]
    allowed = (causal & (doc_ids[:, None] == doc_ids[None, :])).astype(jnp.float32)
    scores = jnp.einsum("hft,hfs->hts", q_feat, k_feat, precision=split_mode) * allowed[None, :, :]
    numerator = jnp.einsum("hts,shd->thd", scores, head_values, precision=split_mode)
    numerator = numerator + carry_mask[:, None, None] * jnp.einsum(
        "hft,hfd->thd", q_feat, state_in, precision=split_mode
    )
    denominator = jnp.sum(scores, axis=2).T + carry_mask[:, None] * jnp.einsum(
        "hft,hf->th", q_feat, normer_in, precision=split_mode
    )
    return numerator / denominator[:, :, None]


def packed_join(key, prefix):
    def join(earlier, later):
        empty_later = later[key] == 0.0
        same_doc = earlier[key] == later[key]
        position = lax.broadcasted_iota(jnp.int32, later.shape, 0)
        addend = jnp.where(same_doc & (position >= prefix), earlier, 0.0)
        return jnp.where(empty_later, earlier, later + addend)

    return join


def body(queries, keys, values, seg_ids, conv_weight, out_weight, out_grad):
    local_heads = queries.shape[0] // FD
    length = queries.shape[1]
    head_width = values.shape[1] // local_heads
    reach = -(-(MOST - 1) // length)
    grad_attn = lax.dot_general(
        lax.all_gather(out_grad, "head", axis=1, tiled=True),
        out_weight,
        (((1,), (1,)), ((), ())),
        preferred_element_type=jnp.float32,
    )
    doc_ids = (seg_ids + 1).astype(jnp.float32)
    query_rows = queries.astype(jnp.float32)
    key_heads = keys.astype(jnp.float32).reshape(local_heads, FD, length)
    head_values = values.astype(jnp.float32).reshape(length, local_heads, head_width)
    taps = conv_weight.astype(jnp.float32)
    k_feat, feature_pullback = jax.vjp(features, key_heads)
    tail_mask = (doc_ids == doc_ids[length - 1]).astype(jnp.float32)
    tail_feat = k_feat * tail_mask[None, None, :]
    tail_state = jnp.einsum("hfs,shd->hfd", tail_feat, head_values, precision=split_mode)
    tail_normer = jnp.sum(tail_feat, axis=2)
    row_count = query_rows.shape[0]
    prefix = 2 + 2 * row_count
    forward_piece = jnp.concatenate(
        [
            doc_ids[length - 2 :],
            query_rows[:, length - 2 :].reshape(-1),
            tail_normer.reshape(-1),
            tail_state.reshape(-1),
        ]
    )
    packed = entering(forward_piece, "ctx", packed_join(1, prefix), False, reach)
    before = (
        packed[:2],
        packed[2:prefix].reshape(row_count, 2),
        packed[prefix + tail_normer.size :].reshape(tail_state.shape),
        packed[prefix : prefix + tail_normer.size].reshape(tail_normer.shape),
    )
    query_ext = jnp.concatenate([before[1], query_rows], axis=1)
    ids_before = jnp.concatenate([before[0], doc_ids])
    q_conv = taps[0][:, None] * query_rows
    for offset in (1, 2):
        same_doc = (ids_before[2 - offset : 2 - offset + length] == doc_ids).astype(jnp.float32)
        q_conv = (
            q_conv
            + taps[offset][:, None]
            * query_ext[:, 2 - offset : 2 - offset + length]
            * same_doc[None, :]
        )
    carry_mask = (doc_ids == before[0][1]).astype(jnp.float32)

    def local_forward(q_conv_in, k_feat_in, values_in, state_in, normer_in):
        q_feat = features(q_conv_in.reshape(local_heads, FD, length))
        result = block_output(
            q_feat, k_feat_in, values_in, doc_ids, carry_mask, state_in, normer_in
        )
        return result.reshape(length, local_heads * head_width)

    _, local_pullback = jax.vjp(local_forward, q_conv, k_feat, head_values, before[2], before[3])
    grad_qconv, grad_kfeat, grad_heads, grad_state, grad_normer = local_pullback(grad_attn)
    backward_piece = jnp.concatenate(
        [
            doc_ids[:2],
            grad_qconv[:, :2].reshape(-1),
            grad_normer.reshape(-1),
            grad_state.reshape(-1),
        ]
    )
    packed = entering(backward_piece, "ctx", packed_join(0, prefix), True, reach)
    after = (
        packed[:2],
        packed[2:prefix].reshape(row_count, 2),
        packed[prefix + grad_normer.size :].reshape(grad_state.shape),
        packed[prefix : prefix + grad_normer.size].reshape(grad_normer.shape),
    )
    head_mask = (doc_ids == after[0][0]).astype(jnp.float32)
    flowing = (
        jnp.einsum("hfd,shd->hfs", after[2], head_values, precision=split_mode)
        + after[3][:, :, None]
    )
    grad_kfeat = grad_kfeat + flowing * head_mask[None, None, :]
    grad_heads = grad_heads + jnp.einsum(
        "hfs,hfd->shd", k_feat * head_mask[None, None, :], after[2], precision=split_mode
    )
    (grad_key_heads,) = feature_pullback(grad_kfeat)
    grad_ext = jnp.concatenate([grad_qconv, after[1]], axis=1)
    ids_after = jnp.concatenate([doc_ids, after[0]])
    grad_queries = taps[0][:, None] * grad_qconv
    for offset in (1, 2):
        same_doc = (ids_after[offset : offset + length] == doc_ids).astype(jnp.float32)
        grad_queries = (
            grad_queries
            + taps[offset][:, None] * grad_ext[:, offset : offset + length] * same_doc[None, :]
        )
    grad_keys = grad_key_heads.reshape(local_heads * FD, length)
    grad_values = grad_heads.reshape(length, local_heads * head_width)
    return (grad_queries, grad_keys, grad_values)


def solution(mesh):
    in_specs = (
        P("head", "ctx"),
        P("head", "ctx"),
        P("ctx", "head"),
        P("ctx"),
        P(None, "head"),
        P("head", None),
        P("ctx", "head"),
    )
    out_specs = (P("head", "ctx"), P("head", "ctx"), P("ctx", "head"))
    return jax.shard_map(body, mesh=mesh, in_specs=in_specs, out_specs=out_specs, check_vma=False)
```

```python
import jax
import jax.numpy as jnp
import numpy as np
from jax import lax
from jax.sharding import PartitionSpec as P

FD = 16
MOST = 2048


half_root = 0.7071067811865476
split_mode = lax.Precision.HIGH


def shifted(piece, axis, step, reverse):
    size = lax.axis_size(axis)
    if reverse:
        pairs = [(source, source - step) for source in range(step, size)]
    else:
        pairs = [(source, source + step) for source in range(size - step)]
    return lax.ppermute(piece, axis, pairs)


def fold(combine, pieces):
    total = pieces[0]
    for piece in pieces[1:]:
        total = combine(total, piece)
    return total


def entering(shard, axis, combine, reverse, reach):
    size = lax.axis_size(axis)
    fan = 1
    while fan * fan < reach:
        fan += 1
    near = [step for step in range(fan - 1, 0, -1) if step < size]
    total = fold(combine, [shifted(shard, axis, step, reverse) for step in near] + [shard])
    far = [1 + fan * k for k in range(-(-reach // fan) - 1, -1, -1)]
    far = [step for step in far if step < size]
    return fold(combine, [shifted(total, axis, step, reverse) for step in far])


def features(entries):
    scaled = entries * 0.5
    width = scaled.shape[-2]
    cross = jnp.concatenate(
        [scaled[..., i : i + 1, :] * scaled[..., i + 1 :, :] for i in range(width - 1)], axis=-2
    )
    return jnp.concatenate(
        [jnp.ones_like(scaled[..., :1, :]), scaled, scaled * scaled * half_root, cross], axis=-2
    )


def block_output(q_feat, k_feat, head_values, doc_ids, carry_mask, state_in, normer_in):
    length = doc_ids.shape[0]
    causal = jnp.arange(length)[:, None] >= jnp.arange(length)[None, :]
    allowed = (causal & (doc_ids[:, None] == doc_ids[None, :])).astype(jnp.float32)
    scores = jnp.einsum("hft,hfs->hts", q_feat, k_feat, precision=split_mode) * allowed[None, :, :]
    numerator = jnp.einsum("hts,shd->thd", scores, head_values, precision=split_mode)
    numerator = numerator + carry_mask[:, None, None] * jnp.einsum(
        "hft,hfd->thd", q_feat, state_in, precision=split_mode
    )
    denominator = jnp.sum(scores, axis=2).T + carry_mask[:, None] * jnp.einsum(
        "hft,hf->th", q_feat, normer_in, precision=split_mode
    )
    return numerator / denominator[:, :, None]


def packed_join(key, prefix):
    def join(earlier, later):
        empty_later = later[key] == 0.0
        same_doc = earlier[key] == later[key]
        position = lax.broadcasted_iota(jnp.int32, later.shape, 0)
        addend = jnp.where(same_doc & (position >= prefix), earlier, 0.0)
        return jnp.where(empty_later, earlier, later + addend)

    return join


def body(queries, keys, values, seg_ids, conv_weight, out_weight, out_grad):
    local_heads = queries.shape[0] // FD
    length = queries.shape[1]
    head_width = values.shape[1] // local_heads
    reach = -(-(MOST - 1) // length)
    grad_attn = lax.dot_general(
        lax.all_gather(out_grad, "head", axis=1, tiled=True),
        out_weight,
        (((1,), (1,)), ((), ())),
        preferred_element_type=jnp.float32,
    )
    doc_ids = (seg_ids + 1).astype(jnp.float32)
    query_rows = queries.astype(jnp.float32)
    key_heads = keys.astype(jnp.float32).reshape(local_heads, FD, length)
    head_values = values.astype(jnp.float32).reshape(length, local_heads, head_width)
    taps = conv_weight.astype(jnp.float32)
    k_feat, feature_pullback = jax.vjp(features, key_heads)
    tail_mask = (doc_ids == doc_ids[length - 1]).astype(jnp.float32)
    tail_feat = k_feat * tail_mask[None, None, :]
    tail_state = jnp.einsum("hfs,shd->hfd", tail_feat, head_values, precision=split_mode)
    tail_normer = jnp.sum(tail_feat, axis=2)
    row_count = query_rows.shape[0]
    prefix = 2 + 2 * row_count
    forward_piece = jnp.concatenate(
        [
            doc_ids[length - 2 :],
            query_rows[:, length - 2 :].reshape(-1),
            tail_normer.reshape(-1),
            tail_state.reshape(-1),
        ]
    )
    packed = entering(forward_piece, "ctx", packed_join(1, prefix), False, reach)
    before = (
        packed[:2],
        packed[2:prefix].reshape(row_count, 2),
        packed[prefix + tail_normer.size :].reshape(tail_state.shape),
        packed[prefix : prefix + tail_normer.size].reshape(tail_normer.shape),
    )
    query_ext = jnp.concatenate([before[1], query_rows], axis=1)
    ids_before = jnp.concatenate([before[0], doc_ids])
    q_conv = taps[0][:, None] * query_rows
    for offset in (1, 2):
        same_doc = (ids_before[2 - offset : 2 - offset + length] == doc_ids).astype(jnp.float32)
        q_conv = (
            q_conv
            + taps[offset][:, None]
            * query_ext[:, 2 - offset : 2 - offset + length]
            * same_doc[None, :]
        )
    carry_mask = (doc_ids == before[0][1]).astype(jnp.float32)

    def local_forward(q_conv_in, k_feat_in, values_in, state_in, normer_in):
        q_feat = features(q_conv_in.reshape(local_heads, FD, length))
        result = block_output(
            q_feat, k_feat_in, values_in, doc_ids, carry_mask, state_in, normer_in
        )
        return result.reshape(length, local_heads * head_width)

    _, local_pullback = jax.vjp(local_forward, q_conv, k_feat, head_values, before[2], before[3])
    grad_qconv, grad_kfeat, grad_heads, grad_state, grad_normer = local_pullback(grad_attn)
    backward_piece = jnp.concatenate(
        [
            doc_ids[:2],
            grad_qconv[:, :2].reshape(-1),
            grad_normer.reshape(-1),
            grad_state.reshape(-1),
        ]
    )
    packed = entering(backward_piece, "ctx", packed_join(0, prefix), True, reach)
    after = (
        packed[:2],
        packed[2:prefix].reshape(row_count, 2),
        packed[prefix + grad_normer.size :].reshape(grad_state.shape),
        packed[prefix : prefix + grad_normer.size].reshape(grad_normer.shape),
    )
    head_mask = (doc_ids == after[0][0]).astype(jnp.float32)
    flowing = (
        jnp.einsum("hfd,shd->hfs", after[2], head_values, precision=split_mode)
        + after[3][:, :, None]
    )
    grad_kfeat = grad_kfeat + flowing * head_mask[None, None, :]
    grad_heads = grad_heads + jnp.einsum(
        "hfs,hfd->shd", k_feat * head_mask[None, None, :], after[2], precision=split_mode
    )
    (grad_key_heads,) = feature_pullback(grad_kfeat)
    grad_ext = jnp.concatenate([grad_qconv, after[1]], axis=1)
    ids_after = jnp.concatenate([doc_ids, after[0]])
    grad_queries = taps[0][:, None] * grad_qconv
    for offset in (1, 2):
        same_doc = (ids_after[offset : offset + length] == doc_ids).astype(jnp.float32)
        grad_queries = (
            grad_queries
            + taps[offset][:, None] * grad_ext[:, offset : offset + length] * same_doc[None, :]
        )
    grad_keys = grad_key_heads.reshape(local_heads * FD, length)
    grad_values = grad_heads.reshape(length, local_heads * head_width)
    return (grad_queries, grad_keys, grad_values)


def solution(mesh):
    in_specs = (
        P("head", "ctx"),
        P("head", "ctx"),
        P("ctx", "head"),
        P("ctx"),
        P(None, "head"),
        P("head", None),
        P("ctx", "head"),
    )
    out_specs = (P("head", "ctx"), P("head", "ctx"), P("ctx", "head"))
    return jax.shard_map(body, mesh=mesh, in_specs=in_specs, out_specs=out_specs, check_vma=False)
```

```python
import jax
import jax.numpy as jnp
import numpy as np
from jax import lax
from jax.sharding import PartitionSpec as P

FD = 16
MOST = 2048


half_root = 0.7071067811865476
split_mode = lax.Precision.HIGH


def shifted(piece, axis, step, reverse):
    size = lax.axis_size(axis)
    if reverse:
        pairs = [(source, source - step) for source in range(step, size)]
    else:
        pairs = [(source, source + step) for source in range(size - step)]
    return lax.ppermute(piece, axis, pairs)


def fold(combine, pieces):
    total = pieces[0]
    for piece in pieces[1:]:
        total = combine(total, piece)
    return total


def entering(shard, axis, combine, reverse, reach):
    size = lax.axis_size(axis)
    fan = 1
    while fan * fan < reach:
        fan += 1
    near = [step for step in range(fan - 1, 0, -1) if step < size]
    total = fold(combine, [shifted(shard, axis, step, reverse) for step in near] + [shard])
    far = [1 + fan * k for k in range(-(-reach // fan) - 1, -1, -1)]
    far = [step for step in far if step < size]
    return fold(combine, [shifted(total, axis, step, reverse) for step in far])


def features(entries):
    scaled = entries * 0.5
    width = scaled.shape[-2]
    cross = jnp.concatenate(
        [scaled[..., i : i + 1, :] * scaled[..., i + 1 :, :] for i in range(width - 1)], axis=-2
    )
    return jnp.concatenate(
        [jnp.ones_like(scaled[..., :1, :]), scaled, scaled * scaled * half_root, cross], axis=-2
    )


def block_output(q_feat, k_feat, head_values, doc_ids, carry_mask, state_in, normer_in):
    length = doc_ids.shape[0]
    causal = jnp.arange(length)[:, None] >= jnp.arange(length)[None, :]
    allowed = (causal & (doc_ids[:, None] == doc_ids[None, :])).astype(jnp.float32)
    scores = jnp.einsum("hft,hfs->hts", q_feat, k_feat, precision=split_mode) * allowed[None, :, :]
    numerator = jnp.einsum("hts,shd->thd", scores, head_values, precision=split_mode)
    numerator = numerator + carry_mask[:, None, None] * jnp.einsum(
        "hft,hfd->thd", q_feat, state_in, precision=split_mode
    )
    denominator = jnp.sum(scores, axis=2).T + carry_mask[:, None] * jnp.einsum(
        "hft,hf->th", q_feat, normer_in, precision=split_mode
    )
    return numerator / denominator[:, :, None]


def packed_join(key_row):
    def join(earlier, later):
        empty_later = later[key_row : key_row + 1] == 0.0
        same_doc = earlier[key_row : key_row + 1] == later[key_row : key_row + 1]
        row = lax.broadcasted_iota(jnp.int32, later.shape, 0)
        addend = jnp.where(same_doc & (row < key_row), earlier, 0.0)
        return jnp.where(empty_later, earlier, later + addend)

    return join


def pack(state, normer, key, edge):
    lanes = state.shape[-1]
    state_rows = state.reshape(-1, lanes)
    normer_flat = normer.reshape(-1)
    normer_rows = -(-normer_flat.size // lanes)
    normer_part = jnp.pad(normer_flat, (0, normer_rows * lanes - normer_flat.size))
    key_part = jnp.broadcast_to(key, (1, lanes))
    edge_rows = -(-edge.size // lanes)
    edge_part = jnp.pad(edge, (0, edge_rows * lanes - edge.size)).reshape(edge_rows, lanes)
    rows = state_rows.shape[0] + normer_rows + 1 + edge_rows
    tail = -rows % 8
    return jnp.concatenate(
        [
            state_rows,
            normer_part.reshape(normer_rows, lanes),
            key_part,
            edge_part,
            jnp.zeros((tail, lanes), state.dtype),
        ]
    )


def unpack(packed, state_shape, normer_shape, edge_size):
    lanes = state_shape[-1]
    state_rows = int(np.prod(state_shape[:-1]))
    normer_size = int(np.prod(normer_shape))
    key_row = state_rows + -(-normer_size // lanes)
    state = packed[:state_rows].reshape(state_shape)
    normer = packed[state_rows:key_row].reshape(-1)[:normer_size].reshape(normer_shape)
    edge_rows = -(-edge_size // lanes)
    edge = packed[key_row + 1 : key_row + 1 + edge_rows].reshape(-1)[:edge_size]
    return state, normer, edge


def body(queries, keys, values, seg_ids, conv_weight, out_weight, out_grad):
    local_heads = queries.shape[0] // FD
    length = queries.shape[1]
    head_width = values.shape[1] // local_heads
    reach = -(-(MOST - 1) // length)
    grad_attn = lax.dot_general(
        lax.all_gather(out_grad, "head", axis=1, tiled=True),
        out_weight,
        (((1,), (1,)), ((), ())),
        preferred_element_type=jnp.float32,
    )
    doc_ids = (seg_ids + 1).astype(jnp.float32)
    query_rows = queries.astype(jnp.float32)
    key_heads = keys.astype(jnp.float32).reshape(local_heads, FD, length)
    head_values = values.astype(jnp.float32).reshape(length, local_heads, head_width)
    taps = conv_weight.astype(jnp.float32)
    k_feat, feature_pullback = jax.vjp(features, key_heads)
    tail_mask = (doc_ids == doc_ids[length - 1]).astype(jnp.float32)
    tail_feat = k_feat * tail_mask[None, None, :]
    tail_state = jnp.einsum("hfs,shd->hfd", tail_feat, head_values, precision=split_mode)
    tail_normer = jnp.sum(tail_feat, axis=2)
    row_count = query_rows.shape[0]
    key_row = tail_state.size // head_width + -(-tail_normer.size // head_width)
    forward_piece = pack(
        tail_state,
        tail_normer,
        doc_ids[length - 1],
        jnp.concatenate([doc_ids[length - 2 :], query_rows[:, length - 2 :].reshape(-1)]),
    )
    packed = entering(forward_piece, "ctx", packed_join(key_row), False, reach)
    state_in, normer_in, edge = unpack(packed, tail_state.shape, tail_normer.shape, 2 + 2 * row_count)
    before = (edge[:2], edge[2:].reshape(row_count, 2), state_in, normer_in)
    query_ext = jnp.concatenate([before[1], query_rows], axis=1)
    ids_before = jnp.concatenate([before[0], doc_ids])
    q_conv = taps[0][:, None] * query_rows
    for offset in (1, 2):
        same_doc = (ids_before[2 - offset : 2 - offset + length] == doc_ids).astype(jnp.float32)
        q_conv = (
            q_conv
            + taps[offset][:, None]
            * query_ext[:, 2 - offset : 2 - offset + length]
            * same_doc[None, :]
        )
    carry_mask = (doc_ids == before[0][1]).astype(jnp.float32)

    def local_forward(q_conv_in, k_feat_in, values_in, state_in, normer_in):
        q_feat = features(q_conv_in.reshape(local_heads, FD, length))
        result = block_output(
            q_feat, k_feat_in, values_in, doc_ids, carry_mask, state_in, normer_in
        )
        return result.reshape(length, local_heads * head_width)

    _, local_pullback = jax.vjp(local_forward, q_conv, k_feat, head_values, before[2], before[3])
    grad_qconv, grad_kfeat, grad_heads, grad_state, grad_normer = local_pullback(grad_attn)
    backward_piece = pack(
        grad_state,
        grad_normer,
        doc_ids[0],
        jnp.concatenate([doc_ids[:2], grad_qconv[:, :2].reshape(-1)]),
    )
    packed = entering(backward_piece, "ctx", packed_join(key_row), True, reach)
    state_out, normer_out, edge = unpack(packed, grad_state.shape, grad_normer.shape, 2 + 2 * row_count)
    after = (edge[:2], edge[2:].reshape(row_count, 2), state_out, normer_out)
    head_mask = (doc_ids == after[0][0]).astype(jnp.float32)
    flowing = (
        jnp.einsum("hfd,shd->hfs", after[2], head_values, precision=split_mode)
        + after[3][:, :, None]
    )
    grad_kfeat = grad_kfeat + flowing * head_mask[None, None, :]
    grad_heads = grad_heads + jnp.einsum(
        "hfs,hfd->shd", k_feat * head_mask[None, None, :], after[2], precision=split_mode
    )
    (grad_key_heads,) = feature_pullback(grad_kfeat)
    grad_ext = jnp.concatenate([grad_qconv, after[1]], axis=1)
    ids_after = jnp.concatenate([doc_ids, after[0]])
    grad_queries = taps[0][:, None] * grad_qconv
    for offset in (1, 2):
        same_doc = (ids_after[offset : offset + length] == doc_ids).astype(jnp.float32)
        grad_queries = (
            grad_queries
            + taps[offset][:, None] * grad_ext[:, offset : offset + length] * same_doc[None, :]
        )
    grad_keys = grad_key_heads.reshape(local_heads * FD, length)
    grad_values = grad_heads.reshape(length, local_heads * head_width)
    return (grad_queries, grad_keys, grad_values)


def solution(mesh):
    in_specs = (
        P("head", "ctx"),
        P("head", "ctx"),
        P("ctx", "head"),
        P("ctx"),
        P(None, "head"),
        P("head", None),
        P("ctx", "head"),
    )
    out_specs = (P("head", "ctx"), P("head", "ctx"), P("ctx", "head"))
    return jax.shard_map(body, mesh=mesh, in_specs=in_specs, out_specs=out_specs, check_vma=False)
```

```python
import jax
import jax.numpy as jnp
import numpy as np
from jax import lax
from jax.sharding import PartitionSpec as P

FD = 16
MOST = 2048


half_root = 0.7071067811865476
split_mode = lax.Precision.HIGH


def shifted(piece, axis, step, reverse):
    size = lax.axis_size(axis)
    if reverse:
        pairs = [(source, source - step) for source in range(step, size)]
    else:
        pairs = [(source, source + step) for source in range(size - step)]
    return lax.ppermute(piece, axis, pairs)


def fold(combine, pieces):
    total = pieces[0]
    for piece in pieces[1:]:
        total = combine(total, piece)
    return total


def window_steps(reach, size):
    fan = 1
    while fan * fan < reach:
        fan += 1
    near = [step for step in range(fan - 1, 0, -1) if step < size]
    far = [1 + fan * k for k in range(-(-reach // fan) - 1, -1, -1)]
    return near, [step for step in far if step < size]


def entering(shard, axis, combine, reverse, reach):
    near, far = window_steps(reach, lax.axis_size(axis))
    total = fold(combine, [shifted(shard, axis, step, reverse) for step in near] + [shard])
    return fold(combine, [shifted(total, axis, step, reverse) for step in far])


def rows_of(flat, lanes):
    count = -(-flat.size // lanes)
    return jnp.pad(flat, (0, count * lanes - flat.size)).reshape(count, lanes)


def raw_pack(keys, values, doc_ids, edge):
    lanes = keys.shape[1]
    parts = [values.T, keys, doc_ids.astype(keys.dtype)[None, :], rows_of(edge, lanes)]
    rows = sum(part.shape[0] for part in parts)
    parts.append(jnp.zeros((-rows % 16, lanes), keys.dtype))
    return jnp.concatenate(parts)


def raw_unpack(packed, value_rows, key_rows, edge_size):
    lanes = packed.shape[1]
    ids_row = value_rows + key_rows
    edge_rows = -(-edge_size // lanes)
    return (
        packed[:value_rows],
        packed[value_rows:ids_row],
        packed[ids_row].astype(jnp.float32),
        packed[ids_row + 1 : ids_row + 1 + edge_rows].reshape(-1)[:edge_size],
    )


def features(entries):
    scaled = entries * 0.5
    width = scaled.shape[-2]
    cross = jnp.concatenate(
        [scaled[..., i : i + 1, :] * scaled[..., i + 1 :, :] for i in range(width - 1)], axis=-2
    )
    return jnp.concatenate(
        [jnp.ones_like(scaled[..., :1, :]), scaled, scaled * scaled * half_root, cross], axis=-2
    )


def block_output(q_feat, k_feat, head_values, doc_ids, carry_mask, state_in, normer_in):
    length = doc_ids.shape[0]
    causal = jnp.arange(length)[:, None] >= jnp.arange(length)[None, :]
    allowed = (causal & (doc_ids[:, None] == doc_ids[None, :])).astype(jnp.float32)
    scores = jnp.einsum("hft,hfs->hts", q_feat, k_feat, precision=split_mode) * allowed[None, :, :]
    numerator = jnp.einsum("hts,shd->thd", scores, head_values, precision=split_mode)
    numerator = numerator + carry_mask[:, None, None] * jnp.einsum(
        "hft,hfd->thd", q_feat, state_in, precision=split_mode
    )
    denominator = jnp.sum(scores, axis=2).T + carry_mask[:, None] * jnp.einsum(
        "hft,hf->th", q_feat, normer_in, precision=split_mode
    )
    return numerator / denominator[:, :, None]


def packed_join(key_row):
    def join(earlier, later):
        empty_later = later[key_row : key_row + 1] == 0.0
        same_doc = earlier[key_row : key_row + 1] == later[key_row : key_row + 1]
        row = lax.broadcasted_iota(jnp.int32, later.shape, 0)
        addend = jnp.where(same_doc & (row < key_row), earlier, 0.0)
        return jnp.where(empty_later, earlier, later + addend)

    return join


def pack(state, normer, key, edge):
    lanes = state.shape[-1]
    state_rows = state.reshape(-1, lanes)
    normer_flat = normer.reshape(-1)
    normer_rows = -(-normer_flat.size // lanes)
    normer_part = jnp.pad(normer_flat, (0, normer_rows * lanes - normer_flat.size))
    key_part = jnp.broadcast_to(key, (1, lanes))
    edge_rows = -(-edge.size // lanes)
    edge_part = jnp.pad(edge, (0, edge_rows * lanes - edge.size)).reshape(edge_rows, lanes)
    rows = state_rows.shape[0] + normer_rows + 1 + edge_rows
    tail = -rows % 8
    return jnp.concatenate(
        [
            state_rows,
            normer_part.reshape(normer_rows, lanes),
            key_part,
            edge_part,
            jnp.zeros((tail, lanes), state.dtype),
        ]
    )


def unpack(packed, state_shape, normer_shape, edge_size):
    lanes = state_shape[-1]
    state_rows = int(np.prod(state_shape[:-1]))
    normer_size = int(np.prod(normer_shape))
    key_row = state_rows + -(-normer_size // lanes)
    state = packed[:state_rows].reshape(state_shape)
    normer = packed[state_rows:key_row].reshape(-1)[:normer_size].reshape(normer_shape)
    edge_rows = -(-edge_size // lanes)
    edge = packed[key_row + 1 : key_row + 1 + edge_rows].reshape(-1)[:edge_size]
    return state, normer, edge


def body(queries, keys, values, seg_ids, conv_weight, out_weight, out_grad):
    local_heads = queries.shape[0] // FD
    length = queries.shape[1]
    head_width = values.shape[1] // local_heads
    reach = -(-(MOST - 1) // length)
    grad_attn = lax.dot_general(
        lax.all_gather(out_grad, "head", axis=1, tiled=True),
        out_weight,
        (((1,), (1,)), ((), ())),
        preferred_element_type=jnp.float32,
    )
    doc_ids = (seg_ids + 1).astype(jnp.float32)
    query_rows = queries.astype(jnp.float32)
    key_heads = keys.astype(jnp.float32).reshape(local_heads, FD, length)
    head_values = values.astype(jnp.float32).reshape(length, local_heads, head_width)
    taps = conv_weight.astype(jnp.float32)
    k_feat, feature_pullback = jax.vjp(features, key_heads)
    row_count = query_rows.shape[0]
    near, far = window_steps(reach, lax.axis_size("ctx"))
    raw = raw_pack(keys, values, doc_ids, queries[:, length - 2 :].reshape(-1))
    received = [
        raw_unpack(shifted(raw, "ctx", step, False), values.shape[1], row_count, 2 * row_count)
        for step in near
    ]
    window_keys = jnp.concatenate([part[1] for part in received], axis=1).astype(jnp.float32)
    window_feat = jnp.concatenate(
        [features(window_keys.reshape(local_heads, FD, -1)), k_feat], axis=2
    )
    window_values = jnp.concatenate(
        [part[0] for part in received] + [values.T], axis=1
    ).astype(jnp.float32)
    window_ids = jnp.concatenate([part[2] for part in received] + [doc_ids])
    tail_mask = (window_ids == doc_ids[length - 1]).astype(jnp.float32)
    tail_feat = window_feat * tail_mask[None, None, :]
    tail_state = jnp.einsum(
        "hft,hdt->hfd",
        tail_feat,
        window_values.reshape(local_heads, head_width, -1),
        precision=split_mode,
    )
    tail_normer = jnp.sum(tail_feat, axis=2)
    key_row = tail_state.size // head_width + -(-tail_normer.size // head_width)
    forward_piece = pack(tail_state, tail_normer, doc_ids[length - 1], jnp.zeros((1,), jnp.float32))
    join = packed_join(key_row)
    packed = fold(join, [shifted(forward_piece, "ctx", step, False) for step in far])
    state_in, normer_in, _ = unpack(packed, tail_state.shape, tail_normer.shape, 1)
    previous = received[-1] if near else raw_unpack(jnp.zeros_like(raw), values.shape[1], row_count, 2 * row_count)
    before = (
        previous[2][length - 2 :],
        previous[3].astype(jnp.float32).reshape(row_count, 2),
        state_in,
        normer_in,
    )
    query_ext = jnp.concatenate([before[1], query_rows], axis=1)
    ids_before = jnp.concatenate([before[0], doc_ids])
    q_conv = taps[0][:, None] * query_rows
    for offset in (1, 2):
        same_doc = (ids_before[2 - offset : 2 - offset + length] == doc_ids).astype(jnp.float32)
        q_conv = (
            q_conv
            + taps[offset][:, None]
            * query_ext[:, 2 - offset : 2 - offset + length]
            * same_doc[None, :]
        )
    carry_mask = (doc_ids == before[0][1]).astype(jnp.float32)

    def local_forward(q_conv_in, k_feat_in, values_in, state_in, normer_in):
        q_feat = features(q_conv_in.reshape(local_heads, FD, length))
        result = block_output(
            q_feat, k_feat_in, values_in, doc_ids, carry_mask, state_in, normer_in
        )
        return result.reshape(length, local_heads * head_width)

    _, local_pullback = jax.vjp(local_forward, q_conv, k_feat, head_values, before[2], before[3])
    grad_qconv, grad_kfeat, grad_heads, grad_state, grad_normer = local_pullback(grad_attn)
    backward_piece = pack(
        grad_state,
        grad_normer,
        doc_ids[0],
        jnp.concatenate([doc_ids[:2], grad_qconv[:, :2].reshape(-1)]),
    )
    packed = entering(backward_piece, "ctx", packed_join(key_row), True, reach)
    state_out, normer_out, edge = unpack(packed, grad_state.shape, grad_normer.shape, 2 + 2 * row_count)
    after = (edge[:2], edge[2:].reshape(row_count, 2), state_out, normer_out)
    head_mask = (doc_ids == after[0][0]).astype(jnp.float32)
    flowing = (
        jnp.einsum("hfd,shd->hfs", after[2], head_values, precision=split_mode)
        + after[3][:, :, None]
    )
    grad_kfeat = grad_kfeat + flowing * head_mask[None, None, :]
    grad_heads = grad_heads + jnp.einsum(
        "hfs,hfd->shd", k_feat * head_mask[None, None, :], after[2], precision=split_mode
    )
    (grad_key_heads,) = feature_pullback(grad_kfeat)
    grad_ext = jnp.concatenate([grad_qconv, after[1]], axis=1)
    ids_after = jnp.concatenate([doc_ids, after[0]])
    grad_queries = taps[0][:, None] * grad_qconv
    for offset in (1, 2):
        same_doc = (ids_after[offset : offset + length] == doc_ids).astype(jnp.float32)
        grad_queries = (
            grad_queries
            + taps[offset][:, None] * grad_ext[:, offset : offset + length] * same_doc[None, :]
        )
    grad_keys = grad_key_heads.reshape(local_heads * FD, length)
    grad_values = grad_heads.reshape(length, local_heads * head_width)
    return (grad_queries, grad_keys, grad_values)


def solution(mesh):
    in_specs = (
        P("head", "ctx"),
        P("head", "ctx"),
        P("ctx", "head"),
        P("ctx"),
        P(None, "head"),
        P("head", None),
        P("ctx", "head"),
    )
    out_specs = (P("head", "ctx"), P("head", "ctx"), P("ctx", "head"))
    return jax.shard_map(body, mesh=mesh, in_specs=in_specs, out_specs=out_specs, check_vma=False)
```

```python
import jax
import jax.numpy as jnp
import numpy as np
from jax import lax
from jax.sharding import PartitionSpec as P

FD = 16
MOST = 2048


half_root = 0.7071067811865476
split_mode = lax.Precision.HIGH
exact_mode = lax.Precision.HIGHEST


def shifted(piece, axis, step, reverse):
    size = lax.axis_size(axis)
    if reverse:
        pairs = [(source, source - step) for source in range(step, size)]
    else:
        pairs = [(source, source + step) for source in range(size - step)]
    return lax.ppermute(piece, axis, pairs)


def fold(combine, pieces):
    total = pieces[0]
    for piece in pieces[1:]:
        total = combine(total, piece)
    return total


def window_steps(reach, size):
    fan = 1
    while fan * fan < reach:
        fan += 1
    near = [step for step in range(fan - 1, 0, -1) if step < size]
    far = [1 + fan * k for k in range(-(-reach // fan) - 1, -1, -1)]
    return near, [step for step in far if step < size]


def entering(shard, axis, combine, reverse, reach):
    near, far = window_steps(reach, lax.axis_size(axis))
    total = fold(combine, [shifted(shard, axis, step, reverse) for step in near] + [shard])
    return fold(combine, [shifted(total, axis, step, reverse) for step in far])


def rows_of(flat, lanes):
    count = -(-flat.size // lanes)
    return jnp.pad(flat, (0, count * lanes - flat.size)).reshape(count, lanes)


def raw_pack(keys, values, doc_ids, edge):
    lanes = keys.shape[1]
    parts = [values.T, keys, doc_ids.astype(keys.dtype)[None, :], rows_of(edge, lanes)]
    rows = sum(part.shape[0] for part in parts)
    parts.append(jnp.zeros((-rows % 16, lanes), keys.dtype))
    return jnp.concatenate(parts)


def raw_unpack(packed, value_rows, key_rows, edge_size):
    lanes = packed.shape[1]
    ids_row = value_rows + key_rows
    edge_rows = -(-edge_size // lanes)
    return (
        packed[:value_rows],
        packed[value_rows:ids_row],
        packed[ids_row].astype(jnp.float32),
        packed[ids_row + 1 : ids_row + 1 + edge_rows].reshape(-1)[:edge_size],
    )


def feature_tables(width):
    count = 1 + 2 * width + width * (width - 1) // 2
    left = np.zeros((count, width), np.float32)
    right = np.zeros((count, width), np.float32)
    left_one = np.zeros((count, 1), np.float32)
    right_one = np.zeros((count, 1), np.float32)
    weight = np.ones((count, 1), np.float32)
    left_one[0] = 1.0
    right_one[0] = 1.0
    for i in range(width):
        left[1 + i, i] = 1.0
        right_one[1 + i] = 1.0
        left[1 + width + i, i] = 1.0
        right[1 + width + i, i] = 1.0
        weight[1 + width + i] = half_root
    row_index, col_index = np.triu_indices(width, 1)
    for n, (i, j) in enumerate(zip(row_index, col_index)):
        left[1 + 2 * width + n, i] = 1.0
        right[1 + 2 * width + n, j] = 1.0
    return left, right, left_one, right_one, weight


def features(entries):
    scaled = entries * 0.5
    left, right, left_one, right_one, weight = feature_tables(scaled.shape[-2])
    first = jnp.einsum("rk,...kt->...rt", left, scaled, precision=exact_mode) + left_one
    second = jnp.einsum("rk,...kt->...rt", right, scaled, precision=exact_mode) + right_one
    return first * second * weight


def block_output(q_feat, k_feat, head_values, doc_ids, carry_mask, state_in, normer_in):
    length = doc_ids.shape[0]
    causal = jnp.arange(length)[:, None] >= jnp.arange(length)[None, :]
    allowed = (causal & (doc_ids[:, None] == doc_ids[None, :])).astype(jnp.float32)
    scores = jnp.einsum("hft,hfs->hts", q_feat, k_feat, precision=split_mode) * allowed[None, :, :]
    numerator = jnp.einsum("hts,shd->thd", scores, head_values, precision=split_mode)
    numerator = numerator + carry_mask[:, None, None] * jnp.einsum(
        "hft,hfd->thd", q_feat, state_in, precision=split_mode
    )
    denominator = jnp.sum(scores, axis=2).T + carry_mask[:, None] * jnp.einsum(
        "hft,hf->th", q_feat, normer_in, precision=split_mode
    )
    return numerator / denominator[:, :, None]


def packed_join(key_row):
    def join(earlier, later):
        empty_later = later[key_row : key_row + 1] == 0.0
        same_doc = earlier[key_row : key_row + 1] == later[key_row : key_row + 1]
        row = lax.broadcasted_iota(jnp.int32, later.shape, 0)
        addend = jnp.where(same_doc & (row < key_row), earlier, 0.0)
        return jnp.where(empty_later, earlier, later + addend)

    return join


def pack(state, normer, key, edge):
    lanes = state.shape[-1]
    state_rows = state.reshape(-1, lanes)
    normer_flat = normer.reshape(-1)
    normer_rows = -(-normer_flat.size // lanes)
    normer_part = jnp.pad(normer_flat, (0, normer_rows * lanes - normer_flat.size))
    key_part = jnp.broadcast_to(key, (1, lanes))
    edge_rows = -(-edge.size // lanes)
    edge_part = jnp.pad(edge, (0, edge_rows * lanes - edge.size)).reshape(edge_rows, lanes)
    rows = state_rows.shape[0] + normer_rows + 1 + edge_rows
    tail = -rows % 8
    return jnp.concatenate(
        [
            state_rows,
            normer_part.reshape(normer_rows, lanes),
            key_part,
            edge_part,
            jnp.zeros((tail, lanes), state.dtype),
        ]
    )


def unpack(packed, state_shape, normer_shape, edge_size):
    lanes = state_shape[-1]
    state_rows = int(np.prod(state_shape[:-1]))
    normer_size = int(np.prod(normer_shape))
    key_row = state_rows + -(-normer_size // lanes)
    state = packed[:state_rows].reshape(state_shape)
    normer = packed[state_rows:key_row].reshape(-1)[:normer_size].reshape(normer_shape)
    edge_rows = -(-edge_size // lanes)
    edge = packed[key_row + 1 : key_row + 1 + edge_rows].reshape(-1)[:edge_size]
    return state, normer, edge


def body(queries, keys, values, seg_ids, conv_weight, out_weight, out_grad):
    local_heads = queries.shape[0] // FD
    length = queries.shape[1]
    head_width = values.shape[1] // local_heads
    reach = -(-(MOST - 1) // length)
    grad_attn = lax.dot_general(
        lax.all_gather(out_grad, "head", axis=1, tiled=True),
        out_weight,
        (((1,), (1,)), ((), ())),
        preferred_element_type=jnp.float32,
    )
    doc_ids = (seg_ids + 1).astype(jnp.float32)
    query_rows = queries.astype(jnp.float32)
    key_heads = keys.astype(jnp.float32).reshape(local_heads, FD, length)
    head_values = values.astype(jnp.float32).reshape(length, local_heads, head_width)
    taps = conv_weight.astype(jnp.float32)
    k_feat, feature_pullback = jax.vjp(features, key_heads)
    row_count = query_rows.shape[0]
    near, far = window_steps(reach, lax.axis_size("ctx"))
    raw = raw_pack(keys, values, doc_ids, queries[:, length - 2 :].reshape(-1))
    received = [
        raw_unpack(shifted(raw, "ctx", step, False), values.shape[1], row_count, 2 * row_count)
        for step in near
    ]
    window_keys = jnp.concatenate([part[1] for part in received], axis=1).astype(jnp.float32)
    window_feat = jnp.concatenate(
        [features(window_keys.reshape(local_heads, FD, -1)), k_feat], axis=2
    )
    window_values = jnp.concatenate(
        [part[0] for part in received] + [values.T], axis=1
    ).astype(jnp.float32)
    window_ids = jnp.concatenate([part[2] for part in received] + [doc_ids])
    tail_mask = (window_ids == doc_ids[length - 1]).astype(jnp.float32)
    tail_feat = window_feat * tail_mask[None, None, :]
    tail_state = jnp.einsum(
        "hft,hdt->hfd",
        tail_feat,
        window_values.reshape(local_heads, head_width, -1),
        precision=split_mode,
    )
    tail_normer = jnp.sum(tail_feat, axis=2)
    key_row = tail_state.size // head_width + -(-tail_normer.size // head_width)
    forward_piece = pack(tail_state, tail_normer, doc_ids[length - 1], jnp.zeros((1,), jnp.float32))
    join = packed_join(key_row)
    packed = fold(join, [shifted(forward_piece, "ctx", step, False) for step in far])
    state_in, normer_in, _ = unpack(packed, tail_state.shape, tail_normer.shape, 1)
    previous = received[-1] if near else raw_unpack(jnp.zeros_like(raw), values.shape[1], row_count, 2 * row_count)
    before = (
        previous[2][length - 2 :],
        previous[3].astype(jnp.float32).reshape(row_count, 2),
        state_in,
        normer_in,
    )
    query_ext = jnp.concatenate([before[1], query_rows], axis=1)
    ids_before = jnp.concatenate([before[0], doc_ids])
    q_conv = taps[0][:, None] * query_rows
    for offset in (1, 2):
        same_doc = (ids_before[2 - offset : 2 - offset + length] == doc_ids).astype(jnp.float32)
        q_conv = (
            q_conv
            + taps[offset][:, None]
            * query_ext[:, 2 - offset : 2 - offset + length]
            * same_doc[None, :]
        )
    carry_mask = (doc_ids == before[0][1]).astype(jnp.float32)

    def local_forward(q_conv_in, k_feat_in, values_in, state_in, normer_in):
        q_feat = features(q_conv_in.reshape(local_heads, FD, length))
        result = block_output(
            q_feat, k_feat_in, values_in, doc_ids, carry_mask, state_in, normer_in
        )
        return result.reshape(length, local_heads * head_width)

    _, local_pullback = jax.vjp(local_forward, q_conv, k_feat, head_values, before[2], before[3])
    grad_qconv, grad_kfeat, grad_heads, grad_state, grad_normer = local_pullback(grad_attn)
    backward_piece = pack(
        grad_state,
        grad_normer,
        doc_ids[0],
        jnp.concatenate([doc_ids[:2], grad_qconv[:, :2].reshape(-1)]),
    )
    packed = entering(backward_piece, "ctx", packed_join(key_row), True, reach)
    state_out, normer_out, edge = unpack(packed, grad_state.shape, grad_normer.shape, 2 + 2 * row_count)
    after = (edge[:2], edge[2:].reshape(row_count, 2), state_out, normer_out)
    head_mask = (doc_ids == after[0][0]).astype(jnp.float32)
    flowing = (
        jnp.einsum("hfd,shd->hfs", after[2], head_values, precision=split_mode)
        + after[3][:, :, None]
    )
    grad_kfeat = grad_kfeat + flowing * head_mask[None, None, :]
    grad_heads = grad_heads + jnp.einsum(
        "hfs,hfd->shd", k_feat * head_mask[None, None, :], after[2], precision=split_mode
    )
    (grad_key_heads,) = feature_pullback(grad_kfeat)
    grad_ext = jnp.concatenate([grad_qconv, after[1]], axis=1)
    ids_after = jnp.concatenate([doc_ids, after[0]])
    grad_queries = taps[0][:, None] * grad_qconv
    for offset in (1, 2):
        same_doc = (ids_after[offset : offset + length] == doc_ids).astype(jnp.float32)
        grad_queries = (
            grad_queries
            + taps[offset][:, None] * grad_ext[:, offset : offset + length] * same_doc[None, :]
        )
    grad_keys = grad_key_heads.reshape(local_heads * FD, length)
    grad_values = grad_heads.reshape(length, local_heads * head_width)
    return (grad_queries, grad_keys, grad_values)


def solution(mesh):
    in_specs = (
        P("head", "ctx"),
        P("head", "ctx"),
        P("ctx", "head"),
        P("ctx"),
        P(None, "head"),
        P("head", None),
        P("ctx", "head"),
    )
    out_specs = (P("head", "ctx"), P("head", "ctx"), P("ctx", "head"))
    return jax.shard_map(body, mesh=mesh, in_specs=in_specs, out_specs=out_specs, check_vma=False)
```

```python
import jax
import jax.numpy as jnp
import numpy as np
from jax import lax
from jax.sharding import PartitionSpec as P
from jax.experimental import pallas as pl
from jax.experimental.pallas import tpu as pltpu

FD = 16
MOST = 2048
INTERPRET = False


half_root = 0.7071067811865476
split_mode = lax.Precision.HIGH
exact_mode = lax.Precision.HIGHEST


def shifted(piece, axis, step, reverse):
    size = lax.axis_size(axis)
    if reverse:
        pairs = [(source, source - step) for source in range(step, size)]
    else:
        pairs = [(source, source + step) for source in range(size - step)]
    return lax.ppermute(piece, axis, pairs)


def fold(combine, pieces):
    total = pieces[0]
    for piece in pieces[1:]:
        total = combine(total, piece)
    return total


def window_steps(reach, size):
    fan = 1
    while fan * fan < reach:
        fan += 1
    near = [step for step in range(fan - 1, 0, -1) if step < size]
    far = [1 + fan * k for k in range(-(-reach // fan) - 1, -1, -1)]
    return near, [step for step in far if step < size]


def entering(shard, axis, combine, reverse, reach):
    near, far = window_steps(reach, lax.axis_size(axis))
    total = fold(combine, [shifted(shard, axis, step, reverse) for step in near] + [shard])
    return fold(combine, [shifted(total, axis, step, reverse) for step in far])


def rows_of(flat, lanes):
    count = -(-flat.size // lanes)
    return jnp.pad(flat, (0, count * lanes - flat.size)).reshape(count, lanes)


def raw_pack(keys, values, doc_ids, edge):
    lanes = keys.shape[1]
    parts = [values.T, keys, doc_ids.astype(keys.dtype)[None, :], rows_of(edge, lanes)]
    rows = sum(part.shape[0] for part in parts)
    parts.append(jnp.zeros((-rows % 16, lanes), keys.dtype))
    return jnp.concatenate(parts)


def raw_unpack(packed, value_rows, key_rows, edge_size):
    lanes = packed.shape[1]
    ids_row = value_rows + key_rows
    edge_rows = -(-edge_size // lanes)
    return (
        packed[:value_rows],
        packed[value_rows:ids_row],
        packed[ids_row].astype(jnp.float32),
        packed[ids_row + 1 : ids_row + 1 + edge_rows].reshape(-1)[:edge_size],
    )


def feature_tables(width):
    count = 1 + 2 * width + width * (width - 1) // 2
    left = np.zeros((count, width), np.float32)
    right = np.zeros((count, width), np.float32)
    left_one = np.zeros((count, 1), np.float32)
    right_one = np.zeros((count, 1), np.float32)
    weight = np.ones((count, 1), np.float32)
    left_one[0] = 1.0
    right_one[0] = 1.0
    for i in range(width):
        left[1 + i, i] = 1.0
        right_one[1 + i] = 1.0
        left[1 + width + i, i] = 1.0
        right[1 + width + i, i] = 1.0
        weight[1 + width + i] = half_root
    row_index, col_index = np.triu_indices(width, 1)
    for n, (i, j) in enumerate(zip(row_index, col_index)):
        left[1 + 2 * width + n, i] = 1.0
        right[1 + 2 * width + n, j] = 1.0
    return left, right, left_one, right_one, weight


def window_tables(heads, width):
    left, right, left_one, right_one, weight = feature_tables(width)
    count = left.shape[0]
    big_left = np.zeros((heads * count, heads * width), np.float32)
    big_right = np.zeros((heads * count, heads * width), np.float32)
    aux = np.zeros((heads * count, 128), np.float32)
    for h in range(heads):
        rows = slice(h * count, (h + 1) * count)
        big_left[rows, h * width : (h + 1) * width] = left
        big_right[rows, h * width : (h + 1) * width] = right
        aux[rows, 0:1] = left_one
        aux[rows, 1:2] = right_one
        aux[rows, 2:3] = weight
        aux[rows, 3] = h
    return big_left, big_right, aux


def window_state(pieces, heads, width, value_rows, out_rows):
    big_left, big_right, aux = window_tables(heads, width)
    feature_rows = big_left.shape[0]
    head_width = value_rows // heads
    key_rows = heads * width
    ids_row = value_rows + key_rows
    normer_rows = -(-feature_rows // head_width)
    key_row = feature_rows + normer_rows
    dims = (((1,), (1,)), ((), ()))

    def kernel(*refs):
        piece_refs = refs[: len(pieces)]
        left_ref, right_ref, aux_ref, out_ref = refs[len(pieces) :]
        own_ids = piece_refs[-1][ids_row : ids_row + 1, :].astype(jnp.float32)
        last = jnp.max(own_ids, axis=1, keepdims=True)
        block = aux_ref[...]
        left_one = block[:, 0:1]
        right_one = block[:, 1:2]
        weight = block[:, 2:3]
        head_of = block[:, 3:4]
        state = jnp.zeros((feature_rows, value_rows), jnp.float32)
        normer = jnp.zeros((8, feature_rows), jnp.float32)
        ones = jnp.ones((8, piece_refs[0].shape[1]), jnp.float32)
        for ref in piece_refs:
            ids = ref[ids_row : ids_row + 1, :].astype(jnp.float32)
            mask = (ids == last).astype(jnp.float32)
            scaled = ref[value_rows:ids_row, :].astype(jnp.float32) * 0.5
            first = jnp.dot(left_ref[...], scaled, precision=exact_mode, preferred_element_type=jnp.float32)
            second = jnp.dot(right_ref[...], scaled, precision=exact_mode, preferred_element_type=jnp.float32)
            feat = (first + left_one) * (second + right_one) * weight * mask
            high = feat.astype(jnp.bfloat16)
            low = (feat - high.astype(jnp.float32)).astype(jnp.bfloat16)
            vals = ref[0:value_rows, :]
            state = state + lax.dot_general(high, vals, dims, preferred_element_type=jnp.float32)
            state = state + lax.dot_general(low, vals, dims, preferred_element_type=jnp.float32)
            normer = normer + lax.dot_general(
                ones, feat, dims, precision=exact_mode, preferred_element_type=jnp.float32
            )
        chosen = jnp.zeros((feature_rows, head_width), jnp.float32)
        for h in range(heads):
            chosen = jnp.where(head_of == h, state[:, h * head_width : (h + 1) * head_width], chosen)
        out_ref[...] = jnp.zeros(out_ref.shape, jnp.float32)
        out_ref[0:feature_rows, :] = chosen
        for k in range(normer_rows):
            stop = min(feature_rows, (k + 1) * head_width)
            out_ref[feature_rows + k : feature_rows + k + 1, 0 : stop - k * head_width] = normer[
                0:1, k * head_width : stop
            ]
        out_ref[key_row : key_row + 1, :] = jnp.broadcast_to(last, (1, head_width))

    return pl.pallas_call(
        kernel,
        out_shape=jax.ShapeDtypeStruct((out_rows, head_width), jnp.float32),
        interpret=INTERPRET,
    )(*pieces, jnp.asarray(big_left), jnp.asarray(big_right), jnp.asarray(aux))


def features(entries):
    scaled = entries * 0.5
    left, right, left_one, right_one, weight = feature_tables(scaled.shape[-2])
    first = jnp.einsum("rk,...kt->...rt", left, scaled, precision=exact_mode) + left_one
    second = jnp.einsum("rk,...kt->...rt", right, scaled, precision=exact_mode) + right_one
    return first * second * weight


def block_output(q_feat, k_feat, head_values, doc_ids, carry_mask, state_in, normer_in):
    length = doc_ids.shape[0]
    causal = jnp.arange(length)[:, None] >= jnp.arange(length)[None, :]
    allowed = (causal & (doc_ids[:, None] == doc_ids[None, :])).astype(jnp.float32)
    scores = jnp.einsum("hft,hfs->hts", q_feat, k_feat, precision=split_mode) * allowed[None, :, :]
    numerator = jnp.einsum("hts,shd->thd", scores, head_values, precision=split_mode)
    numerator = numerator + carry_mask[:, None, None] * jnp.einsum(
        "hft,hfd->thd", q_feat, state_in, precision=split_mode
    )
    denominator = jnp.sum(scores, axis=2).T + carry_mask[:, None] * jnp.einsum(
        "hft,hf->th", q_feat, normer_in, precision=split_mode
    )
    return numerator / denominator[:, :, None]


def packed_join(key_row):
    def join(earlier, later):
        empty_later = later[key_row : key_row + 1] == 0.0
        same_doc = earlier[key_row : key_row + 1] == later[key_row : key_row + 1]
        row = lax.broadcasted_iota(jnp.int32, later.shape, 0)
        addend = jnp.where(same_doc & (row < key_row), earlier, 0.0)
        return jnp.where(empty_later, earlier, later + addend)

    return join


def pack(state, normer, key, edge):
    lanes = state.shape[-1]
    state_rows = state.reshape(-1, lanes)
    normer_flat = normer.reshape(-1)
    normer_rows = -(-normer_flat.size // lanes)
    normer_part = jnp.pad(normer_flat, (0, normer_rows * lanes - normer_flat.size))
    key_part = jnp.broadcast_to(key, (1, lanes))
    edge_rows = -(-edge.size // lanes)
    edge_part = jnp.pad(edge, (0, edge_rows * lanes - edge.size)).reshape(edge_rows, lanes)
    rows = state_rows.shape[0] + normer_rows + 1 + edge_rows
    tail = -rows % 8
    return jnp.concatenate(
        [
            state_rows,
            normer_part.reshape(normer_rows, lanes),
            key_part,
            edge_part,
            jnp.zeros((tail, lanes), state.dtype),
        ]
    )


def unpack(packed, state_shape, normer_shape, edge_size):
    lanes = state_shape[-1]
    state_rows = int(np.prod(state_shape[:-1]))
    normer_size = int(np.prod(normer_shape))
    key_row = state_rows + -(-normer_size // lanes)
    state = packed[:state_rows].reshape(state_shape)
    normer = packed[state_rows:key_row].reshape(-1)[:normer_size].reshape(normer_shape)
    edge_rows = -(-edge_size // lanes)
    edge = packed[key_row + 1 : key_row + 1 + edge_rows].reshape(-1)[:edge_size]
    return state, normer, edge


def body(queries, keys, values, seg_ids, conv_weight, out_weight, out_grad):
    local_heads = queries.shape[0] // FD
    length = queries.shape[1]
    head_width = values.shape[1] // local_heads
    reach = -(-(MOST - 1) // length)
    grad_attn = lax.dot_general(
        lax.all_gather(out_grad, "head", axis=1, tiled=True),
        out_weight,
        (((1,), (1,)), ((), ())),
        preferred_element_type=jnp.float32,
    )
    doc_ids = (seg_ids + 1).astype(jnp.float32)
    query_rows = queries.astype(jnp.float32)
    key_heads = keys.astype(jnp.float32).reshape(local_heads, FD, length)
    head_values = values.astype(jnp.float32).reshape(length, local_heads, head_width)
    taps = conv_weight.astype(jnp.float32)
    k_feat, feature_pullback = jax.vjp(features, key_heads)
    row_count = query_rows.shape[0]
    near, far = window_steps(reach, lax.axis_size("ctx"))
    raw = raw_pack(keys, values, doc_ids, queries[:, length - 2 :].reshape(-1))
    feature_count = 1 + 2 * FD + FD * (FD - 1) // 2
    state_shape = (local_heads, feature_count, head_width)
    normer_shape = (local_heads, feature_count)
    key_row = local_heads * feature_count + -(-local_heads * feature_count // head_width)
    out_rows = key_row + 2 + (-(key_row + 2) % 8)
    received = [shifted(raw, "ctx", step, False) for step in near]
    forward_piece = window_state(
        received + [raw],
        local_heads,
        FD,
        values.shape[1],
        out_rows,
    )
    join = packed_join(key_row)
    packed = fold(join, [shifted(forward_piece, "ctx", step, False) for step in far])
    state_in, normer_in, _ = unpack(packed, state_shape, normer_shape, 1)
    previous = raw_unpack(received[-1], values.shape[1], row_count, 2 * row_count)
    before = (
        previous[2][length - 2 :],
        previous[3].astype(jnp.float32).reshape(row_count, 2),
        state_in,
        normer_in,
    )
    query_ext = jnp.concatenate([before[1], query_rows], axis=1)
    ids_before = jnp.concatenate([before[0], doc_ids])
    q_conv = taps[0][:, None] * query_rows
    for offset in (1, 2):
        same_doc = (ids_before[2 - offset : 2 - offset + length] == doc_ids).astype(jnp.float32)
        q_conv = (
            q_conv
            + taps[offset][:, None]
            * query_ext[:, 2 - offset : 2 - offset + length]
            * same_doc[None, :]
        )
    carry_mask = (doc_ids == before[0][1]).astype(jnp.float32)

    def local_forward(q_conv_in, k_feat_in, values_in, state_in, normer_in):
        q_feat = features(q_conv_in.reshape(local_heads, FD, length))
        result = block_output(
            q_feat, k_feat_in, values_in, doc_ids, carry_mask, state_in, normer_in
        )
        return result.reshape(length, local_heads * head_width)

    _, local_pullback = jax.vjp(local_forward, q_conv, k_feat, head_values, before[2], before[3])
    grad_qconv, grad_kfeat, grad_heads, grad_state, grad_normer = local_pullback(grad_attn)
    backward_piece = pack(
        grad_state,
        grad_normer,
        doc_ids[0],
        jnp.concatenate([doc_ids[:2], grad_qconv[:, :2].reshape(-1)]),
    )
    packed = entering(backward_piece, "ctx", packed_join(key_row), True, reach)
    state_out, normer_out, edge = unpack(packed, grad_state.shape, grad_normer.shape, 2 + 2 * row_count)
    after = (edge[:2], edge[2:].reshape(row_count, 2), state_out, normer_out)
    head_mask = (doc_ids == after[0][0]).astype(jnp.float32)
    flowing = (
        jnp.einsum("hfd,shd->hfs", after[2], head_values, precision=split_mode)
        + after[3][:, :, None]
    )
    grad_kfeat = grad_kfeat + flowing * head_mask[None, None, :]
    grad_heads = grad_heads + jnp.einsum(
        "hfs,hfd->shd", k_feat * head_mask[None, None, :], after[2], precision=split_mode
    )
    (grad_key_heads,) = feature_pullback(grad_kfeat)
    grad_ext = jnp.concatenate([grad_qconv, after[1]], axis=1)
    ids_after = jnp.concatenate([doc_ids, after[0]])
    grad_queries = taps[0][:, None] * grad_qconv
    for offset in (1, 2):
        same_doc = (ids_after[offset : offset + length] == doc_ids).astype(jnp.float32)
        grad_queries = (
            grad_queries
            + taps[offset][:, None] * grad_ext[:, offset : offset + length] * same_doc[None, :]
        )
    grad_keys = grad_key_heads.reshape(local_heads * FD, length)
    grad_values = grad_heads.reshape(length, local_heads * head_width)
    return (grad_queries, grad_keys, grad_values)


def solution(mesh):
    in_specs = (
        P("head", "ctx"),
        P("head", "ctx"),
        P("ctx", "head"),
        P("ctx"),
        P(None, "head"),
        P("head", None),
        P("ctx", "head"),
    )
    out_specs = (P("head", "ctx"), P("head", "ctx"), P("ctx", "head"))
    return jax.shard_map(body, mesh=mesh, in_specs=in_specs, out_specs=out_specs, check_vma=False)
```

```python
import jax
import jax.numpy as jnp
import numpy as np
from jax import lax
from jax.sharding import PartitionSpec as P
from jax.experimental import pallas as pl
from jax.experimental.pallas import tpu as pltpu

FD = 16
MOST = 2048
INTERPRET = False


half_root = 0.7071067811865476
split_mode = lax.Precision.HIGH
exact_mode = lax.Precision.HIGHEST


def shifted(piece, axis, step, reverse):
    size = lax.axis_size(axis)
    if reverse:
        pairs = [(source, source - step) for source in range(step, size)]
    else:
        pairs = [(source, source + step) for source in range(size - step)]
    return lax.ppermute(piece, axis, pairs)


def fold(combine, pieces):
    total = pieces[0]
    for piece in pieces[1:]:
        total = combine(total, piece)
    return total


def window_steps(reach, size):
    fan = 1
    while fan * fan < reach:
        fan += 1
    near = [step for step in range(fan - 1, 0, -1) if step < size]
    far = [1 + fan * k for k in range(-(-reach // fan) - 1, -1, -1)]
    return near, [step for step in far if step < size]


def entering(shard, axis, combine, reverse, reach):
    near, far = window_steps(reach, lax.axis_size(axis))
    total = fold(combine, [shifted(shard, axis, step, reverse) for step in near] + [shard])
    return fold(combine, [shifted(total, axis, step, reverse) for step in far])


def rows_of(flat, lanes):
    count = -(-flat.size // lanes)
    return jnp.pad(flat, (0, count * lanes - flat.size)).reshape(count, lanes)


def raw_pack(keys, values, doc_ids, edge):
    lanes = keys.shape[1]
    parts = [values.T, keys, doc_ids.astype(keys.dtype)[None, :], rows_of(edge, lanes)]
    rows = sum(part.shape[0] for part in parts)
    parts.append(jnp.zeros((-rows % 16, lanes), keys.dtype))
    return jnp.concatenate(parts)


def raw_unpack(packed, value_rows, key_rows, edge_size):
    lanes = packed.shape[1]
    ids_row = value_rows + key_rows
    edge_rows = -(-edge_size // lanes)
    return (
        packed[:value_rows],
        packed[value_rows:ids_row],
        packed[ids_row].astype(jnp.float32),
        packed[ids_row + 1 : ids_row + 1 + edge_rows].reshape(-1)[:edge_size],
    )


def feature_tables(width):
    count = 1 + 2 * width + width * (width - 1) // 2
    left = np.zeros((count, width), np.float32)
    right = np.zeros((count, width), np.float32)
    left_one = np.zeros((count, 1), np.float32)
    right_one = np.zeros((count, 1), np.float32)
    weight = np.ones((count, 1), np.float32)
    left_one[0] = 1.0
    right_one[0] = 1.0
    for i in range(width):
        left[1 + i, i] = 1.0
        right_one[1 + i] = 1.0
        left[1 + width + i, i] = 1.0
        right[1 + width + i, i] = 1.0
        weight[1 + width + i] = half_root
    row_index, col_index = np.triu_indices(width, 1)
    for n, (i, j) in enumerate(zip(row_index, col_index)):
        left[1 + 2 * width + n, i] = 1.0
        right[1 + 2 * width + n, j] = 1.0
    return left, right, left_one, right_one, weight


def window_tables(heads, width):
    left, right, left_one, right_one, weight = feature_tables(width)
    count = left.shape[0]
    big_left = np.zeros((heads * count, heads * width), np.float32)
    big_right = np.zeros((heads * count, heads * width), np.float32)
    aux = np.zeros((heads * count, 128), np.float32)
    for h in range(heads):
        rows = slice(h * count, (h + 1) * count)
        big_left[rows, h * width : (h + 1) * width] = left
        big_right[rows, h * width : (h + 1) * width] = right
        aux[rows, 0:1] = left_one
        aux[rows, 1:2] = right_one
        aux[rows, 2:3] = weight
        aux[rows, 3] = h
    return big_left, big_right, aux


def window_state(pieces, heads, width, value_rows, out_rows):
    big_left, big_right, aux = window_tables(heads, width)
    feature_rows = big_left.shape[0]
    head_width = value_rows // heads
    key_rows = heads * width
    ids_row = value_rows + key_rows
    normer_rows = -(-feature_rows // head_width)
    key_row = feature_rows + normer_rows
    dims = (((1,), (1,)), ((), ()))

    def kernel(*refs):
        piece_refs = refs[: len(pieces)]
        left_ref, right_ref, aux_ref, out_ref = refs[len(pieces) :]
        own_ids = piece_refs[-1][ids_row : ids_row + 1, :].astype(jnp.float32)
        last = jnp.max(own_ids, axis=1, keepdims=True)
        block = aux_ref[...]
        left_one = block[:, 0:1]
        right_one = block[:, 1:2]
        weight = block[:, 2:3]
        head_of = block[:, 3:4]
        state = jnp.zeros((feature_rows, value_rows), jnp.float32)
        normer = jnp.zeros((8, feature_rows), jnp.float32)
        ones = jnp.ones((8, piece_refs[0].shape[1]), jnp.float32)
        for ref in piece_refs:
            ids = ref[ids_row : ids_row + 1, :].astype(jnp.float32)
            mask = (ids == last).astype(jnp.float32)
            scaled = ref[value_rows:ids_row, :] * jnp.asarray(0.5, ref.dtype)
            first = jnp.dot(left_ref[...], scaled, preferred_element_type=jnp.float32)
            second = jnp.dot(right_ref[...], scaled, preferred_element_type=jnp.float32)
            feat = (first + left_one) * (second + right_one) * weight * mask
            high = feat.astype(jnp.bfloat16)
            low = (feat - high.astype(jnp.float32)).astype(jnp.bfloat16)
            vals = ref[0:value_rows, :]
            state = state + lax.dot_general(high, vals, dims, preferred_element_type=jnp.float32)
            state = state + lax.dot_general(low, vals, dims, preferred_element_type=jnp.float32)
            normer = normer + lax.dot_general(
                ones, feat, dims, precision=exact_mode, preferred_element_type=jnp.float32
            )
        chosen = jnp.zeros((feature_rows, head_width), jnp.float32)
        for h in range(heads):
            chosen = jnp.where(head_of == h, state[:, h * head_width : (h + 1) * head_width], chosen)
        out_ref[...] = jnp.zeros(out_ref.shape, jnp.float32)
        out_ref[0:feature_rows, :] = chosen
        for k in range(normer_rows):
            stop = min(feature_rows, (k + 1) * head_width)
            out_ref[feature_rows + k : feature_rows + k + 1, 0 : stop - k * head_width] = normer[
                0:1, k * head_width : stop
            ]
        out_ref[key_row : key_row + 1, :] = jnp.broadcast_to(last, (1, head_width))

    return pl.pallas_call(
        kernel,
        out_shape=jax.ShapeDtypeStruct((out_rows, head_width), jnp.float32),
        interpret=INTERPRET,
    )(
        *pieces,
        jnp.asarray(big_left, jnp.bfloat16),
        jnp.asarray(big_right, jnp.bfloat16),
        jnp.asarray(aux),
    )


def features(entries):
    scaled = entries * 0.5
    left, right, left_one, right_one, weight = feature_tables(scaled.shape[-2])
    first = jnp.einsum("rk,...kt->...rt", left, scaled, precision=exact_mode) + left_one
    second = jnp.einsum("rk,...kt->...rt", right, scaled, precision=exact_mode) + right_one
    return first * second * weight


def block_output(q_feat, k_feat, head_values, doc_ids, carry_mask, state_in, normer_in):
    length = doc_ids.shape[0]
    causal = jnp.arange(length)[:, None] >= jnp.arange(length)[None, :]
    allowed = (causal & (doc_ids[:, None] == doc_ids[None, :])).astype(jnp.float32)
    scores = jnp.einsum("hft,hfs->hts", q_feat, k_feat, precision=split_mode) * allowed[None, :, :]
    numerator = jnp.einsum("hts,shd->thd", scores, head_values, precision=split_mode)
    numerator = numerator + carry_mask[:, None, None] * jnp.einsum(
        "hft,hfd->thd", q_feat, state_in, precision=split_mode
    )
    denominator = jnp.sum(scores, axis=2).T + carry_mask[:, None] * jnp.einsum(
        "hft,hf->th", q_feat, normer_in, precision=split_mode
    )
    return numerator / denominator[:, :, None]


def packed_join(key_row):
    def join(earlier, later):
        empty_later = later[key_row : key_row + 1] == 0.0
        same_doc = earlier[key_row : key_row + 1] == later[key_row : key_row + 1]
        row = lax.broadcasted_iota(jnp.int32, later.shape, 0)
        addend = jnp.where(same_doc & (row < key_row), earlier, 0.0)
        return jnp.where(empty_later, earlier, later + addend)

    return join


def pack(state, normer, key, edge):
    lanes = state.shape[-1]
    state_rows = state.reshape(-1, lanes)
    normer_flat = normer.reshape(-1)
    normer_rows = -(-normer_flat.size // lanes)
    normer_part = jnp.pad(normer_flat, (0, normer_rows * lanes - normer_flat.size))
    key_part = jnp.broadcast_to(key, (1, lanes))
    edge_rows = -(-edge.size // lanes)
    edge_part = jnp.pad(edge, (0, edge_rows * lanes - edge.size)).reshape(edge_rows, lanes)
    rows = state_rows.shape[0] + normer_rows + 1 + edge_rows
    tail = -rows % 8
    return jnp.concatenate(
        [
            state_rows,
            normer_part.reshape(normer_rows, lanes),
            key_part,
            edge_part,
            jnp.zeros((tail, lanes), state.dtype),
        ]
    )


def unpack(packed, state_shape, normer_shape, edge_size):
    lanes = state_shape[-1]
    state_rows = int(np.prod(state_shape[:-1]))
    normer_size = int(np.prod(normer_shape))
    key_row = state_rows + -(-normer_size // lanes)
    state = packed[:state_rows].reshape(state_shape)
    normer = packed[state_rows:key_row].reshape(-1)[:normer_size].reshape(normer_shape)
    edge_rows = -(-edge_size // lanes)
    edge = packed[key_row + 1 : key_row + 1 + edge_rows].reshape(-1)[:edge_size]
    return state, normer, edge


def body(queries, keys, values, seg_ids, conv_weight, out_weight, out_grad):
    local_heads = queries.shape[0] // FD
    length = queries.shape[1]
    head_width = values.shape[1] // local_heads
    reach = -(-(MOST - 1) // length)
    grad_attn = lax.dot_general(
        lax.all_gather(out_grad, "head", axis=1, tiled=True),
        out_weight,
        (((1,), (1,)), ((), ())),
        preferred_element_type=jnp.float32,
    )
    doc_ids = (seg_ids + 1).astype(jnp.float32)
    query_rows = queries.astype(jnp.float32)
    key_heads = keys.astype(jnp.float32).reshape(local_heads, FD, length)
    head_values = values.astype(jnp.float32).reshape(length, local_heads, head_width)
    taps = conv_weight.astype(jnp.float32)
    k_feat, feature_pullback = jax.vjp(features, key_heads)
    row_count = query_rows.shape[0]
    near, far = window_steps(reach, lax.axis_size("ctx"))
    raw = raw_pack(keys, values, doc_ids, queries[:, length - 2 :].reshape(-1))
    feature_count = 1 + 2 * FD + FD * (FD - 1) // 2
    state_shape = (local_heads, feature_count, head_width)
    normer_shape = (local_heads, feature_count)
    key_row = local_heads * feature_count + -(-local_heads * feature_count // head_width)
    out_rows = key_row + 2 + (-(key_row + 2) % 8)
    received = [shifted(raw, "ctx", step, False) for step in near]
    forward_piece = window_state(
        received + [raw],
        local_heads,
        FD,
        values.shape[1],
        out_rows,
    )
    join = packed_join(key_row)
    packed = fold(join, [shifted(forward_piece, "ctx", step, False) for step in far])
    state_in, normer_in, _ = unpack(packed, state_shape, normer_shape, 1)
    previous = raw_unpack(received[-1], values.shape[1], row_count, 2 * row_count)
    before = (
        previous[2][length - 2 :],
        previous[3].astype(jnp.float32).reshape(row_count, 2),
        state_in,
        normer_in,
    )
    query_ext = jnp.concatenate([before[1], query_rows], axis=1)
    ids_before = jnp.concatenate([before[0], doc_ids])
    q_conv = taps[0][:, None] * query_rows
    for offset in (1, 2):
        same_doc = (ids_before[2 - offset : 2 - offset + length] == doc_ids).astype(jnp.float32)
        q_conv = (
            q_conv
            + taps[offset][:, None]
            * query_ext[:, 2 - offset : 2 - offset + length]
            * same_doc[None, :]
        )
    carry_mask = (doc_ids == before[0][1]).astype(jnp.float32)

    def local_forward(q_conv_in, k_feat_in, values_in, state_in, normer_in):
        q_feat = features(q_conv_in.reshape(local_heads, FD, length))
        result = block_output(
            q_feat, k_feat_in, values_in, doc_ids, carry_mask, state_in, normer_in
        )
        return result.reshape(length, local_heads * head_width)

    _, local_pullback = jax.vjp(local_forward, q_conv, k_feat, head_values, before[2], before[3])
    grad_qconv, grad_kfeat, grad_heads, grad_state, grad_normer = local_pullback(grad_attn)
    backward_piece = pack(
        grad_state,
        grad_normer,
        doc_ids[0],
        jnp.concatenate([doc_ids[:2], grad_qconv[:, :2].reshape(-1)]),
    )
    packed = entering(backward_piece, "ctx", packed_join(key_row), True, reach)
    state_out, normer_out, edge = unpack(packed, grad_state.shape, grad_normer.shape, 2 + 2 * row_count)
    after = (edge[:2], edge[2:].reshape(row_count, 2), state_out, normer_out)
    head_mask = (doc_ids == after[0][0]).astype(jnp.float32)
    flowing = (
        jnp.einsum("hfd,shd->hfs", after[2], head_values, precision=split_mode)
        + after[3][:, :, None]
    )
    grad_kfeat = grad_kfeat + flowing * head_mask[None, None, :]
    grad_heads = grad_heads + jnp.einsum(
        "hfs,hfd->shd", k_feat * head_mask[None, None, :], after[2], precision=split_mode
    )
    (grad_key_heads,) = feature_pullback(grad_kfeat)
    grad_ext = jnp.concatenate([grad_qconv, after[1]], axis=1)
    ids_after = jnp.concatenate([doc_ids, after[0]])
    grad_queries = taps[0][:, None] * grad_qconv
    for offset in (1, 2):
        same_doc = (ids_after[offset : offset + length] == doc_ids).astype(jnp.float32)
        grad_queries = (
            grad_queries
            + taps[offset][:, None] * grad_ext[:, offset : offset + length] * same_doc[None, :]
        )
    grad_keys = grad_key_heads.reshape(local_heads * FD, length)
    grad_values = grad_heads.reshape(length, local_heads * head_width)
    return (grad_queries, grad_keys, grad_values)


def solution(mesh):
    in_specs = (
        P("head", "ctx"),
        P("head", "ctx"),
        P("ctx", "head"),
        P("ctx"),
        P(None, "head"),
        P("head", None),
        P("ctx", "head"),
    )
    out_specs = (P("head", "ctx"), P("head", "ctx"), P("ctx", "head"))
    return jax.shard_map(body, mesh=mesh, in_specs=in_specs, out_specs=out_specs, check_vma=False)
```

```python
import jax
import jax.numpy as jnp
import numpy as np
from jax import lax
from jax.sharding import PartitionSpec as P
from jax.experimental import pallas as pl
from jax.experimental.pallas import tpu as pltpu

FD = 16
MOST = 2048
INTERPRET = False


half_root = 0.7071067811865476
split_mode = lax.Precision.HIGH
exact_mode = lax.Precision.HIGHEST


def shifted(piece, axis, step, reverse):
    size = lax.axis_size(axis)
    if reverse:
        pairs = [(source, source - step) for source in range(step, size)]
    else:
        pairs = [(source, source + step) for source in range(size - step)]
    return lax.ppermute(piece, axis, pairs)


def fold(combine, pieces):
    total = pieces[0]
    for piece in pieces[1:]:
        total = combine(total, piece)
    return total


def window_steps(reach, size):
    fan = 1
    while fan * fan < reach:
        fan += 1
    near = [step for step in range(fan - 1, 0, -1) if step < size]
    far = [1 + fan * k for k in range(-(-reach // fan) - 1, -1, -1)]
    return near, [step for step in far if step < size]


def entering(shard, axis, combine, reverse, reach):
    near, far = window_steps(reach, lax.axis_size(axis))
    total = fold(combine, [shifted(shard, axis, step, reverse) for step in near] + [shard])
    return fold(combine, [shifted(total, axis, step, reverse) for step in far])


def rows_of(flat, lanes):
    count = -(-flat.size // lanes)
    return jnp.pad(flat, (0, count * lanes - flat.size)).reshape(count, lanes)


def raw_pack(keys, values, doc_ids, edge):
    lanes = keys.shape[1]
    parts = [values.T, keys, doc_ids.astype(keys.dtype)[None, :], rows_of(edge, lanes)]
    rows = sum(part.shape[0] for part in parts)
    parts.append(jnp.zeros((-rows % 16, lanes), keys.dtype))
    return jnp.concatenate(parts)


def raw_unpack(packed, value_rows, key_rows, edge_size):
    lanes = packed.shape[1]
    ids_row = value_rows + key_rows
    edge_rows = -(-edge_size // lanes)
    return (
        packed[:value_rows],
        packed[value_rows:ids_row],
        packed[ids_row].astype(jnp.float32),
        packed[ids_row + 1 : ids_row + 1 + edge_rows].reshape(-1)[:edge_size],
    )


def feature_tables(width):
    count = 1 + 2 * width + width * (width - 1) // 2
    left = np.zeros((count, width), np.float32)
    right = np.zeros((count, width), np.float32)
    left_one = np.zeros((count, 1), np.float32)
    right_one = np.zeros((count, 1), np.float32)
    weight = np.ones((count, 1), np.float32)
    left_one[0] = 1.0
    right_one[0] = 1.0
    for i in range(width):
        left[1 + i, i] = 1.0
        right_one[1 + i] = 1.0
        left[1 + width + i, i] = 1.0
        right[1 + width + i, i] = 1.0
        weight[1 + width + i] = half_root
    row_index, col_index = np.triu_indices(width, 1)
    for n, (i, j) in enumerate(zip(row_index, col_index)):
        left[1 + 2 * width + n, i] = 1.0
        right[1 + 2 * width + n, j] = 1.0
    return left, right, left_one, right_one, weight


def window_tables(heads, width):
    left, right, left_one, right_one, weight = feature_tables(width)
    count = left.shape[0]
    big_left = np.zeros((heads * count, heads * width), np.float32)
    big_right = np.zeros((heads * count, heads * width), np.float32)
    aux = np.zeros((heads * count, 128), np.float32)
    for h in range(heads):
        rows = slice(h * count, (h + 1) * count)
        big_left[rows, h * width : (h + 1) * width] = left
        big_right[rows, h * width : (h + 1) * width] = right
        aux[rows, 0:1] = left_one
        aux[rows, 1:2] = right_one
        aux[rows, 2:3] = weight
        aux[rows, 3] = h
    return big_left, big_right, aux


def window_state(pieces, heads, width, value_rows, out_rows):
    big_left, big_right, aux = window_tables(heads, width)
    feature_rows = big_left.shape[0]
    head_width = value_rows // heads
    key_rows = heads * width
    ids_row = value_rows + key_rows
    normer_rows = -(-feature_rows // head_width)
    key_row = feature_rows + normer_rows
    dims = (((1,), (1,)), ((), ()))

    def kernel(*refs):
        piece_refs = refs[: len(pieces)]
        left_ref, right_ref, aux_ref, out_ref = refs[len(pieces) :]
        own_ids = piece_refs[-1][ids_row : ids_row + 1, :].astype(jnp.float32)
        last = jnp.max(own_ids, axis=1, keepdims=True)
        block = aux_ref[...]
        left_one = block[:, 0:1]
        right_one = block[:, 1:2]
        weight = block[:, 2:3]
        head_of = block[:, 3:4]
        state = jnp.zeros((feature_rows, value_rows), jnp.float32)
        normer = jnp.zeros((8, feature_rows), jnp.float32)
        ones = jnp.ones((8, piece_refs[0].shape[1]), jnp.float32)
        for ref in piece_refs:
            ids = ref[ids_row : ids_row + 1, :].astype(jnp.float32)
            mask = (ids == last).astype(jnp.float32)
            scaled = ref[value_rows:ids_row, :] * jnp.asarray(0.5, ref.dtype)
            first = jnp.dot(left_ref[...], scaled, preferred_element_type=jnp.float32)
            second = jnp.dot(right_ref[...], scaled, preferred_element_type=jnp.float32)
            feat = (first + left_one) * (second + right_one) * weight * mask
            high = feat.astype(jnp.bfloat16)
            low = (feat - high.astype(jnp.float32)).astype(jnp.bfloat16)
            vals = ref[0:value_rows, :]
            state = state + lax.dot_general(high, vals, dims, preferred_element_type=jnp.float32)
            state = state + lax.dot_general(low, vals, dims, preferred_element_type=jnp.float32)
            normer = normer + lax.dot_general(
                ones, feat, dims, precision=exact_mode, preferred_element_type=jnp.float32
            )
        chosen = jnp.zeros((feature_rows, head_width), jnp.float32)
        for h in range(heads):
            chosen = jnp.where(head_of == h, state[:, h * head_width : (h + 1) * head_width], chosen)
        out_ref[...] = jnp.zeros(out_ref.shape, jnp.float32)
        out_ref[0:feature_rows, :] = chosen
        for k in range(normer_rows):
            stop = min(feature_rows, (k + 1) * head_width)
            out_ref[feature_rows + k : feature_rows + k + 1, 0 : stop - k * head_width] = normer[
                0:1, k * head_width : stop
            ]
        out_ref[key_row : key_row + 1, :] = jnp.broadcast_to(last, (1, head_width))

    return pl.pallas_call(
        kernel,
        out_shape=jax.ShapeDtypeStruct((out_rows, head_width), jnp.float32),
        interpret=INTERPRET,
    )(
        *pieces,
        jnp.asarray(big_left, jnp.bfloat16),
        jnp.asarray(big_right, jnp.bfloat16),
        jnp.asarray(aux),
    )


def features(entries):
    scaled = entries * 0.5
    left, right, left_one, right_one, weight = feature_tables(scaled.shape[-2])
    first = jnp.einsum("rk,...kt->...rt", left, scaled, precision=exact_mode) + left_one
    second = jnp.einsum("rk,...kt->...rt", right, scaled, precision=exact_mode) + right_one
    return first * second * weight


def block_output(q_feat, k_feat, head_values, doc_ids, carry_mask, state_in, normer_in):
    length = doc_ids.shape[0]
    causal = jnp.arange(length)[:, None] >= jnp.arange(length)[None, :]
    allowed = (causal & (doc_ids[:, None] == doc_ids[None, :])).astype(jnp.float32)
    scores = jnp.einsum("hft,hfs->hts", q_feat, k_feat, precision=split_mode) * allowed[None, :, :]
    numerator = jnp.einsum("hts,shd->thd", scores, head_values, precision=split_mode)
    numerator = numerator + carry_mask[:, None, None] * jnp.einsum(
        "hft,hfd->thd", q_feat, state_in, precision=split_mode
    )
    denominator = jnp.sum(scores, axis=2).T + carry_mask[:, None] * jnp.einsum(
        "hft,hf->th", q_feat, normer_in, precision=split_mode
    )
    return numerator / denominator[:, :, None]


def packed_join(key_row):
    def join(earlier, later):
        empty_later = later[key_row : key_row + 1] == 0.0
        same_doc = earlier[key_row : key_row + 1] == later[key_row : key_row + 1]
        row = lax.broadcasted_iota(jnp.int32, later.shape, 0)
        addend = jnp.where(same_doc & (row < key_row), earlier, 0.0)
        return jnp.where(empty_later, earlier, later + addend)

    return join


def pack(state, normer, key, edge):
    lanes = state.shape[-1]
    state_rows = state.reshape(-1, lanes)
    normer_flat = normer.reshape(-1)
    normer_rows = -(-normer_flat.size // lanes)
    normer_part = jnp.pad(normer_flat, (0, normer_rows * lanes - normer_flat.size))
    key_part = jnp.broadcast_to(key, (1, lanes))
    edge_rows = -(-edge.size // lanes)
    edge_part = jnp.pad(edge, (0, edge_rows * lanes - edge.size)).reshape(edge_rows, lanes)
    rows = state_rows.shape[0] + normer_rows + 1 + edge_rows
    tail = -rows % 8
    return jnp.concatenate(
        [
            state_rows,
            normer_part.reshape(normer_rows, lanes),
            key_part,
            edge_part,
            jnp.zeros((tail, lanes), state.dtype),
        ]
    )


def unpack(packed, state_shape, normer_shape, edge_size):
    lanes = state_shape[-1]
    state_rows = int(np.prod(state_shape[:-1]))
    normer_size = int(np.prod(normer_shape))
    key_row = state_rows + -(-normer_size // lanes)
    state = packed[:state_rows].reshape(state_shape)
    normer = packed[state_rows:key_row].reshape(-1)[:normer_size].reshape(normer_shape)
    edge_rows = -(-edge_size // lanes)
    edge = packed[key_row + 1 : key_row + 1 + edge_rows].reshape(-1)[:edge_size]
    return state, normer, edge


def body(queries, keys, values, seg_ids, conv_weight, out_weight, out_grad):
    local_heads = queries.shape[0] // FD
    length = queries.shape[1]
    head_width = values.shape[1] // local_heads
    reach = -(-(MOST - 1) // length)
    grad_attn = lax.dot_general(
        lax.all_gather(out_grad, "head", axis=1, tiled=True),
        out_weight,
        (((1,), (1,)), ((), ())),
        preferred_element_type=jnp.float32,
    )
    doc_ids = (seg_ids + 1).astype(jnp.float32)
    query_rows = queries.astype(jnp.float32)
    key_heads = keys.astype(jnp.float32).reshape(local_heads, FD, length)
    head_values = values.astype(jnp.float32).reshape(length, local_heads, head_width)
    taps = conv_weight.astype(jnp.float32)
    row_count = query_rows.shape[0]
    near, far = window_steps(reach, lax.axis_size("ctx"))
    raw = raw_pack(keys, values, doc_ids, queries[:, length - 2 :].reshape(-1))
    feature_count = 1 + 2 * FD + FD * (FD - 1) // 2
    state_shape = (local_heads, feature_count, head_width)
    normer_shape = (local_heads, feature_count)
    key_row = local_heads * feature_count + -(-local_heads * feature_count // head_width)
    out_rows = key_row + 2 + (-(key_row + 2) % 8)
    received = [shifted(raw, "ctx", step, False) for step in near]
    forward_piece = window_state(
        received + [raw],
        local_heads,
        FD,
        values.shape[1],
        out_rows,
    )
    key_late, forward_piece = lax.optimization_barrier((key_heads, forward_piece))
    k_feat, feature_pullback = jax.vjp(features, key_late)
    join = packed_join(key_row)
    packed = fold(join, [shifted(forward_piece, "ctx", step, False) for step in far])
    state_in, normer_in, _ = unpack(packed, state_shape, normer_shape, 1)
    previous = raw_unpack(received[-1], values.shape[1], row_count, 2 * row_count)
    before = (
        previous[2][length - 2 :],
        previous[3].astype(jnp.float32).reshape(row_count, 2),
        state_in,
        normer_in,
    )
    query_ext = jnp.concatenate([before[1], query_rows], axis=1)
    ids_before = jnp.concatenate([before[0], doc_ids])
    q_conv = taps[0][:, None] * query_rows
    for offset in (1, 2):
        same_doc = (ids_before[2 - offset : 2 - offset + length] == doc_ids).astype(jnp.float32)
        q_conv = (
            q_conv
            + taps[offset][:, None]
            * query_ext[:, 2 - offset : 2 - offset + length]
            * same_doc[None, :]
        )
    carry_mask = (doc_ids == before[0][1]).astype(jnp.float32)

    def local_forward(q_conv_in, k_feat_in, values_in, state_in, normer_in):
        q_feat = features(q_conv_in.reshape(local_heads, FD, length))
        result = block_output(
            q_feat, k_feat_in, values_in, doc_ids, carry_mask, state_in, normer_in
        )
        return result.reshape(length, local_heads * head_width)

    _, local_pullback = jax.vjp(local_forward, q_conv, k_feat, head_values, before[2], before[3])
    grad_qconv, grad_kfeat, grad_heads, grad_state, grad_normer = local_pullback(grad_attn)
    backward_piece = pack(
        grad_state,
        grad_normer,
        doc_ids[0],
        jnp.concatenate([doc_ids[:2], grad_qconv[:, :2].reshape(-1)]),
    )
    packed = entering(backward_piece, "ctx", packed_join(key_row), True, reach)
    state_out, normer_out, edge = unpack(packed, grad_state.shape, grad_normer.shape, 2 + 2 * row_count)
    after = (edge[:2], edge[2:].reshape(row_count, 2), state_out, normer_out)
    head_mask = (doc_ids == after[0][0]).astype(jnp.float32)
    flowing = (
        jnp.einsum("hfd,shd->hfs", after[2], head_values, precision=split_mode)
        + after[3][:, :, None]
    )
    grad_kfeat = grad_kfeat + flowing * head_mask[None, None, :]
    grad_heads = grad_heads + jnp.einsum(
        "hfs,hfd->shd", k_feat * head_mask[None, None, :], after[2], precision=split_mode
    )
    (grad_key_heads,) = feature_pullback(grad_kfeat)
    grad_ext = jnp.concatenate([grad_qconv, after[1]], axis=1)
    ids_after = jnp.concatenate([doc_ids, after[0]])
    grad_queries = taps[0][:, None] * grad_qconv
    for offset in (1, 2):
        same_doc = (ids_after[offset : offset + length] == doc_ids).astype(jnp.float32)
        grad_queries = (
            grad_queries
            + taps[offset][:, None] * grad_ext[:, offset : offset + length] * same_doc[None, :]
        )
    grad_keys = grad_key_heads.reshape(local_heads * FD, length)
    grad_values = grad_heads.reshape(length, local_heads * head_width)
    return (grad_queries, grad_keys, grad_values)


def solution(mesh):
    in_specs = (
        P("head", "ctx"),
        P("head", "ctx"),
        P("ctx", "head"),
        P("ctx"),
        P(None, "head"),
        P("head", None),
        P("ctx", "head"),
    )
    out_specs = (P("head", "ctx"), P("head", "ctx"), P("ctx", "head"))
    return jax.shard_map(body, mesh=mesh, in_specs=in_specs, out_specs=out_specs, check_vma=False)
```

```python
import jax
import jax.numpy as jnp
import numpy as np
from jax import lax
from jax.sharding import PartitionSpec as P
from jax.experimental import pallas as pl
from jax.experimental.pallas import tpu as pltpu

FD = 16
MOST = 2048
INTERPRET = False


half_root = 0.7071067811865476
split_mode = lax.Precision.HIGH
exact_mode = lax.Precision.HIGHEST


def shifted(piece, axis, step, reverse):
    size = lax.axis_size(axis)
    if reverse:
        pairs = [(source, source - step) for source in range(step, size)]
    else:
        pairs = [(source, source + step) for source in range(size - step)]
    return lax.ppermute(piece, axis, pairs)


def gather_columns(block, axis):
    size, here = (lax.axis_size(axis), lax.axis_index(axis))
    held = block[None]
    step = 1
    while step < size:
        pairs = [(source, (source + step) % size) for source in range(size)]
        held = jnp.concatenate([held, lax.ppermute(held, axis, pairs)], axis=0)
        step *= 2
    turned = held[:size][::-1]
    doubled = jnp.concatenate([turned, turned], axis=0)
    ordered = lax.dynamic_slice_in_dim(doubled, size - 1 - here, size, axis=0)
    return ordered.transpose(1, 0, 2).reshape(block.shape[0], size * block.shape[1])


def fold(combine, pieces):
    total = pieces[0]
    for piece in pieces[1:]:
        total = combine(total, piece)
    return total


def window_steps(reach, size):
    fan = 1
    while fan * fan < reach:
        fan += 1
    near = [step for step in range(fan - 1, 0, -1) if step < size]
    far = [1 + fan * k for k in range(-(-reach // fan) - 1, -1, -1)]
    return near, [step for step in far if step < size]


def entering(shard, axis, combine, reverse, reach):
    near, far = window_steps(reach, lax.axis_size(axis))
    total = fold(combine, [shifted(shard, axis, step, reverse) for step in near] + [shard])
    return fold(combine, [shifted(total, axis, step, reverse) for step in far])


def rows_of(flat, lanes):
    count = -(-flat.size // lanes)
    return jnp.pad(flat, (0, count * lanes - flat.size)).reshape(count, lanes)


def raw_pack(keys, values, doc_ids, edge):
    lanes = keys.shape[1]
    parts = [values.T, keys, doc_ids.astype(keys.dtype)[None, :], rows_of(edge, lanes)]
    rows = sum(part.shape[0] for part in parts)
    parts.append(jnp.zeros((-rows % 16, lanes), keys.dtype))
    return jnp.concatenate(parts)


def raw_unpack(packed, value_rows, key_rows, edge_size):
    lanes = packed.shape[1]
    ids_row = value_rows + key_rows
    edge_rows = -(-edge_size // lanes)
    return (
        packed[:value_rows],
        packed[value_rows:ids_row],
        packed[ids_row].astype(jnp.float32),
        packed[ids_row + 1 : ids_row + 1 + edge_rows].reshape(-1)[:edge_size],
    )


def feature_tables(width):
    count = 1 + 2 * width + width * (width - 1) // 2
    left = np.zeros((count, width), np.float32)
    right = np.zeros((count, width), np.float32)
    left_one = np.zeros((count, 1), np.float32)
    right_one = np.zeros((count, 1), np.float32)
    weight = np.ones((count, 1), np.float32)
    left_one[0] = 1.0
    right_one[0] = 1.0
    for i in range(width):
        left[1 + i, i] = 1.0
        right_one[1 + i] = 1.0
        left[1 + width + i, i] = 1.0
        right[1 + width + i, i] = 1.0
        weight[1 + width + i] = half_root
    row_index, col_index = np.triu_indices(width, 1)
    for n, (i, j) in enumerate(zip(row_index, col_index)):
        left[1 + 2 * width + n, i] = 1.0
        right[1 + 2 * width + n, j] = 1.0
    return left, right, left_one, right_one, weight


def window_tables(heads, width):
    left, right, left_one, right_one, weight = feature_tables(width)
    count = left.shape[0]
    big_left = np.zeros((heads * count, heads * width), np.float32)
    big_right = np.zeros((heads * count, heads * width), np.float32)
    aux = np.zeros((heads * count, 128), np.float32)
    for h in range(heads):
        rows = slice(h * count, (h + 1) * count)
        big_left[rows, h * width : (h + 1) * width] = left
        big_right[rows, h * width : (h + 1) * width] = right
        aux[rows, 0:1] = left_one
        aux[rows, 1:2] = right_one
        aux[rows, 2:3] = weight
        aux[rows, 3] = h
    return big_left, big_right, aux


def window_state(pieces, heads, width, value_rows, out_rows):
    big_left, big_right, aux = window_tables(heads, width)
    feature_rows = big_left.shape[0]
    head_width = value_rows // heads
    key_rows = heads * width
    ids_row = value_rows + key_rows
    normer_rows = -(-feature_rows // head_width)
    key_row = feature_rows + normer_rows
    dims = (((1,), (1,)), ((), ()))

    def kernel(*refs):
        piece_refs = refs[: len(pieces)]
        left_ref, right_ref, aux_ref, out_ref = refs[len(pieces) :]
        own_ids = piece_refs[-1][ids_row : ids_row + 1, :].astype(jnp.float32)
        last = jnp.max(own_ids, axis=1, keepdims=True)
        block = aux_ref[...]
        left_one = block[:, 0:1]
        right_one = block[:, 1:2]
        weight = block[:, 2:3]
        head_of = block[:, 3:4]
        state = jnp.zeros((feature_rows, value_rows), jnp.float32)
        normer = jnp.zeros((8, feature_rows), jnp.float32)
        ones = jnp.ones((8, piece_refs[0].shape[1]), jnp.float32)
        for ref in piece_refs:
            ids = ref[ids_row : ids_row + 1, :].astype(jnp.float32)
            mask = (ids == last).astype(jnp.float32)
            scaled = ref[value_rows:ids_row, :] * jnp.asarray(0.5, ref.dtype)
            first = jnp.dot(left_ref[...], scaled, preferred_element_type=jnp.float32)
            second = jnp.dot(right_ref[...], scaled, preferred_element_type=jnp.float32)
            feat = (first + left_one) * (second + right_one) * weight * mask
            high = feat.astype(jnp.bfloat16)
            low = (feat - high.astype(jnp.float32)).astype(jnp.bfloat16)
            vals = ref[0:value_rows, :]
            state = state + lax.dot_general(high, vals, dims, preferred_element_type=jnp.float32)
            state = state + lax.dot_general(low, vals, dims, preferred_element_type=jnp.float32)
            normer = normer + lax.dot_general(
                ones, feat, dims, precision=exact_mode, preferred_element_type=jnp.float32
            )
        chosen = jnp.zeros((feature_rows, head_width), jnp.float32)
        for h in range(heads):
            chosen = jnp.where(head_of == h, state[:, h * head_width : (h + 1) * head_width], chosen)
        out_ref[...] = jnp.zeros(out_ref.shape, jnp.float32)
        out_ref[0:feature_rows, :] = chosen
        for k in range(normer_rows):
            stop = min(feature_rows, (k + 1) * head_width)
            out_ref[feature_rows + k : feature_rows + k + 1, 0 : stop - k * head_width] = normer[
                0:1, k * head_width : stop
            ]
        out_ref[key_row : key_row + 1, :] = jnp.broadcast_to(last, (1, head_width))

    return pl.pallas_call(
        kernel,
        out_shape=jax.ShapeDtypeStruct((out_rows, head_width), jnp.float32),
        interpret=INTERPRET,
    )(
        *pieces,
        jnp.asarray(big_left, jnp.bfloat16),
        jnp.asarray(big_right, jnp.bfloat16),
        jnp.asarray(aux),
    )


def features(entries):
    scaled = entries * 0.5
    left, right, left_one, right_one, weight = feature_tables(scaled.shape[-2])
    first = jnp.einsum("rk,...kt->...rt", left, scaled, precision=exact_mode) + left_one
    second = jnp.einsum("rk,...kt->...rt", right, scaled, precision=exact_mode) + right_one
    return first * second * weight


def block_output(q_feat, k_feat, head_values, doc_ids, carry_mask, state_in, normer_in):
    length = doc_ids.shape[0]
    causal = jnp.arange(length)[:, None] >= jnp.arange(length)[None, :]
    allowed = (causal & (doc_ids[:, None] == doc_ids[None, :])).astype(jnp.float32)
    scores = jnp.einsum("hft,hfs->hts", q_feat, k_feat, precision=split_mode) * allowed[None, :, :]
    numerator = jnp.einsum("hts,shd->thd", scores, head_values, precision=split_mode)
    numerator = numerator + carry_mask[:, None, None] * jnp.einsum(
        "hft,hfd->thd", q_feat, state_in, precision=split_mode
    )
    denominator = jnp.sum(scores, axis=2).T + carry_mask[:, None] * jnp.einsum(
        "hft,hf->th", q_feat, normer_in, precision=split_mode
    )
    return numerator / denominator[:, :, None]


def packed_join(key_row):
    def join(earlier, later):
        empty_later = later[key_row : key_row + 1] == 0.0
        same_doc = earlier[key_row : key_row + 1] == later[key_row : key_row + 1]
        row = lax.broadcasted_iota(jnp.int32, later.shape, 0)
        addend = jnp.where(same_doc & (row < key_row), earlier, 0.0)
        return jnp.where(empty_later, earlier, later + addend)

    return join


def pack(state, normer, key, edge):
    lanes = state.shape[-1]
    state_rows = state.reshape(-1, lanes)
    normer_flat = normer.reshape(-1)
    normer_rows = -(-normer_flat.size // lanes)
    normer_part = jnp.pad(normer_flat, (0, normer_rows * lanes - normer_flat.size))
    key_part = jnp.broadcast_to(key, (1, lanes))
    edge_rows = -(-edge.size // lanes)
    edge_part = jnp.pad(edge, (0, edge_rows * lanes - edge.size)).reshape(edge_rows, lanes)
    rows = state_rows.shape[0] + normer_rows + 1 + edge_rows
    tail = -rows % 8
    return jnp.concatenate(
        [
            state_rows,
            normer_part.reshape(normer_rows, lanes),
            key_part,
            edge_part,
            jnp.zeros((tail, lanes), state.dtype),
        ]
    )


def unpack(packed, state_shape, normer_shape, edge_size):
    lanes = state_shape[-1]
    state_rows = int(np.prod(state_shape[:-1]))
    normer_size = int(np.prod(normer_shape))
    key_row = state_rows + -(-normer_size // lanes)
    state = packed[:state_rows].reshape(state_shape)
    normer = packed[state_rows:key_row].reshape(-1)[:normer_size].reshape(normer_shape)
    edge_rows = -(-edge_size // lanes)
    edge = packed[key_row + 1 : key_row + 1 + edge_rows].reshape(-1)[:edge_size]
    return state, normer, edge


def body(queries, keys, values, seg_ids, conv_weight, out_weight, out_grad):
    local_heads = queries.shape[0] // FD
    length = queries.shape[1]
    head_width = values.shape[1] // local_heads
    reach = -(-(MOST - 1) // length)
    grad_attn = lax.dot_general(
        gather_columns(out_grad, "head"),
        out_weight,
        (((1,), (1,)), ((), ())),
        preferred_element_type=jnp.float32,
    )
    doc_ids = (seg_ids + 1).astype(jnp.float32)
    query_rows = queries.astype(jnp.float32)
    key_heads = keys.astype(jnp.float32).reshape(local_heads, FD, length)
    head_values = values.astype(jnp.float32).reshape(length, local_heads, head_width)
    taps = conv_weight.astype(jnp.float32)
    row_count = query_rows.shape[0]
    near, far = window_steps(reach, lax.axis_size("ctx"))
    raw = raw_pack(keys, values, doc_ids, queries[:, length - 2 :].reshape(-1))
    feature_count = 1 + 2 * FD + FD * (FD - 1) // 2
    state_shape = (local_heads, feature_count, head_width)
    normer_shape = (local_heads, feature_count)
    key_row = local_heads * feature_count + -(-local_heads * feature_count // head_width)
    out_rows = key_row + 2 + (-(key_row + 2) % 8)
    received = [shifted(raw, "ctx", step, False) for step in near]
    forward_piece = window_state(
        received + [raw],
        local_heads,
        FD,
        values.shape[1],
        out_rows,
    )
    key_late, forward_piece = lax.optimization_barrier((key_heads, forward_piece))
    k_feat, feature_pullback = jax.vjp(features, key_late)
    join = packed_join(key_row)
    packed = fold(join, [shifted(forward_piece, "ctx", step, False) for step in far])
    state_in, normer_in, _ = unpack(packed, state_shape, normer_shape, 1)
    previous = raw_unpack(received[-1], values.shape[1], row_count, 2 * row_count)
    before = (
        previous[2][length - 2 :],
        previous[3].astype(jnp.float32).reshape(row_count, 2),
        state_in,
        normer_in,
    )
    query_ext = jnp.concatenate([before[1], query_rows], axis=1)
    ids_before = jnp.concatenate([before[0], doc_ids])
    q_conv = taps[0][:, None] * query_rows
    for offset in (1, 2):
        same_doc = (ids_before[2 - offset : 2 - offset + length] == doc_ids).astype(jnp.float32)
        q_conv = (
            q_conv
            + taps[offset][:, None]
            * query_ext[:, 2 - offset : 2 - offset + length]
            * same_doc[None, :]
        )
    carry_mask = (doc_ids == before[0][1]).astype(jnp.float32)

    def local_forward(q_conv_in, k_feat_in, values_in, state_in, normer_in):
        q_feat = features(q_conv_in.reshape(local_heads, FD, length))
        result = block_output(
            q_feat, k_feat_in, values_in, doc_ids, carry_mask, state_in, normer_in
        )
        return result.reshape(length, local_heads * head_width)

    _, local_pullback = jax.vjp(local_forward, q_conv, k_feat, head_values, before[2], before[3])
    grad_qconv, grad_kfeat, grad_heads, grad_state, grad_normer = local_pullback(grad_attn)
    backward_piece = pack(
        grad_state,
        grad_normer,
        doc_ids[0],
        jnp.concatenate([doc_ids[:2], grad_qconv[:, :2].reshape(-1)]),
    )
    packed = entering(backward_piece, "ctx", packed_join(key_row), True, reach)
    state_out, normer_out, edge = unpack(packed, grad_state.shape, grad_normer.shape, 2 + 2 * row_count)
    after = (edge[:2], edge[2:].reshape(row_count, 2), state_out, normer_out)
    head_mask = (doc_ids == after[0][0]).astype(jnp.float32)
    flowing = (
        jnp.einsum("hfd,shd->hfs", after[2], head_values, precision=split_mode)
        + after[3][:, :, None]
    )
    grad_kfeat = grad_kfeat + flowing * head_mask[None, None, :]
    grad_heads = grad_heads + jnp.einsum(
        "hfs,hfd->shd", k_feat * head_mask[None, None, :], after[2], precision=split_mode
    )
    (grad_key_heads,) = feature_pullback(grad_kfeat)
    grad_ext = jnp.concatenate([grad_qconv, after[1]], axis=1)
    ids_after = jnp.concatenate([doc_ids, after[0]])
    grad_queries = taps[0][:, None] * grad_qconv
    for offset in (1, 2):
        same_doc = (ids_after[offset : offset + length] == doc_ids).astype(jnp.float32)
        grad_queries = (
            grad_queries
            + taps[offset][:, None] * grad_ext[:, offset : offset + length] * same_doc[None, :]
        )
    grad_keys = grad_key_heads.reshape(local_heads * FD, length)
    grad_values = grad_heads.reshape(length, local_heads * head_width)
    return (grad_queries, grad_keys, grad_values)


def solution(mesh):
    in_specs = (
        P("head", "ctx"),
        P("head", "ctx"),
        P("ctx", "head"),
        P("ctx"),
        P(None, "head"),
        P("head", None),
        P("ctx", "head"),
    )
    out_specs = (P("head", "ctx"), P("head", "ctx"), P("ctx", "head"))
    return jax.shard_map(body, mesh=mesh, in_specs=in_specs, out_specs=out_specs, check_vma=False)
```

```python
import jax
import jax.numpy as jnp
import numpy as np
from jax import lax
from jax.sharding import PartitionSpec as P
from jax.experimental import pallas as pl
from jax.experimental.pallas import tpu as pltpu

FD = 16
MOST = 2048
INTERPRET = False


half_root = 0.7071067811865476
split_mode = lax.Precision.HIGH
exact_mode = lax.Precision.HIGHEST


def shifted(piece, axis, step, reverse):
    size = lax.axis_size(axis)
    if reverse:
        pairs = [(source, source - step) for source in range(step, size)]
    else:
        pairs = [(source, source + step) for source in range(size - step)]
    return lax.ppermute(piece, axis, pairs)


def fold(combine, pieces):
    total = pieces[0]
    for piece in pieces[1:]:
        total = combine(total, piece)
    return total


def window_steps(reach, size):
    fan = 1
    while fan * fan < reach:
        fan += 1
    near = [step for step in range(fan - 1, 0, -1) if step < size]
    far = [1 + fan * k for k in range(-(-reach // fan) - 1, -1, -1)]
    return near, [step for step in far if step < size]


def entering(shard, axis, combine, reverse, reach):
    size = lax.axis_size(axis)
    near, far = window_steps(reach, size)
    total = shard
    step = 1
    while step <= len(near):
        total = combine(shifted(total, axis, step, reverse), total)
        step *= 2
    return fold(combine, [shifted(total, axis, step, reverse) for step in far])


def rows_of(flat, lanes):
    count = -(-flat.size // lanes)
    return jnp.pad(flat, (0, count * lanes - flat.size)).reshape(count, lanes)


def raw_pack(keys, values, doc_ids, edge):
    lanes = keys.shape[1]
    parts = [values.T, keys, doc_ids.astype(keys.dtype)[None, :], rows_of(edge, lanes)]
    rows = sum(part.shape[0] for part in parts)
    parts.append(jnp.zeros((-rows % 16, lanes), keys.dtype))
    return jnp.concatenate(parts)


def raw_unpack(packed, value_rows, key_rows, edge_size):
    lanes = packed.shape[1]
    ids_row = value_rows + key_rows
    edge_rows = -(-edge_size // lanes)
    return (
        packed[:value_rows],
        packed[value_rows:ids_row],
        packed[ids_row].astype(jnp.float32),
        packed[ids_row + 1 : ids_row + 1 + edge_rows].reshape(-1)[:edge_size],
    )


def feature_tables(width):
    count = 1 + 2 * width + width * (width - 1) // 2
    left = np.zeros((count, width), np.float32)
    right = np.zeros((count, width), np.float32)
    left_one = np.zeros((count, 1), np.float32)
    right_one = np.zeros((count, 1), np.float32)
    weight = np.ones((count, 1), np.float32)
    left_one[0] = 1.0
    right_one[0] = 1.0
    for i in range(width):
        left[1 + i, i] = 1.0
        right_one[1 + i] = 1.0
        left[1 + width + i, i] = 1.0
        right[1 + width + i, i] = 1.0
        weight[1 + width + i] = half_root
    row_index, col_index = np.triu_indices(width, 1)
    for n, (i, j) in enumerate(zip(row_index, col_index)):
        left[1 + 2 * width + n, i] = 1.0
        right[1 + 2 * width + n, j] = 1.0
    return left, right, left_one, right_one, weight


def window_tables(heads, width):
    left, right, left_one, right_one, weight = feature_tables(width)
    count = left.shape[0]
    big_left = np.zeros((heads * count, heads * width), np.float32)
    big_right = np.zeros((heads * count, heads * width), np.float32)
    aux = np.zeros((heads * count, 128), np.float32)
    for h in range(heads):
        rows = slice(h * count, (h + 1) * count)
        big_left[rows, h * width : (h + 1) * width] = left
        big_right[rows, h * width : (h + 1) * width] = right
        aux[rows, 0:1] = left_one
        aux[rows, 1:2] = right_one
        aux[rows, 2:3] = weight
        aux[rows, 3] = h
    return big_left, big_right, aux


def window_state(pieces, heads, width, value_rows, out_rows):
    big_left, big_right, aux = window_tables(heads, width)
    feature_rows = big_left.shape[0]
    head_width = value_rows // heads
    key_rows = heads * width
    ids_row = value_rows + key_rows
    normer_rows = -(-feature_rows // head_width)
    key_row = feature_rows + normer_rows
    dims = (((1,), (1,)), ((), ()))

    def kernel(*refs):
        piece_refs = refs[: len(pieces)]
        left_ref, right_ref, aux_ref, out_ref = refs[len(pieces) :]
        own_ids = piece_refs[-1][ids_row : ids_row + 1, :].astype(jnp.float32)
        last = jnp.max(own_ids, axis=1, keepdims=True)
        block = aux_ref[...]
        left_one = block[:, 0:1]
        right_one = block[:, 1:2]
        weight = block[:, 2:3]
        head_of = block[:, 3:4]
        state = jnp.zeros((feature_rows, value_rows), jnp.float32)
        normer = jnp.zeros((8, feature_rows), jnp.float32)
        ones = jnp.ones((8, piece_refs[0].shape[1]), jnp.float32)
        for ref in piece_refs:
            ids = ref[ids_row : ids_row + 1, :].astype(jnp.float32)
            mask = (ids == last).astype(jnp.float32)
            scaled = ref[value_rows:ids_row, :] * jnp.asarray(0.5, ref.dtype)
            first = jnp.dot(left_ref[...], scaled, preferred_element_type=jnp.float32)
            second = jnp.dot(right_ref[...], scaled, preferred_element_type=jnp.float32)
            feat = (first + left_one) * (second + right_one) * weight * mask
            high = feat.astype(jnp.bfloat16)
            low = (feat - high.astype(jnp.float32)).astype(jnp.bfloat16)
            vals = ref[0:value_rows, :]
            state = state + lax.dot_general(high, vals, dims, preferred_element_type=jnp.float32)
            state = state + lax.dot_general(low, vals, dims, preferred_element_type=jnp.float32)
            normer = normer + lax.dot_general(
                ones, feat, dims, precision=exact_mode, preferred_element_type=jnp.float32
            )
        chosen = jnp.zeros((feature_rows, head_width), jnp.float32)
        for h in range(heads):
            chosen = jnp.where(head_of == h, state[:, h * head_width : (h + 1) * head_width], chosen)
        out_ref[...] = jnp.zeros(out_ref.shape, jnp.float32)
        out_ref[0:feature_rows, :] = chosen
        for k in range(normer_rows):
            stop = min(feature_rows, (k + 1) * head_width)
            out_ref[feature_rows + k : feature_rows + k + 1, 0 : stop - k * head_width] = normer[
                0:1, k * head_width : stop
            ]
        out_ref[key_row : key_row + 1, :] = jnp.broadcast_to(last, (1, head_width))

    return pl.pallas_call(
        kernel,
        out_shape=jax.ShapeDtypeStruct((out_rows, head_width), jnp.float32),
        interpret=INTERPRET,
    )(
        *pieces,
        jnp.asarray(big_left, jnp.bfloat16),
        jnp.asarray(big_right, jnp.bfloat16),
        jnp.asarray(aux),
    )


def features(entries):
    scaled = entries * 0.5
    left, right, left_one, right_one, weight = feature_tables(scaled.shape[-2])
    first = jnp.einsum("rk,...kt->...rt", left, scaled, precision=exact_mode) + left_one
    second = jnp.einsum("rk,...kt->...rt", right, scaled, precision=exact_mode) + right_one
    return first * second * weight


def block_output(q_feat, k_feat, head_values, doc_ids, carry_mask, state_in, normer_in):
    length = doc_ids.shape[0]
    causal = jnp.arange(length)[:, None] >= jnp.arange(length)[None, :]
    allowed = (causal & (doc_ids[:, None] == doc_ids[None, :])).astype(jnp.float32)
    scores = jnp.einsum("hft,hfs->hts", q_feat, k_feat, precision=split_mode) * allowed[None, :, :]
    numerator = jnp.einsum("hts,shd->thd", scores, head_values, precision=split_mode)
    numerator = numerator + carry_mask[:, None, None] * jnp.einsum(
        "hft,hfd->thd", q_feat, state_in, precision=split_mode
    )
    denominator = jnp.sum(scores, axis=2).T + carry_mask[:, None] * jnp.einsum(
        "hft,hf->th", q_feat, normer_in, precision=split_mode
    )
    return numerator / denominator[:, :, None]


def packed_join(key_row):
    def join(earlier, later):
        empty_later = later[key_row : key_row + 1] == 0.0
        same_doc = earlier[key_row : key_row + 1] == later[key_row : key_row + 1]
        row = lax.broadcasted_iota(jnp.int32, later.shape, 0)
        addend = jnp.where(same_doc & (row < key_row), earlier, 0.0)
        return jnp.where(empty_later, earlier, later + addend)

    return join


def pack(state, normer, key, edge):
    lanes = state.shape[-1]
    state_rows = state.reshape(-1, lanes)
    normer_flat = normer.reshape(-1)
    normer_rows = -(-normer_flat.size // lanes)
    normer_part = jnp.pad(normer_flat, (0, normer_rows * lanes - normer_flat.size))
    key_part = jnp.broadcast_to(key, (1, lanes))
    edge_rows = -(-edge.size // lanes)
    edge_part = jnp.pad(edge, (0, edge_rows * lanes - edge.size)).reshape(edge_rows, lanes)
    rows = state_rows.shape[0] + normer_rows + 1 + edge_rows
    tail = -rows % 8
    return jnp.concatenate(
        [
            state_rows,
            normer_part.reshape(normer_rows, lanes),
            key_part,
            edge_part,
            jnp.zeros((tail, lanes), state.dtype),
        ]
    )


def unpack(packed, state_shape, normer_shape, edge_size):
    lanes = state_shape[-1]
    state_rows = int(np.prod(state_shape[:-1]))
    normer_size = int(np.prod(normer_shape))
    key_row = state_rows + -(-normer_size // lanes)
    state = packed[:state_rows].reshape(state_shape)
    normer = packed[state_rows:key_row].reshape(-1)[:normer_size].reshape(normer_shape)
    edge_rows = -(-edge_size // lanes)
    edge = packed[key_row + 1 : key_row + 1 + edge_rows].reshape(-1)[:edge_size]
    return state, normer, edge


def body(queries, keys, values, seg_ids, conv_weight, out_weight, out_grad):
    local_heads = queries.shape[0] // FD
    length = queries.shape[1]
    head_width = values.shape[1] // local_heads
    reach = -(-(MOST - 1) // length)
    grad_attn = lax.dot_general(
        lax.all_gather(out_grad, "head", axis=1, tiled=True),
        out_weight,
        (((1,), (1,)), ((), ())),
        preferred_element_type=jnp.float32,
    )
    doc_ids = (seg_ids + 1).astype(jnp.float32)
    query_rows = queries.astype(jnp.float32)
    key_heads = keys.astype(jnp.float32).reshape(local_heads, FD, length)
    head_values = values.astype(jnp.float32).reshape(length, local_heads, head_width)
    taps = conv_weight.astype(jnp.float32)
    row_count = query_rows.shape[0]
    near, far = window_steps(reach, lax.axis_size("ctx"))
    raw = raw_pack(keys, values, doc_ids, queries[:, length - 2 :].reshape(-1))
    feature_count = 1 + 2 * FD + FD * (FD - 1) // 2
    state_shape = (local_heads, feature_count, head_width)
    normer_shape = (local_heads, feature_count)
    key_row = local_heads * feature_count + -(-local_heads * feature_count // head_width)
    out_rows = key_row + 2 + (-(key_row + 2) % 8)
    received = [shifted(raw, "ctx", step, False) for step in near]
    forward_piece = window_state(
        received + [raw],
        local_heads,
        FD,
        values.shape[1],
        out_rows,
    )
    key_late, forward_piece = lax.optimization_barrier((key_heads, forward_piece))
    k_feat, feature_pullback = jax.vjp(features, key_late)
    join = packed_join(key_row)
    packed = fold(join, [shifted(forward_piece, "ctx", step, False) for step in far])
    state_in, normer_in, _ = unpack(packed, state_shape, normer_shape, 1)
    previous = raw_unpack(received[-1], values.shape[1], row_count, 2 * row_count)
    before = (
        previous[2][length - 2 :],
        previous[3].astype(jnp.float32).reshape(row_count, 2),
        state_in,
        normer_in,
    )
    query_ext = jnp.concatenate([before[1], query_rows], axis=1)
    ids_before = jnp.concatenate([before[0], doc_ids])
    q_conv = taps[0][:, None] * query_rows
    for offset in (1, 2):
        same_doc = (ids_before[2 - offset : 2 - offset + length] == doc_ids).astype(jnp.float32)
        q_conv = (
            q_conv
            + taps[offset][:, None]
            * query_ext[:, 2 - offset : 2 - offset + length]
            * same_doc[None, :]
        )
    carry_mask = (doc_ids == before[0][1]).astype(jnp.float32)

    def local_forward(q_conv_in, k_feat_in, values_in, state_in, normer_in):
        q_feat = features(q_conv_in.reshape(local_heads, FD, length))
        result = block_output(
            q_feat, k_feat_in, values_in, doc_ids, carry_mask, state_in, normer_in
        )
        return result.reshape(length, local_heads * head_width)

    _, local_pullback = jax.vjp(local_forward, q_conv, k_feat, head_values, before[2], before[3])
    grad_qconv, grad_kfeat, grad_heads, grad_state, grad_normer = local_pullback(grad_attn)
    backward_piece = pack(
        grad_state,
        grad_normer,
        doc_ids[0],
        jnp.concatenate([doc_ids[:2], grad_qconv[:, :2].reshape(-1)]),
    )
    packed = entering(backward_piece, "ctx", packed_join(key_row), True, reach)
    state_out, normer_out, edge = unpack(packed, grad_state.shape, grad_normer.shape, 2 + 2 * row_count)
    after = (edge[:2], edge[2:].reshape(row_count, 2), state_out, normer_out)
    head_mask = (doc_ids == after[0][0]).astype(jnp.float32)
    flowing = (
        jnp.einsum("hfd,shd->hfs", after[2], head_values, precision=split_mode)
        + after[3][:, :, None]
    )
    grad_kfeat = grad_kfeat + flowing * head_mask[None, None, :]
    grad_heads = grad_heads + jnp.einsum(
        "hfs,hfd->shd", k_feat * head_mask[None, None, :], after[2], precision=split_mode
    )
    (grad_key_heads,) = feature_pullback(grad_kfeat)
    grad_ext = jnp.concatenate([grad_qconv, after[1]], axis=1)
    ids_after = jnp.concatenate([doc_ids, after[0]])
    grad_queries = taps[0][:, None] * grad_qconv
    for offset in (1, 2):
        same_doc = (ids_after[offset : offset + length] == doc_ids).astype(jnp.float32)
        grad_queries = (
            grad_queries
            + taps[offset][:, None] * grad_ext[:, offset : offset + length] * same_doc[None, :]
        )
    grad_keys = grad_key_heads.reshape(local_heads * FD, length)
    grad_values = grad_heads.reshape(length, local_heads * head_width)
    return (grad_queries, grad_keys, grad_values)


def solution(mesh):
    in_specs = (
        P("head", "ctx"),
        P("head", "ctx"),
        P("ctx", "head"),
        P("ctx"),
        P(None, "head"),
        P("head", None),
        P("ctx", "head"),
    )
    out_specs = (P("head", "ctx"), P("head", "ctx"), P("ctx", "head"))
    return jax.shard_map(body, mesh=mesh, in_specs=in_specs, out_specs=out_specs, check_vma=False)
```

```python
import jax
import jax.numpy as jnp
import numpy as np
from jax import lax
from jax.sharding import PartitionSpec as P
from jax.experimental import pallas as pl
from jax.experimental.pallas import tpu as pltpu

FD = 16
MOST = 2048
INTERPRET = False


half_root = 0.7071067811865476
split_mode = lax.Precision.HIGH
exact_mode = lax.Precision.HIGHEST


def shifted(piece, axis, step, reverse):
    size = lax.axis_size(axis)
    if reverse:
        pairs = [(source, source - step) for source in range(step, size)]
    else:
        pairs = [(source, source + step) for source in range(size - step)]
    return lax.ppermute(piece, axis, pairs)


def fold(combine, pieces):
    total = pieces[0]
    for piece in pieces[1:]:
        total = combine(total, piece)
    return total


def window_steps(reach, size):
    fan = 1
    while fan * fan < reach:
        fan += 1
    near = [step for step in range(fan - 1, 0, -1) if step < size]
    far = [1 + fan * k for k in range(-(-reach // fan) - 1, -1, -1)]
    return near, [step for step in far if step < size]


def fold_kernel(key_row, pieces):
    def kernel(*refs):
        out_ref = refs[-1]
        total = refs[0][...]
        row = lax.broadcasted_iota(jnp.int32, total.shape, 0)
        for ref in refs[1:-1]:
            later = ref[...]
            empty_later = later[key_row : key_row + 1, :] == 0.0
            same_doc = total[key_row : key_row + 1, :] == later[key_row : key_row + 1, :]
            addend = jnp.where(same_doc & (row < key_row), total, 0.0)
            total = jnp.where(empty_later, total, later + addend)
        out_ref[...] = total

    return pl.pallas_call(
        kernel,
        out_shape=jax.ShapeDtypeStruct(pieces[0].shape, pieces[0].dtype),
        interpret=INTERPRET,
    )(*pieces)


def entering(shard, axis, key_row, reverse, reach):
    size = lax.axis_size(axis)
    near, far = window_steps(reach, size)
    total = shard
    step = 1
    while step <= len(near):
        total = fold_kernel(key_row, [shifted(total, axis, step, reverse), total])
        step *= 2
    return fold_kernel(key_row, [shifted(total, axis, step, reverse) for step in far])


def rows_of(flat, lanes):
    count = -(-flat.size // lanes)
    return jnp.pad(flat, (0, count * lanes - flat.size)).reshape(count, lanes)


def raw_pack(keys, values, doc_ids, edge):
    lanes = keys.shape[1]
    parts = [values.T, keys, doc_ids.astype(keys.dtype)[None, :], rows_of(edge, lanes)]
    rows = sum(part.shape[0] for part in parts)
    parts.append(jnp.zeros((-rows % 16, lanes), keys.dtype))
    return jnp.concatenate(parts)


def raw_unpack(packed, value_rows, key_rows, edge_size):
    lanes = packed.shape[1]
    ids_row = value_rows + key_rows
    edge_rows = -(-edge_size // lanes)
    return (
        packed[:value_rows],
        packed[value_rows:ids_row],
        packed[ids_row].astype(jnp.float32),
        packed[ids_row + 1 : ids_row + 1 + edge_rows].reshape(-1)[:edge_size],
    )


def feature_tables(width):
    count = 1 + 2 * width + width * (width - 1) // 2
    left = np.zeros((count, width), np.float32)
    right = np.zeros((count, width), np.float32)
    left_one = np.zeros((count, 1), np.float32)
    right_one = np.zeros((count, 1), np.float32)
    weight = np.ones((count, 1), np.float32)
    left_one[0] = 1.0
    right_one[0] = 1.0
    for i in range(width):
        left[1 + i, i] = 1.0
        right_one[1 + i] = 1.0
        left[1 + width + i, i] = 1.0
        right[1 + width + i, i] = 1.0
        weight[1 + width + i] = half_root
    row_index, col_index = np.triu_indices(width, 1)
    for n, (i, j) in enumerate(zip(row_index, col_index)):
        left[1 + 2 * width + n, i] = 1.0
        right[1 + 2 * width + n, j] = 1.0
    return left, right, left_one, right_one, weight


def window_tables(heads, width):
    left, right, left_one, right_one, weight = feature_tables(width)
    count = left.shape[0]
    big_left = np.zeros((heads * count, heads * width), np.float32)
    big_right = np.zeros((heads * count, heads * width), np.float32)
    aux = np.zeros((heads * count, 128), np.float32)
    for h in range(heads):
        rows = slice(h * count, (h + 1) * count)
        big_left[rows, h * width : (h + 1) * width] = left
        big_right[rows, h * width : (h + 1) * width] = right
        aux[rows, 0:1] = left_one
        aux[rows, 1:2] = right_one
        aux[rows, 2:3] = weight
        aux[rows, 3] = h
    return big_left, big_right, aux


def window_state(pieces, heads, width, value_rows, out_rows):
    big_left, big_right, aux = window_tables(heads, width)
    feature_rows = big_left.shape[0]
    head_width = value_rows // heads
    key_rows = heads * width
    ids_row = value_rows + key_rows
    normer_rows = -(-feature_rows // head_width)
    key_row = feature_rows + normer_rows
    dims = (((1,), (1,)), ((), ()))

    def kernel(*refs):
        piece_refs = refs[: len(pieces)]
        left_ref, right_ref, aux_ref, out_ref = refs[len(pieces) :]
        own_ids = piece_refs[-1][ids_row : ids_row + 1, :].astype(jnp.float32)
        last = jnp.max(own_ids, axis=1, keepdims=True)
        block = aux_ref[...]
        left_one = block[:, 0:1]
        right_one = block[:, 1:2]
        weight = block[:, 2:3]
        head_of = block[:, 3:4]
        state = jnp.zeros((feature_rows, value_rows), jnp.float32)
        normer = jnp.zeros((8, feature_rows), jnp.float32)
        ones = jnp.ones((8, piece_refs[0].shape[1]), jnp.float32)
        for ref in piece_refs:
            ids = ref[ids_row : ids_row + 1, :].astype(jnp.float32)
            mask = (ids == last).astype(jnp.float32)
            scaled = ref[value_rows:ids_row, :] * jnp.asarray(0.5, ref.dtype)
            first = jnp.dot(left_ref[...], scaled, preferred_element_type=jnp.float32)
            second = jnp.dot(right_ref[...], scaled, preferred_element_type=jnp.float32)
            feat = (first + left_one) * (second + right_one) * weight * mask
            high = feat.astype(jnp.bfloat16)
            low = (feat - high.astype(jnp.float32)).astype(jnp.bfloat16)
            vals = ref[0:value_rows, :]
            state = state + lax.dot_general(high, vals, dims, preferred_element_type=jnp.float32)
            state = state + lax.dot_general(low, vals, dims, preferred_element_type=jnp.float32)
            normer = normer + lax.dot_general(
                ones, feat, dims, precision=exact_mode, preferred_element_type=jnp.float32
            )
        chosen = jnp.zeros((feature_rows, head_width), jnp.float32)
        for h in range(heads):
            chosen = jnp.where(head_of == h, state[:, h * head_width : (h + 1) * head_width], chosen)
        out_ref[...] = jnp.zeros(out_ref.shape, jnp.float32)
        out_ref[0:feature_rows, :] = chosen
        for k in range(normer_rows):
            stop = min(feature_rows, (k + 1) * head_width)
            out_ref[feature_rows + k : feature_rows + k + 1, 0 : stop - k * head_width] = normer[
                0:1, k * head_width : stop
            ]
        out_ref[key_row : key_row + 1, :] = jnp.broadcast_to(last, (1, head_width))

    return pl.pallas_call(
        kernel,
        out_shape=jax.ShapeDtypeStruct((out_rows, head_width), jnp.float32),
        interpret=INTERPRET,
    )(
        *pieces,
        jnp.asarray(big_left, jnp.bfloat16),
        jnp.asarray(big_right, jnp.bfloat16),
        jnp.asarray(aux),
    )


def features(entries):
    scaled = entries * 0.5
    left, right, left_one, right_one, weight = feature_tables(scaled.shape[-2])
    first = jnp.einsum("rk,...kt->...rt", left, scaled, precision=exact_mode) + left_one
    second = jnp.einsum("rk,...kt->...rt", right, scaled, precision=exact_mode) + right_one
    return first * second * weight


def block_output(q_feat, k_feat, head_values, doc_ids, carry_mask, state_in, normer_in):
    length = doc_ids.shape[0]
    causal = jnp.arange(length)[:, None] >= jnp.arange(length)[None, :]
    allowed = (causal & (doc_ids[:, None] == doc_ids[None, :])).astype(jnp.float32)
    scores = jnp.einsum("hft,hfs->hts", q_feat, k_feat, precision=split_mode) * allowed[None, :, :]
    numerator = jnp.einsum("hts,shd->thd", scores, head_values, precision=split_mode)
    numerator = numerator + carry_mask[:, None, None] * jnp.einsum(
        "hft,hfd->thd", q_feat, state_in, precision=split_mode
    )
    denominator = jnp.sum(scores, axis=2).T + carry_mask[:, None] * jnp.einsum(
        "hft,hf->th", q_feat, normer_in, precision=split_mode
    )
    return numerator / denominator[:, :, None]


def packed_join(key_row):
    def join(earlier, later):
        empty_later = later[key_row : key_row + 1] == 0.0
        same_doc = earlier[key_row : key_row + 1] == later[key_row : key_row + 1]
        row = lax.broadcasted_iota(jnp.int32, later.shape, 0)
        addend = jnp.where(same_doc & (row < key_row), earlier, 0.0)
        return jnp.where(empty_later, earlier, later + addend)

    return join


def pack(state, normer, key, edge):
    lanes = state.shape[-1]
    state_rows = state.reshape(-1, lanes)
    normer_flat = normer.reshape(-1)
    normer_rows = -(-normer_flat.size // lanes)
    normer_part = jnp.pad(normer_flat, (0, normer_rows * lanes - normer_flat.size))
    key_part = jnp.broadcast_to(key, (1, lanes))
    edge_rows = -(-edge.size // lanes)
    edge_part = jnp.pad(edge, (0, edge_rows * lanes - edge.size)).reshape(edge_rows, lanes)
    rows = state_rows.shape[0] + normer_rows + 1 + edge_rows
    tail = -rows % 8
    return jnp.concatenate(
        [
            state_rows,
            normer_part.reshape(normer_rows, lanes),
            key_part,
            edge_part,
            jnp.zeros((tail, lanes), state.dtype),
        ]
    )


def unpack(packed, state_shape, normer_shape, edge_size):
    lanes = state_shape[-1]
    state_rows = int(np.prod(state_shape[:-1]))
    normer_size = int(np.prod(normer_shape))
    key_row = state_rows + -(-normer_size // lanes)
    state = packed[:state_rows].reshape(state_shape)
    normer = packed[state_rows:key_row].reshape(-1)[:normer_size].reshape(normer_shape)
    edge_rows = -(-edge_size // lanes)
    edge = packed[key_row + 1 : key_row + 1 + edge_rows].reshape(-1)[:edge_size]
    return state, normer, edge


def body(queries, keys, values, seg_ids, conv_weight, out_weight, out_grad):
    local_heads = queries.shape[0] // FD
    length = queries.shape[1]
    head_width = values.shape[1] // local_heads
    reach = -(-(MOST - 1) // length)
    grad_attn = lax.dot_general(
        lax.all_gather(out_grad, "head", axis=1, tiled=True),
        out_weight,
        (((1,), (1,)), ((), ())),
        preferred_element_type=jnp.float32,
    )
    doc_ids = (seg_ids + 1).astype(jnp.float32)
    query_rows = queries.astype(jnp.float32)
    key_heads = keys.astype(jnp.float32).reshape(local_heads, FD, length)
    head_values = values.astype(jnp.float32).reshape(length, local_heads, head_width)
    taps = conv_weight.astype(jnp.float32)
    row_count = query_rows.shape[0]
    near, far = window_steps(reach, lax.axis_size("ctx"))
    raw = raw_pack(keys, values, doc_ids, queries[:, length - 2 :].reshape(-1))
    feature_count = 1 + 2 * FD + FD * (FD - 1) // 2
    state_shape = (local_heads, feature_count, head_width)
    normer_shape = (local_heads, feature_count)
    key_row = local_heads * feature_count + -(-local_heads * feature_count // head_width)
    out_rows = key_row + 2 + (-(key_row + 2) % 8)
    received = [shifted(raw, "ctx", step, False) for step in near]
    forward_piece = window_state(
        received + [raw],
        local_heads,
        FD,
        values.shape[1],
        out_rows,
    )
    key_late, forward_piece = lax.optimization_barrier((key_heads, forward_piece))
    k_feat, feature_pullback = jax.vjp(features, key_late)
    packed = fold_kernel(key_row, [shifted(forward_piece, "ctx", step, False) for step in far])
    state_in, normer_in, _ = unpack(packed, state_shape, normer_shape, 1)
    previous = raw_unpack(received[-1], values.shape[1], row_count, 2 * row_count)
    before = (
        previous[2][length - 2 :],
        previous[3].astype(jnp.float32).reshape(row_count, 2),
        state_in,
        normer_in,
    )
    query_ext = jnp.concatenate([before[1], query_rows], axis=1)
    ids_before = jnp.concatenate([before[0], doc_ids])
    q_conv = taps[0][:, None] * query_rows
    for offset in (1, 2):
        same_doc = (ids_before[2 - offset : 2 - offset + length] == doc_ids).astype(jnp.float32)
        q_conv = (
            q_conv
            + taps[offset][:, None]
            * query_ext[:, 2 - offset : 2 - offset + length]
            * same_doc[None, :]
        )
    carry_mask = (doc_ids == before[0][1]).astype(jnp.float32)

    def local_forward(q_conv_in, k_feat_in, values_in, state_in, normer_in):
        q_feat = features(q_conv_in.reshape(local_heads, FD, length))
        result = block_output(
            q_feat, k_feat_in, values_in, doc_ids, carry_mask, state_in, normer_in
        )
        return result.reshape(length, local_heads * head_width)

    _, local_pullback = jax.vjp(local_forward, q_conv, k_feat, head_values, before[2], before[3])
    grad_qconv, grad_kfeat, grad_heads, grad_state, grad_normer = local_pullback(grad_attn)
    backward_piece = pack(
        grad_state,
        grad_normer,
        doc_ids[0],
        jnp.concatenate([doc_ids[:2], grad_qconv[:, :2].reshape(-1)]),
    )
    packed = entering(backward_piece, "ctx", key_row, True, reach)
    state_out, normer_out, edge = unpack(packed, grad_state.shape, grad_normer.shape, 2 + 2 * row_count)
    after = (edge[:2], edge[2:].reshape(row_count, 2), state_out, normer_out)
    head_mask = (doc_ids == after[0][0]).astype(jnp.float32)
    flowing = (
        jnp.einsum("hfd,shd->hfs", after[2], head_values, precision=split_mode)
        + after[3][:, :, None]
    )
    grad_kfeat = grad_kfeat + flowing * head_mask[None, None, :]
    grad_heads = grad_heads + jnp.einsum(
        "hfs,hfd->shd", k_feat * head_mask[None, None, :], after[2], precision=split_mode
    )
    (grad_key_heads,) = feature_pullback(grad_kfeat)
    grad_ext = jnp.concatenate([grad_qconv, after[1]], axis=1)
    ids_after = jnp.concatenate([doc_ids, after[0]])
    grad_queries = taps[0][:, None] * grad_qconv
    for offset in (1, 2):
        same_doc = (ids_after[offset : offset + length] == doc_ids).astype(jnp.float32)
        grad_queries = (
            grad_queries
            + taps[offset][:, None] * grad_ext[:, offset : offset + length] * same_doc[None, :]
        )
    grad_keys = grad_key_heads.reshape(local_heads * FD, length)
    grad_values = grad_heads.reshape(length, local_heads * head_width)
    return (grad_queries, grad_keys, grad_values)


def solution(mesh):
    in_specs = (
        P("head", "ctx"),
        P("head", "ctx"),
        P("ctx", "head"),
        P("ctx"),
        P(None, "head"),
        P("head", None),
        P("ctx", "head"),
    )
    out_specs = (P("head", "ctx"), P("head", "ctx"), P("ctx", "head"))
    return jax.shard_map(body, mesh=mesh, in_specs=in_specs, out_specs=out_specs, check_vma=False)
```

```python
import jax
import jax.numpy as jnp
import numpy as np
from jax import lax
from jax.sharding import PartitionSpec as P
from jax.experimental import pallas as pl
from jax.experimental.pallas import tpu as pltpu

FD = 16
MOST = 2048
INTERPRET = False


half_root = 0.7071067811865476
split_mode = lax.Precision.HIGH
exact_mode = lax.Precision.HIGHEST


def shifted(piece, axis, step, reverse):
    size = lax.axis_size(axis)
    if reverse:
        pairs = [(source, source - step) for source in range(step, size)]
    else:
        pairs = [(source, source + step) for source in range(size - step)]
    return lax.ppermute(piece, axis, pairs)


def fold(combine, pieces):
    total = pieces[0]
    for piece in pieces[1:]:
        total = combine(total, piece)
    return total


def window_steps(reach, size):
    fan = 1
    while fan * fan < reach:
        fan += 1
    near = [step for step in range(fan - 1, 0, -1) if step < size]
    far = [1 + fan * k for k in range(-(-reach // fan) - 1, -1, -1)]
    return near, [step for step in far if step < size]


def entering(shard, axis, combine, reverse, reach):
    size = lax.axis_size(axis)
    near, far = window_steps(reach, size)
    total = shard
    step = 1
    while step <= len(near):
        total = combine(shifted(total, axis, step, reverse), total)
        step *= 2
    return fold(combine, [shifted(total, axis, step, reverse) for step in far])


def rows_of(flat, lanes):
    count = -(-flat.size // lanes)
    return jnp.pad(flat, (0, count * lanes - flat.size)).reshape(count, lanes)


def raw_pack(keys, values, doc_ids, edge):
    lanes = keys.shape[1]
    parts = [values.T, keys, doc_ids.astype(keys.dtype)[None, :], rows_of(edge, lanes)]
    rows = sum(part.shape[0] for part in parts)
    parts.append(jnp.zeros((-rows % 16, lanes), keys.dtype))
    return jnp.concatenate(parts)


def raw_unpack(packed, value_rows, key_rows, edge_size):
    lanes = packed.shape[1]
    ids_row = value_rows + key_rows
    edge_rows = -(-edge_size // lanes)
    return (
        packed[:value_rows],
        packed[value_rows:ids_row],
        packed[ids_row].astype(jnp.float32),
        packed[ids_row + 1 : ids_row + 1 + edge_rows].reshape(-1)[:edge_size],
    )


def feature_tables(width):
    count = 1 + 2 * width + width * (width - 1) // 2
    left = np.zeros((count, width), np.float32)
    right = np.zeros((count, width), np.float32)
    left_one = np.zeros((count, 1), np.float32)
    right_one = np.zeros((count, 1), np.float32)
    weight = np.ones((count, 1), np.float32)
    left_one[0] = 1.0
    right_one[0] = 1.0
    for i in range(width):
        left[1 + i, i] = 1.0
        right_one[1 + i] = 1.0
        left[1 + width + i, i] = 1.0
        right[1 + width + i, i] = 1.0
        weight[1 + width + i] = half_root
    row_index, col_index = np.triu_indices(width, 1)
    for n, (i, j) in enumerate(zip(row_index, col_index)):
        left[1 + 2 * width + n, i] = 1.0
        right[1 + 2 * width + n, j] = 1.0
    return left, right, left_one, right_one, weight


def window_tables(heads, width):
    left, right, left_one, right_one, weight = feature_tables(width)
    count = left.shape[0]
    big_left = np.zeros((heads * count, heads * width), np.float32)
    big_right = np.zeros((heads * count, heads * width), np.float32)
    aux = np.zeros((heads * count, 128), np.float32)
    for h in range(heads):
        rows = slice(h * count, (h + 1) * count)
        big_left[rows, h * width : (h + 1) * width] = left
        big_right[rows, h * width : (h + 1) * width] = right
        aux[rows, 0:1] = left_one
        aux[rows, 1:2] = right_one
        aux[rows, 2:3] = weight
        aux[rows, 3] = h
    return big_left, big_right, aux


def window_state(pieces, heads, width, value_rows, out_rows):
    big_left, big_right, aux = window_tables(heads, width)
    feature_rows = big_left.shape[0]
    head_width = value_rows // heads
    key_rows = heads * width
    ids_row = value_rows + key_rows
    normer_rows = -(-feature_rows // head_width)
    key_row = feature_rows + normer_rows
    dims = (((1,), (1,)), ((), ()))

    def kernel(*refs):
        piece_refs = refs[: len(pieces)]
        left_ref, right_ref, aux_ref, out_ref = refs[len(pieces) :]
        own_ids = piece_refs[-1][ids_row : ids_row + 1, :].astype(jnp.float32)
        last = jnp.max(own_ids, axis=1, keepdims=True)
        block = aux_ref[...]
        left_one = block[:, 0:1]
        right_one = block[:, 1:2]
        weight = block[:, 2:3]
        head_of = block[:, 3:4]
        state = jnp.zeros((feature_rows, value_rows), jnp.float32)
        normer = jnp.zeros((8, feature_rows), jnp.float32)
        ones = jnp.ones((8, piece_refs[0].shape[1]), jnp.float32)
        for ref in piece_refs:
            ids = ref[ids_row : ids_row + 1, :].astype(jnp.float32)
            mask = (ids == last).astype(jnp.float32)
            scaled = ref[value_rows:ids_row, :] * jnp.asarray(0.5, ref.dtype)
            first = jnp.dot(left_ref[...], scaled, preferred_element_type=jnp.float32)
            second = jnp.dot(right_ref[...], scaled, preferred_element_type=jnp.float32)
            feat = (first + left_one) * (second + right_one) * weight * mask
            high = feat.astype(jnp.bfloat16)
            low = (feat - high.astype(jnp.float32)).astype(jnp.bfloat16)
            vals = ref[0:value_rows, :]
            state = state + lax.dot_general(high, vals, dims, preferred_element_type=jnp.float32)
            state = state + lax.dot_general(low, vals, dims, preferred_element_type=jnp.float32)
            normer = normer + lax.dot_general(
                ones, feat, dims, precision=exact_mode, preferred_element_type=jnp.float32
            )
        chosen = jnp.zeros((feature_rows, head_width), jnp.float32)
        for h in range(heads):
            chosen = jnp.where(head_of == h, state[:, h * head_width : (h + 1) * head_width], chosen)
        out_ref[...] = jnp.zeros(out_ref.shape, jnp.float32)
        out_ref[0:feature_rows, :] = chosen
        for k in range(normer_rows):
            stop = min(feature_rows, (k + 1) * head_width)
            out_ref[feature_rows + k : feature_rows + k + 1, 0 : stop - k * head_width] = normer[
                0:1, k * head_width : stop
            ]
        out_ref[key_row : key_row + 1, :] = jnp.broadcast_to(last, (1, head_width))

    return pl.pallas_call(
        kernel,
        out_shape=jax.ShapeDtypeStruct((out_rows, head_width), jnp.float32),
        interpret=INTERPRET,
    )(
        *pieces,
        jnp.asarray(big_left, jnp.bfloat16),
        jnp.asarray(big_right, jnp.bfloat16),
        jnp.asarray(aux),
    )


def features(entries):
    scaled = entries * 0.5
    left, right, left_one, right_one, weight = feature_tables(scaled.shape[-2])
    first = jnp.einsum("rk,...kt->...rt", left, scaled, precision=exact_mode) + left_one
    second = jnp.einsum("rk,...kt->...rt", right, scaled, precision=exact_mode) + right_one
    return first * second * weight


def block_output(q_feat, k_feat, head_values, doc_ids, carry_mask, state_in, normer_in):
    length = doc_ids.shape[0]
    causal = jnp.arange(length)[:, None] >= jnp.arange(length)[None, :]
    allowed = (causal & (doc_ids[:, None] == doc_ids[None, :])).astype(jnp.float32)
    scores = jnp.einsum("hft,hfs->hts", q_feat, k_feat, precision=split_mode) * allowed[None, :, :]
    numerator = jnp.einsum("hts,shd->thd", scores, head_values, precision=split_mode)
    numerator = numerator + carry_mask[:, None, None] * jnp.einsum(
        "hft,hfd->thd", q_feat, state_in, precision=split_mode
    )
    denominator = jnp.sum(scores, axis=2).T + carry_mask[:, None] * jnp.einsum(
        "hft,hf->th", q_feat, normer_in, precision=split_mode
    )
    return numerator / denominator[:, :, None]


def packed_join(key_row):
    def join(earlier, later):
        empty_later = later[key_row : key_row + 1] == 0.0
        same_doc = earlier[key_row : key_row + 1] == later[key_row : key_row + 1]
        row = lax.broadcasted_iota(jnp.int32, later.shape, 0)
        addend = jnp.where(same_doc & (row < key_row), earlier, 0.0)
        return jnp.where(empty_later, earlier, later + addend)

    return join


def pack(state, normer, key, edge):
    lanes = state.shape[-1]
    state_rows = state.reshape(-1, lanes)
    normer_flat = normer.reshape(-1)
    normer_rows = -(-normer_flat.size // lanes)
    normer_part = jnp.pad(normer_flat, (0, normer_rows * lanes - normer_flat.size))
    key_part = jnp.broadcast_to(key, (1, lanes))
    edge_rows = -(-edge.size // lanes)
    edge_part = jnp.pad(edge, (0, edge_rows * lanes - edge.size)).reshape(edge_rows, lanes)
    rows = state_rows.shape[0] + normer_rows + 1 + edge_rows
    tail = -rows % 8
    return jnp.concatenate(
        [
            state_rows,
            normer_part.reshape(normer_rows, lanes),
            key_part,
            edge_part,
            jnp.zeros((tail, lanes), state.dtype),
        ]
    )


def unpack(packed, state_shape, normer_shape, edge_size):
    lanes = state_shape[-1]
    state_rows = int(np.prod(state_shape[:-1]))
    normer_size = int(np.prod(normer_shape))
    key_row = state_rows + -(-normer_size // lanes)
    state = packed[:state_rows].reshape(state_shape)
    normer = packed[state_rows:key_row].reshape(-1)[:normer_size].reshape(normer_shape)
    edge_rows = -(-edge_size // lanes)
    edge = packed[key_row + 1 : key_row + 1 + edge_rows].reshape(-1)[:edge_size]
    return state, normer, edge


def body(queries, keys, values, seg_ids, conv_weight, out_weight, out_grad):
    local_heads = queries.shape[0] // FD
    length = queries.shape[1]
    head_width = values.shape[1] // local_heads
    reach = -(-(MOST - 1) // length)
    head_count = lax.axis_size("head")
    blocks = lax.all_to_all(
        jnp.broadcast_to(out_grad[None], (head_count,) + out_grad.shape), "head", 0, 0
    )
    grad_attn = lax.dot_general(
        blocks,
        out_weight.reshape(out_weight.shape[0], head_count, out_grad.shape[1]),
        (((0, 2), (1, 2)), ((), ())),
        preferred_element_type=jnp.float32,
    )
    doc_ids = (seg_ids + 1).astype(jnp.float32)
    query_rows = queries.astype(jnp.float32)
    key_heads = keys.astype(jnp.float32).reshape(local_heads, FD, length)
    head_values = values.astype(jnp.float32).reshape(length, local_heads, head_width)
    taps = conv_weight.astype(jnp.float32)
    row_count = query_rows.shape[0]
    near, far = window_steps(reach, lax.axis_size("ctx"))
    raw = raw_pack(keys, values, doc_ids, queries[:, length - 2 :].reshape(-1))
    feature_count = 1 + 2 * FD + FD * (FD - 1) // 2
    state_shape = (local_heads, feature_count, head_width)
    normer_shape = (local_heads, feature_count)
    key_row = local_heads * feature_count + -(-local_heads * feature_count // head_width)
    out_rows = key_row + 2 + (-(key_row + 2) % 8)
    received = [shifted(raw, "ctx", step, False) for step in near]
    forward_piece = window_state(
        received + [raw],
        local_heads,
        FD,
        values.shape[1],
        out_rows,
    )
    key_late, forward_piece = lax.optimization_barrier((key_heads, forward_piece))
    k_feat, feature_pullback = jax.vjp(features, key_late)
    join = packed_join(key_row)
    packed = fold(join, [shifted(forward_piece, "ctx", step, False) for step in far])
    state_in, normer_in, _ = unpack(packed, state_shape, normer_shape, 1)
    previous = raw_unpack(received[-1], values.shape[1], row_count, 2 * row_count)
    before = (
        previous[2][length - 2 :],
        previous[3].astype(jnp.float32).reshape(row_count, 2),
        state_in,
        normer_in,
    )
    query_ext = jnp.concatenate([before[1], query_rows], axis=1)
    ids_before = jnp.concatenate([before[0], doc_ids])
    q_conv = taps[0][:, None] * query_rows
    for offset in (1, 2):
        same_doc = (ids_before[2 - offset : 2 - offset + length] == doc_ids).astype(jnp.float32)
        q_conv = (
            q_conv
            + taps[offset][:, None]
            * query_ext[:, 2 - offset : 2 - offset + length]
            * same_doc[None, :]
        )
    carry_mask = (doc_ids == before[0][1]).astype(jnp.float32)

    def local_forward(q_conv_in, k_feat_in, values_in, state_in, normer_in):
        q_feat = features(q_conv_in.reshape(local_heads, FD, length))
        result = block_output(
            q_feat, k_feat_in, values_in, doc_ids, carry_mask, state_in, normer_in
        )
        return result.reshape(length, local_heads * head_width)

    _, local_pullback = jax.vjp(local_forward, q_conv, k_feat, head_values, before[2], before[3])
    grad_qconv, grad_kfeat, grad_heads, grad_state, grad_normer = local_pullback(grad_attn)
    backward_piece = pack(
        grad_state,
        grad_normer,
        doc_ids[0],
        jnp.concatenate([doc_ids[:2], grad_qconv[:, :2].reshape(-1)]),
    )
    packed = entering(backward_piece, "ctx", packed_join(key_row), True, reach)
    state_out, normer_out, edge = unpack(packed, grad_state.shape, grad_normer.shape, 2 + 2 * row_count)
    after = (edge[:2], edge[2:].reshape(row_count, 2), state_out, normer_out)
    head_mask = (doc_ids == after[0][0]).astype(jnp.float32)
    flowing = (
        jnp.einsum("hfd,shd->hfs", after[2], head_values, precision=split_mode)
        + after[3][:, :, None]
    )
    grad_kfeat = grad_kfeat + flowing * head_mask[None, None, :]
    grad_heads = grad_heads + jnp.einsum(
        "hfs,hfd->shd", k_feat * head_mask[None, None, :], after[2], precision=split_mode
    )
    (grad_key_heads,) = feature_pullback(grad_kfeat)
    grad_ext = jnp.concatenate([grad_qconv, after[1]], axis=1)
    ids_after = jnp.concatenate([doc_ids, after[0]])
    grad_queries = taps[0][:, None] * grad_qconv
    for offset in (1, 2):
        same_doc = (ids_after[offset : offset + length] == doc_ids).astype(jnp.float32)
        grad_queries = (
            grad_queries
            + taps[offset][:, None] * grad_ext[:, offset : offset + length] * same_doc[None, :]
        )
    grad_keys = grad_key_heads.reshape(local_heads * FD, length)
    grad_values = grad_heads.reshape(length, local_heads * head_width)
    return (grad_queries, grad_keys, grad_values)


def solution(mesh):
    in_specs = (
        P("head", "ctx"),
        P("head", "ctx"),
        P("ctx", "head"),
        P("ctx"),
        P(None, "head"),
        P("head", None),
        P("ctx", "head"),
    )
    out_specs = (P("head", "ctx"), P("head", "ctx"), P("ctx", "head"))
    return jax.shard_map(body, mesh=mesh, in_specs=in_specs, out_specs=out_specs, check_vma=False)
```

```python
import jax
import jax.numpy as jnp
import numpy as np
from jax import lax
from jax.sharding import PartitionSpec as P
from jax.experimental import pallas as pl
from jax.experimental.pallas import tpu as pltpu

FD = 16
MOST = 2048
INTERPRET = False


half_root = 0.7071067811865476
split_mode = lax.Precision.HIGH
exact_mode = lax.Precision.HIGHEST


def shifted(piece, axis, step, reverse):
    size = lax.axis_size(axis)
    if reverse:
        pairs = [(source, source - step) for source in range(step, size)]
    else:
        pairs = [(source, source + step) for source in range(size - step)]
    return lax.ppermute(piece, axis, pairs)


def fold(combine, pieces):
    total = pieces[0]
    for piece in pieces[1:]:
        total = combine(total, piece)
    return total


def window_steps(reach, size):
    fan = 1
    while fan * fan < reach:
        fan += 1
    near = [step for step in range(fan - 1, 0, -1) if step < size]
    far = [1 + fan * k for k in range(-(-reach // fan) - 1, -1, -1)]
    return near, [step for step in far if step < size]


def entering(shard, axis, combine, reverse, reach):
    size = lax.axis_size(axis)
    near, far = window_steps(reach, size)
    total = shard
    step = 1
    while step <= len(near):
        total = combine(shifted(total, axis, step, reverse), total)
        step *= 2
    return fold(combine, [shifted(total, axis, step, reverse) for step in far])


def rows_of(flat, lanes):
    count = -(-flat.size // lanes)
    return jnp.pad(flat, (0, count * lanes - flat.size)).reshape(count, lanes)


def raw_pack(keys, values, doc_ids, edge):
    lanes = keys.shape[1]
    parts = [values.T, keys, doc_ids.astype(keys.dtype)[None, :], rows_of(edge, lanes)]
    rows = sum(part.shape[0] for part in parts)
    parts.append(jnp.zeros((-rows % 16, lanes), keys.dtype))
    return jnp.concatenate(parts)


def raw_unpack(packed, value_rows, key_rows, edge_size):
    lanes = packed.shape[1]
    ids_row = value_rows + key_rows
    edge_rows = -(-edge_size // lanes)
    return (
        packed[:value_rows],
        packed[value_rows:ids_row],
        packed[ids_row].astype(jnp.float32),
        packed[ids_row + 1 : ids_row + 1 + edge_rows].reshape(-1)[:edge_size],
    )


def feature_tables(width):
    count = 1 + 2 * width + width * (width - 1) // 2
    left = np.zeros((count, width), np.float32)
    right = np.zeros((count, width), np.float32)
    left_one = np.zeros((count, 1), np.float32)
    right_one = np.zeros((count, 1), np.float32)
    weight = np.ones((count, 1), np.float32)
    left_one[0] = 1.0
    right_one[0] = 1.0
    for i in range(width):
        left[1 + i, i] = 1.0
        right_one[1 + i] = 1.0
        left[1 + width + i, i] = 1.0
        right[1 + width + i, i] = 1.0
        weight[1 + width + i] = half_root
    row_index, col_index = np.triu_indices(width, 1)
    for n, (i, j) in enumerate(zip(row_index, col_index)):
        left[1 + 2 * width + n, i] = 1.0
        right[1 + 2 * width + n, j] = 1.0
    return left, right, left_one, right_one, weight


def window_tables(heads, width):
    left, right, left_one, right_one, weight = feature_tables(width)
    count = left.shape[0]
    big_left = np.zeros((heads * count, heads * width), np.float32)
    big_right = np.zeros((heads * count, heads * width), np.float32)
    aux = np.zeros((heads * count, 128), np.float32)
    for h in range(heads):
        rows = slice(h * count, (h + 1) * count)
        big_left[rows, h * width : (h + 1) * width] = left
        big_right[rows, h * width : (h + 1) * width] = right
        aux[rows, 0:1] = left_one
        aux[rows, 1:2] = right_one
        aux[rows, 2:3] = weight
        aux[rows, 3] = h
    return big_left, big_right, aux


def window_state(pieces, heads, width, value_rows, out_rows):
    big_left, big_right, aux = window_tables(heads, width)
    feature_rows = big_left.shape[0]
    head_width = value_rows // heads
    key_rows = heads * width
    ids_row = value_rows + key_rows
    normer_rows = -(-feature_rows // head_width)
    key_row = feature_rows + normer_rows
    dims = (((1,), (1,)), ((), ()))

    def kernel(*refs):
        piece_refs = refs[: len(pieces)]
        left_ref, right_ref, aux_ref, out_ref = refs[len(pieces) :]
        own_ids = piece_refs[-1][ids_row : ids_row + 1, :].astype(jnp.float32)
        last = jnp.max(own_ids, axis=1, keepdims=True)
        block = aux_ref[...]
        left_one = block[:, 0:1]
        right_one = block[:, 1:2]
        weight = block[:, 2:3]
        head_of = block[:, 3:4]
        state = jnp.zeros((feature_rows, value_rows), jnp.float32)
        normer = jnp.zeros((8, feature_rows), jnp.float32)
        ones = jnp.ones((8, piece_refs[0].shape[1]), jnp.float32)
        for ref in piece_refs:
            ids = ref[ids_row : ids_row + 1, :].astype(jnp.float32)
            mask = (ids == last).astype(jnp.float32)
            scaled = ref[value_rows:ids_row, :] * jnp.asarray(0.5, ref.dtype)
            first = jnp.dot(left_ref[...], scaled, preferred_element_type=jnp.float32)
            second = jnp.dot(right_ref[...], scaled, preferred_element_type=jnp.float32)
            feat = (first + left_one) * (second + right_one) * weight * mask
            high = feat.astype(jnp.bfloat16)
            low = (feat - high.astype(jnp.float32)).astype(jnp.bfloat16)
            vals = ref[0:value_rows, :]
            state = state + lax.dot_general(high, vals, dims, preferred_element_type=jnp.float32)
            state = state + lax.dot_general(low, vals, dims, preferred_element_type=jnp.float32)
            normer = normer + lax.dot_general(
                ones, feat, dims, precision=exact_mode, preferred_element_type=jnp.float32
            )
        chosen = jnp.zeros((feature_rows, head_width), jnp.float32)
        for h in range(heads):
            chosen = jnp.where(head_of == h, state[:, h * head_width : (h + 1) * head_width], chosen)
        out_ref[...] = jnp.zeros(out_ref.shape, jnp.float32)
        out_ref[0:feature_rows, :] = chosen
        for k in range(normer_rows):
            stop = min(feature_rows, (k + 1) * head_width)
            out_ref[feature_rows + k : feature_rows + k + 1, 0 : stop - k * head_width] = normer[
                0:1, k * head_width : stop
            ]
        out_ref[key_row : key_row + 1, :] = jnp.broadcast_to(last, (1, head_width))

    return pl.pallas_call(
        kernel,
        out_shape=jax.ShapeDtypeStruct((out_rows, head_width), jnp.float32),
        interpret=INTERPRET,
    )(
        *pieces,
        jnp.asarray(big_left, jnp.bfloat16),
        jnp.asarray(big_right, jnp.bfloat16),
        jnp.asarray(aux),
    )


def features(entries):
    scaled = entries * 0.5
    left, right, left_one, right_one, weight = feature_tables(scaled.shape[-2])
    first = jnp.einsum("rk,...kt->...rt", left, scaled, precision=exact_mode) + left_one
    second = jnp.einsum("rk,...kt->...rt", right, scaled, precision=exact_mode) + right_one
    return first * second * weight


def block_output(q_feat, k_feat, head_values, doc_ids, carry_mask, state_in, normer_in):
    length = doc_ids.shape[0]
    causal = jnp.arange(length)[:, None] >= jnp.arange(length)[None, :]
    allowed = (causal & (doc_ids[:, None] == doc_ids[None, :])).astype(jnp.float32)
    scores = jnp.einsum("hft,hfs->hts", q_feat, k_feat, precision=split_mode) * allowed[None, :, :]
    numerator = jnp.einsum("hts,shd->thd", scores, head_values, precision=split_mode)
    numerator = numerator + carry_mask[:, None, None] * jnp.einsum(
        "hft,hfd->thd", q_feat, state_in, precision=split_mode
    )
    denominator = jnp.sum(scores, axis=2).T + carry_mask[:, None] * jnp.einsum(
        "hft,hf->th", q_feat, normer_in, precision=split_mode
    )
    return numerator / denominator[:, :, None]


def packed_join(key_row):
    def join(earlier, later):
        empty_later = later[key_row : key_row + 1] == 0.0
        same_doc = earlier[key_row : key_row + 1] == later[key_row : key_row + 1]
        row = lax.broadcasted_iota(jnp.int32, later.shape, 0)
        addend = jnp.where(same_doc & (row < key_row), earlier, 0.0)
        return jnp.where(empty_later, earlier, later + addend)

    return join


def pack(state, normer, key, edge):
    lanes = state.shape[-1]
    state_rows = state.reshape(-1, lanes)
    normer_flat = normer.reshape(-1)
    normer_rows = -(-normer_flat.size // lanes)
    normer_part = jnp.pad(normer_flat, (0, normer_rows * lanes - normer_flat.size))
    key_part = jnp.broadcast_to(key, (1, lanes))
    edge_rows = -(-edge.size // lanes)
    edge_part = jnp.pad(edge, (0, edge_rows * lanes - edge.size)).reshape(edge_rows, lanes)
    rows = state_rows.shape[0] + normer_rows + 1 + edge_rows
    tail = -rows % 8
    return jnp.concatenate(
        [
            state_rows,
            normer_part.reshape(normer_rows, lanes),
            key_part,
            edge_part,
            jnp.zeros((tail, lanes), state.dtype),
        ]
    )


def unpack(packed, state_shape, normer_shape, edge_size):
    lanes = state_shape[-1]
    state_rows = int(np.prod(state_shape[:-1]))
    normer_size = int(np.prod(normer_shape))
    key_row = state_rows + -(-normer_size // lanes)
    state = packed[:state_rows].reshape(state_shape)
    normer = packed[state_rows:key_row].reshape(-1)[:normer_size].reshape(normer_shape)
    edge_rows = -(-edge_size // lanes)
    edge = packed[key_row + 1 : key_row + 1 + edge_rows].reshape(-1)[:edge_size]
    return state, normer, edge


def body(queries, keys, values, seg_ids, conv_weight, out_weight, out_grad):
    local_heads = queries.shape[0] // FD
    length = queries.shape[1]
    head_width = values.shape[1] // local_heads
    reach = -(-(MOST - 1) // length)
    doc_ids = (seg_ids + 1).astype(jnp.float32)
    query_rows = queries.astype(jnp.float32)
    key_heads = keys.astype(jnp.float32).reshape(local_heads, FD, length)
    head_values = values.astype(jnp.float32).reshape(length, local_heads, head_width)
    taps = conv_weight.astype(jnp.float32)
    row_count = query_rows.shape[0]
    near, far = window_steps(reach, lax.axis_size("ctx"))
    raw = raw_pack(keys, values, doc_ids, queries[:, length - 2 :].reshape(-1))
    feature_count = 1 + 2 * FD + FD * (FD - 1) // 2
    state_shape = (local_heads, feature_count, head_width)
    normer_shape = (local_heads, feature_count)
    key_row = local_heads * feature_count + -(-local_heads * feature_count // head_width)
    out_rows = key_row + 2 + (-(key_row + 2) % 8)
    received = [shifted(raw, "ctx", step, False) for step in near]
    forward_piece = window_state(
        received + [raw],
        local_heads,
        FD,
        values.shape[1],
        out_rows,
    )
    key_late, grad_late, forward_piece = lax.optimization_barrier((key_heads, out_grad, forward_piece))
    head_count = lax.axis_size("head")
    blocks = lax.all_to_all(
        jnp.broadcast_to(grad_late[None], (head_count,) + grad_late.shape), "head", 0, 0
    )
    grad_attn = lax.dot_general(
        blocks,
        out_weight.reshape(out_weight.shape[0], head_count, grad_late.shape[1]),
        (((0, 2), (1, 2)), ((), ())),
        preferred_element_type=jnp.float32,
    )
    k_feat, feature_pullback = jax.vjp(features, key_late)
    join = packed_join(key_row)
    packed = fold(join, [shifted(forward_piece, "ctx", step, False) for step in far])
    state_in, normer_in, _ = unpack(packed, state_shape, normer_shape, 1)
    previous = raw_unpack(received[-1], values.shape[1], row_count, 2 * row_count)
    before = (
        previous[2][length - 2 :],
        previous[3].astype(jnp.float32).reshape(row_count, 2),
        state_in,
        normer_in,
    )
    query_ext = jnp.concatenate([before[1], query_rows], axis=1)
    ids_before = jnp.concatenate([before[0], doc_ids])
    q_conv = taps[0][:, None] * query_rows
    for offset in (1, 2):
        same_doc = (ids_before[2 - offset : 2 - offset + length] == doc_ids).astype(jnp.float32)
        q_conv = (
            q_conv
            + taps[offset][:, None]
            * query_ext[:, 2 - offset : 2 - offset + length]
            * same_doc[None, :]
        )
    carry_mask = (doc_ids == before[0][1]).astype(jnp.float32)

    def local_forward(q_conv_in, k_feat_in, values_in, state_in, normer_in):
        q_feat = features(q_conv_in.reshape(local_heads, FD, length))
        result = block_output(
            q_feat, k_feat_in, values_in, doc_ids, carry_mask, state_in, normer_in
        )
        return result.reshape(length, local_heads * head_width)

    _, local_pullback = jax.vjp(local_forward, q_conv, k_feat, head_values, before[2], before[3])
    grad_qconv, grad_kfeat, grad_heads, grad_state, grad_normer = local_pullback(grad_attn)
    backward_piece = pack(
        grad_state,
        grad_normer,
        doc_ids[0],
        jnp.concatenate([doc_ids[:2], grad_qconv[:, :2].reshape(-1)]),
    )
    packed = entering(backward_piece, "ctx", packed_join(key_row), True, reach)
    state_out, normer_out, edge = unpack(packed, grad_state.shape, grad_normer.shape, 2 + 2 * row_count)
    after = (edge[:2], edge[2:].reshape(row_count, 2), state_out, normer_out)
    head_mask = (doc_ids == after[0][0]).astype(jnp.float32)
    flowing = (
        jnp.einsum("hfd,shd->hfs", after[2], head_values, precision=split_mode)
        + after[3][:, :, None]
    )
    grad_kfeat = grad_kfeat + flowing * head_mask[None, None, :]
    grad_heads = grad_heads + jnp.einsum(
        "hfs,hfd->shd", k_feat * head_mask[None, None, :], after[2], precision=split_mode
    )
    (grad_key_heads,) = feature_pullback(grad_kfeat)
    grad_ext = jnp.concatenate([grad_qconv, after[1]], axis=1)
    ids_after = jnp.concatenate([doc_ids, after[0]])
    grad_queries = taps[0][:, None] * grad_qconv
    for offset in (1, 2):
        same_doc = (ids_after[offset : offset + length] == doc_ids).astype(jnp.float32)
        grad_queries = (
            grad_queries
            + taps[offset][:, None] * grad_ext[:, offset : offset + length] * same_doc[None, :]
        )
    grad_keys = grad_key_heads.reshape(local_heads * FD, length)
    grad_values = grad_heads.reshape(length, local_heads * head_width)
    return (grad_queries, grad_keys, grad_values)


def solution(mesh):
    in_specs = (
        P("head", "ctx"),
        P("head", "ctx"),
        P("ctx", "head"),
        P("ctx"),
        P(None, "head"),
        P("head", None),
        P("ctx", "head"),
    )
    out_specs = (P("head", "ctx"), P("head", "ctx"), P("ctx", "head"))
    return jax.shard_map(body, mesh=mesh, in_specs=in_specs, out_specs=out_specs, check_vma=False)
```

```python
import jax
import jax.numpy as jnp
import numpy as np
from jax import lax
from jax.sharding import PartitionSpec as P
from jax.experimental import pallas as pl
from jax.experimental.pallas import tpu as pltpu

FD = 16
MOST = 2048
INTERPRET = False


half_root = 0.7071067811865476
split_mode = lax.Precision.HIGH
exact_mode = lax.Precision.HIGHEST


def shifted(piece, axis, step, reverse):
    size = lax.axis_size(axis)
    if reverse:
        pairs = [(source, source - step) for source in range(step, size)]
    else:
        pairs = [(source, source + step) for source in range(size - step)]
    return lax.ppermute(piece, axis, pairs)


def fold(combine, pieces):
    total = pieces[0]
    for piece in pieces[1:]:
        total = combine(total, piece)
    return total


def window_steps(reach, size):
    fan = 1
    while fan * fan < reach:
        fan += 1
    near = [step for step in range(fan - 1, 0, -1) if step < size]
    far = [1 + fan * k for k in range(-(-reach // fan) - 1, -1, -1)]
    return near, [step for step in far if step < size]


def entering(shard, axis, combine, reverse, reach):
    size = lax.axis_size(axis)
    near, far = window_steps(reach, size)
    total = shard
    step = 1
    while step <= len(near):
        total = combine(shifted(total, axis, step, reverse), total)
        step *= 2
    return fold(combine, [shifted(total, axis, step, reverse) for step in far])


def rows_of(flat, lanes):
    count = -(-flat.size // lanes)
    return jnp.pad(flat, (0, count * lanes - flat.size)).reshape(count, lanes)


def raw_pack(keys, values, doc_ids, edge):
    lanes = keys.shape[1]
    parts = [values.T, keys, doc_ids.astype(keys.dtype)[None, :], rows_of(edge, lanes)]
    rows = sum(part.shape[0] for part in parts)
    parts.append(jnp.zeros((-rows % 16, lanes), keys.dtype))
    return jnp.concatenate(parts)


def raw_unpack(packed, value_rows, key_rows, edge_size):
    lanes = packed.shape[1]
    ids_row = value_rows + key_rows
    edge_rows = -(-edge_size // lanes)
    return (
        packed[:value_rows],
        packed[value_rows:ids_row],
        packed[ids_row].astype(jnp.float32),
        packed[ids_row + 1 : ids_row + 1 + edge_rows].reshape(-1)[:edge_size],
    )


def feature_tables(width):
    count = 1 + 2 * width + width * (width - 1) // 2
    left = np.zeros((count, width), np.float32)
    right = np.zeros((count, width), np.float32)
    left_one = np.zeros((count, 1), np.float32)
    right_one = np.zeros((count, 1), np.float32)
    weight = np.ones((count, 1), np.float32)
    left_one[0] = 1.0
    right_one[0] = 1.0
    for i in range(width):
        left[1 + i, i] = 1.0
        right_one[1 + i] = 1.0
        left[1 + width + i, i] = 1.0
        right[1 + width + i, i] = 1.0
        weight[1 + width + i] = half_root
    row_index, col_index = np.triu_indices(width, 1)
    for n, (i, j) in enumerate(zip(row_index, col_index)):
        left[1 + 2 * width + n, i] = 1.0
        right[1 + 2 * width + n, j] = 1.0
    return left, right, left_one, right_one, weight


def window_tables(heads, width):
    left, right, left_one, right_one, weight = feature_tables(width)
    count = left.shape[0]
    big_left = np.zeros((heads * count, heads * width), np.float32)
    big_right = np.zeros((heads * count, heads * width), np.float32)
    aux = np.zeros((heads * count, 128), np.float32)
    for h in range(heads):
        rows = slice(h * count, (h + 1) * count)
        big_left[rows, h * width : (h + 1) * width] = left
        big_right[rows, h * width : (h + 1) * width] = right
        aux[rows, 0:1] = left_one
        aux[rows, 1:2] = right_one
        aux[rows, 2:3] = weight
        aux[rows, 3] = h
    return big_left, big_right, aux


def window_state(pieces, heads, width, value_rows, out_rows):
    big_left, big_right, aux = window_tables(heads, width)
    feature_rows = big_left.shape[0]
    head_width = value_rows // heads
    key_rows = heads * width
    ids_row = value_rows + key_rows
    normer_rows = -(-feature_rows // head_width)
    key_row = feature_rows + normer_rows
    dims = (((1,), (1,)), ((), ()))

    def kernel(*refs):
        piece_refs = refs[: len(pieces)]
        left_ref, right_ref, aux_ref, out_ref = refs[len(pieces) :]
        own_ids = piece_refs[-1][ids_row : ids_row + 1, :].astype(jnp.float32)
        last = jnp.max(own_ids, axis=1, keepdims=True)
        block = aux_ref[...]
        left_one = block[:, 0:1]
        right_one = block[:, 1:2]
        weight = block[:, 2:3]
        head_of = block[:, 3:4]
        state = jnp.zeros((feature_rows, value_rows), jnp.float32)
        normer = jnp.zeros((8, feature_rows), jnp.float32)
        ones = jnp.ones((8, piece_refs[0].shape[1]), jnp.float32)
        for ref in piece_refs:
            ids = ref[ids_row : ids_row + 1, :].astype(jnp.float32)
            mask = (ids == last).astype(jnp.float32)
            scaled = ref[value_rows:ids_row, :] * jnp.asarray(0.5, ref.dtype)
            first = jnp.dot(left_ref[...], scaled, preferred_element_type=jnp.float32)
            second = jnp.dot(right_ref[...], scaled, preferred_element_type=jnp.float32)
            feat = (first + left_one) * (second + right_one) * weight * mask
            high = feat.astype(jnp.bfloat16)
            low = (feat - high.astype(jnp.float32)).astype(jnp.bfloat16)
            vals = ref[0:value_rows, :]
            state = state + lax.dot_general(high, vals, dims, preferred_element_type=jnp.float32)
            state = state + lax.dot_general(low, vals, dims, preferred_element_type=jnp.float32)
            normer = normer + lax.dot_general(
                ones, feat, dims, precision=exact_mode, preferred_element_type=jnp.float32
            )
        chosen = jnp.zeros((feature_rows, head_width), jnp.float32)
        for h in range(heads):
            chosen = jnp.where(head_of == h, state[:, h * head_width : (h + 1) * head_width], chosen)
        out_ref[...] = jnp.zeros(out_ref.shape, jnp.float32)
        out_ref[0:feature_rows, :] = chosen
        for k in range(normer_rows):
            stop = min(feature_rows, (k + 1) * head_width)
            out_ref[feature_rows + k : feature_rows + k + 1, 0 : stop - k * head_width] = normer[
                0:1, k * head_width : stop
            ]
        out_ref[key_row : key_row + 1, :] = jnp.broadcast_to(last, (1, head_width))

    return pl.pallas_call(
        kernel,
        out_shape=jax.ShapeDtypeStruct((out_rows, head_width), jnp.float32),
        interpret=INTERPRET,
    )(
        *pieces,
        jnp.asarray(big_left, jnp.bfloat16),
        jnp.asarray(big_right, jnp.bfloat16),
        jnp.asarray(aux),
    )


def features(entries):
    scaled = entries * 0.5
    left, right, left_one, right_one, weight = feature_tables(scaled.shape[-2])
    first = jnp.einsum("rk,...kt->...rt", left, scaled, precision=exact_mode) + left_one
    second = jnp.einsum("rk,...kt->...rt", right, scaled, precision=exact_mode) + right_one
    return first * second * weight


def block_output(q_feat, k_feat, head_values, doc_ids, carry_mask, state_in, normer_in):
    length = doc_ids.shape[0]
    causal = jnp.arange(length)[:, None] >= jnp.arange(length)[None, :]
    allowed = (causal & (doc_ids[:, None] == doc_ids[None, :])).astype(jnp.float32)
    scores = jnp.einsum("hft,hfs->hts", q_feat, k_feat, precision=split_mode) * allowed[None, :, :]
    numerator = jnp.einsum("hts,shd->thd", scores, head_values, precision=split_mode)
    numerator = numerator + carry_mask[:, None, None] * jnp.einsum(
        "hft,hfd->thd", q_feat, state_in, precision=split_mode
    )
    denominator = jnp.sum(scores, axis=2).T + carry_mask[:, None] * jnp.einsum(
        "hft,hf->th", q_feat, normer_in, precision=split_mode
    )
    return numerator / denominator[:, :, None]


def packed_join(key_row):
    def join(earlier, later):
        empty_later = later[key_row : key_row + 1] == 0.0
        same_doc = earlier[key_row : key_row + 1] == later[key_row : key_row + 1]
        row = lax.broadcasted_iota(jnp.int32, later.shape, 0)
        addend = jnp.where(same_doc & (row < key_row), earlier, 0.0)
        return jnp.where(empty_later, earlier, later + addend)

    return join


def pack(state, normer, key, edge):
    lanes = state.shape[-1]
    state_rows = state.reshape(-1, lanes)
    normer_flat = normer.reshape(-1)
    normer_rows = -(-normer_flat.size // lanes)
    normer_part = jnp.pad(normer_flat, (0, normer_rows * lanes - normer_flat.size))
    key_part = jnp.broadcast_to(key, (1, lanes))
    edge_rows = -(-edge.size // lanes)
    edge_part = jnp.pad(edge, (0, edge_rows * lanes - edge.size)).reshape(edge_rows, lanes)
    rows = state_rows.shape[0] + normer_rows + 1 + edge_rows
    tail = -rows % 8
    return jnp.concatenate(
        [
            state_rows,
            normer_part.reshape(normer_rows, lanes),
            key_part,
            edge_part,
            jnp.zeros((tail, lanes), state.dtype),
        ]
    )


def unpack(packed, state_shape, normer_shape, edge_size):
    lanes = state_shape[-1]
    state_rows = int(np.prod(state_shape[:-1]))
    normer_size = int(np.prod(normer_shape))
    key_row = state_rows + -(-normer_size // lanes)
    state = packed[:state_rows].reshape(state_shape)
    normer = packed[state_rows:key_row].reshape(-1)[:normer_size].reshape(normer_shape)
    edge_rows = -(-edge_size // lanes)
    edge = packed[key_row + 1 : key_row + 1 + edge_rows].reshape(-1)[:edge_size]
    return state, normer, edge


def body(queries, keys, values, seg_ids, conv_weight, out_weight, out_grad):
    local_heads = queries.shape[0] // FD
    length = queries.shape[1]
    head_width = values.shape[1] // local_heads
    reach = -(-(MOST - 1) // length)
    head_count = lax.axis_size("head")
    gathered = lax.all_to_all(
        jnp.broadcast_to(out_grad[None], (head_count,) + out_grad.shape), "head", 0, 2, tiled=True
    )
    grad_attn = lax.dot_general(
        gathered[0],
        out_weight,
        (((1,), (1,)), ((), ())),
        preferred_element_type=jnp.float32,
    )
    doc_ids = (seg_ids + 1).astype(jnp.float32)
    query_rows = queries.astype(jnp.float32)
    key_heads = keys.astype(jnp.float32).reshape(local_heads, FD, length)
    head_values = values.astype(jnp.float32).reshape(length, local_heads, head_width)
    taps = conv_weight.astype(jnp.float32)
    row_count = query_rows.shape[0]
    near, far = window_steps(reach, lax.axis_size("ctx"))
    raw = raw_pack(keys, values, doc_ids, queries[:, length - 2 :].reshape(-1))
    feature_count = 1 + 2 * FD + FD * (FD - 1) // 2
    state_shape = (local_heads, feature_count, head_width)
    normer_shape = (local_heads, feature_count)
    key_row = local_heads * feature_count + -(-local_heads * feature_count // head_width)
    out_rows = key_row + 2 + (-(key_row + 2) % 8)
    received = [shifted(raw, "ctx", step, False) for step in near]
    forward_piece = window_state(
        received + [raw],
        local_heads,
        FD,
        values.shape[1],
        out_rows,
    )
    key_late, forward_piece = lax.optimization_barrier((key_heads, forward_piece))
    k_feat, feature_pullback = jax.vjp(features, key_late)
    join = packed_join(key_row)
    packed = fold(join, [shifted(forward_piece, "ctx", step, False) for step in far])
    state_in, normer_in, _ = unpack(packed, state_shape, normer_shape, 1)
    previous = raw_unpack(received[-1], values.shape[1], row_count, 2 * row_count)
    before = (
        previous[2][length - 2 :],
        previous[3].astype(jnp.float32).reshape(row_count, 2),
        state_in,
        normer_in,
    )
    query_ext = jnp.concatenate([before[1], query_rows], axis=1)
    ids_before = jnp.concatenate([before[0], doc_ids])
    q_conv = taps[0][:, None] * query_rows
    for offset in (1, 2):
        same_doc = (ids_before[2 - offset : 2 - offset + length] == doc_ids).astype(jnp.float32)
        q_conv = (
            q_conv
            + taps[offset][:, None]
            * query_ext[:, 2 - offset : 2 - offset + length]
            * same_doc[None, :]
        )
    carry_mask = (doc_ids == before[0][1]).astype(jnp.float32)

    def local_forward(q_conv_in, k_feat_in, values_in, state_in, normer_in):
        q_feat = features(q_conv_in.reshape(local_heads, FD, length))
        result = block_output(
            q_feat, k_feat_in, values_in, doc_ids, carry_mask, state_in, normer_in
        )
        return result.reshape(length, local_heads * head_width)

    _, local_pullback = jax.vjp(local_forward, q_conv, k_feat, head_values, before[2], before[3])
    grad_qconv, grad_kfeat, grad_heads, grad_state, grad_normer = local_pullback(grad_attn)
    backward_piece = pack(
        grad_state,
        grad_normer,
        doc_ids[0],
        jnp.concatenate([doc_ids[:2], grad_qconv[:, :2].reshape(-1)]),
    )
    packed = entering(backward_piece, "ctx", packed_join(key_row), True, reach)
    state_out, normer_out, edge = unpack(packed, grad_state.shape, grad_normer.shape, 2 + 2 * row_count)
    after = (edge[:2], edge[2:].reshape(row_count, 2), state_out, normer_out)
    head_mask = (doc_ids == after[0][0]).astype(jnp.float32)
    flowing = (
        jnp.einsum("hfd,shd->hfs", after[2], head_values, precision=split_mode)
        + after[3][:, :, None]
    )
    grad_kfeat = grad_kfeat + flowing * head_mask[None, None, :]
    grad_heads = grad_heads + jnp.einsum(
        "hfs,hfd->shd", k_feat * head_mask[None, None, :], after[2], precision=split_mode
    )
    (grad_key_heads,) = feature_pullback(grad_kfeat)
    grad_ext = jnp.concatenate([grad_qconv, after[1]], axis=1)
    ids_after = jnp.concatenate([doc_ids, after[0]])
    grad_queries = taps[0][:, None] * grad_qconv
    for offset in (1, 2):
        same_doc = (ids_after[offset : offset + length] == doc_ids).astype(jnp.float32)
        grad_queries = (
            grad_queries
            + taps[offset][:, None] * grad_ext[:, offset : offset + length] * same_doc[None, :]
        )
    grad_keys = grad_key_heads.reshape(local_heads * FD, length)
    grad_values = grad_heads.reshape(length, local_heads * head_width)
    return (grad_queries, grad_keys, grad_values)


def solution(mesh):
    in_specs = (
        P("head", "ctx"),
        P("head", "ctx"),
        P("ctx", "head"),
        P("ctx"),
        P(None, "head"),
        P("head", None),
        P("ctx", "head"),
    )
    out_specs = (P("head", "ctx"), P("head", "ctx"), P("ctx", "head"))
    return jax.shard_map(body, mesh=mesh, in_specs=in_specs, out_specs=out_specs, check_vma=False)
```

```python
import jax
import jax.numpy as jnp
import numpy as np
from jax import lax
from jax.sharding import PartitionSpec as P
from jax.experimental import pallas as pl
from jax.experimental.pallas import tpu as pltpu

FD = 16
MOST = 2048
INTERPRET = False


half_root = 0.7071067811865476
split_mode = lax.Precision.HIGH
exact_mode = lax.Precision.HIGHEST


def shifted(piece, axis, step, reverse):
    size = lax.axis_size(axis)
    if reverse:
        pairs = [(source, source - step) for source in range(step, size)]
    else:
        pairs = [(source, source + step) for source in range(size - step)]
    return lax.ppermute(piece, axis, pairs)


def fold(combine, pieces):
    total = pieces[0]
    for piece in pieces[1:]:
        total = combine(total, piece)
    return total


def window_steps(reach, size):
    fan = 1
    while fan * fan < reach:
        fan += 1
    near = [step for step in range(fan - 1, 0, -1) if step < size]
    far = [1 + fan * k for k in range(-(-reach // fan) - 1, -1, -1)]
    return near, [step for step in far if step < size]


def entering(shard, axis, combine, reverse, reach):
    size = lax.axis_size(axis)
    near, far = window_steps(reach, size)
    total = shard
    step = 1
    while step * 2 < reach and step < size:
        total = combine(shifted(total, axis, step, reverse), total)
        step *= 2
    far = [1 + step * k for k in range(-(-reach // step) - 1, -1, -1)]
    far = [each for each in far if each < size]
    return fold(combine, [shifted(total, axis, each, reverse) for each in far])


def rows_of(flat, lanes):
    count = -(-flat.size // lanes)
    return jnp.pad(flat, (0, count * lanes - flat.size)).reshape(count, lanes)


def raw_pack(keys, values, doc_ids, edge):
    lanes = keys.shape[1]
    parts = [values.T, keys, doc_ids.astype(keys.dtype)[None, :], rows_of(edge, lanes)]
    rows = sum(part.shape[0] for part in parts)
    parts.append(jnp.zeros((-rows % 16, lanes), keys.dtype))
    return jnp.concatenate(parts)


def raw_unpack(packed, value_rows, key_rows, edge_size):
    lanes = packed.shape[1]
    ids_row = value_rows + key_rows
    edge_rows = -(-edge_size // lanes)
    return (
        packed[:value_rows],
        packed[value_rows:ids_row],
        packed[ids_row].astype(jnp.float32),
        packed[ids_row + 1 : ids_row + 1 + edge_rows].reshape(-1)[:edge_size],
    )


def feature_tables(width):
    count = 1 + 2 * width + width * (width - 1) // 2
    left = np.zeros((count, width), np.float32)
    right = np.zeros((count, width), np.float32)
    left_one = np.zeros((count, 1), np.float32)
    right_one = np.zeros((count, 1), np.float32)
    weight = np.ones((count, 1), np.float32)
    left_one[0] = 1.0
    right_one[0] = 1.0
    for i in range(width):
        left[1 + i, i] = 1.0
        right_one[1 + i] = 1.0
        left[1 + width + i, i] = 1.0
        right[1 + width + i, i] = 1.0
        weight[1 + width + i] = half_root
    row_index, col_index = np.triu_indices(width, 1)
    for n, (i, j) in enumerate(zip(row_index, col_index)):
        left[1 + 2 * width + n, i] = 1.0
        right[1 + 2 * width + n, j] = 1.0
    return left, right, left_one, right_one, weight


def window_tables(heads, width):
    left, right, left_one, right_one, weight = feature_tables(width)
    count = left.shape[0]
    big_left = np.zeros((heads * count, heads * width), np.float32)
    big_right = np.zeros((heads * count, heads * width), np.float32)
    aux = np.zeros((heads * count, 128), np.float32)
    for h in range(heads):
        rows = slice(h * count, (h + 1) * count)
        big_left[rows, h * width : (h + 1) * width] = left
        big_right[rows, h * width : (h + 1) * width] = right
        aux[rows, 0:1] = left_one
        aux[rows, 1:2] = right_one
        aux[rows, 2:3] = weight
        aux[rows, 3] = h
    return big_left, big_right, aux


def window_state(pieces, heads, width, value_rows, out_rows):
    big_left, big_right, aux = window_tables(heads, width)
    feature_rows = big_left.shape[0]
    head_width = value_rows // heads
    key_rows = heads * width
    ids_row = value_rows + key_rows
    normer_rows = -(-feature_rows // head_width)
    key_row = feature_rows + normer_rows
    dims = (((1,), (1,)), ((), ()))

    def kernel(*refs):
        piece_refs = refs[: len(pieces)]
        left_ref, right_ref, aux_ref, out_ref = refs[len(pieces) :]
        own_ids = piece_refs[-1][ids_row : ids_row + 1, :].astype(jnp.float32)
        last = jnp.max(own_ids, axis=1, keepdims=True)
        block = aux_ref[...]
        left_one = block[:, 0:1]
        right_one = block[:, 1:2]
        weight = block[:, 2:3]
        head_of = block[:, 3:4]
        state = jnp.zeros((feature_rows, value_rows), jnp.float32)
        normer = jnp.zeros((8, feature_rows), jnp.float32)
        ones = jnp.ones((8, piece_refs[0].shape[1]), jnp.float32)
        for ref in piece_refs:
            ids = ref[ids_row : ids_row + 1, :].astype(jnp.float32)
            mask = (ids == last).astype(jnp.float32)
            scaled = ref[value_rows:ids_row, :] * jnp.asarray(0.5, ref.dtype)
            first = jnp.dot(left_ref[...], scaled, preferred_element_type=jnp.float32)
            second = jnp.dot(right_ref[...], scaled, preferred_element_type=jnp.float32)
            feat = (first + left_one) * (second + right_one) * weight * mask
            high = feat.astype(jnp.bfloat16)
            low = (feat - high.astype(jnp.float32)).astype(jnp.bfloat16)
            vals = ref[0:value_rows, :]
            state = state + lax.dot_general(high, vals, dims, preferred_element_type=jnp.float32)
            state = state + lax.dot_general(low, vals, dims, preferred_element_type=jnp.float32)
            normer = normer + lax.dot_general(
                ones, feat, dims, precision=exact_mode, preferred_element_type=jnp.float32
            )
        chosen = jnp.zeros((feature_rows, head_width), jnp.float32)
        for h in range(heads):
            chosen = jnp.where(head_of == h, state[:, h * head_width : (h + 1) * head_width], chosen)
        out_ref[...] = jnp.zeros(out_ref.shape, jnp.float32)
        out_ref[0:feature_rows, :] = chosen
        for k in range(normer_rows):
            stop = min(feature_rows, (k + 1) * head_width)
            out_ref[feature_rows + k : feature_rows + k + 1, 0 : stop - k * head_width] = normer[
                0:1, k * head_width : stop
            ]
        out_ref[key_row : key_row + 1, :] = jnp.broadcast_to(last, (1, head_width))

    return pl.pallas_call(
        kernel,
        out_shape=jax.ShapeDtypeStruct((out_rows, head_width), jnp.float32),
        interpret=INTERPRET,
    )(
        *pieces,
        jnp.asarray(big_left, jnp.bfloat16),
        jnp.asarray(big_right, jnp.bfloat16),
        jnp.asarray(aux),
    )


def features(entries):
    scaled = entries * 0.5
    left, right, left_one, right_one, weight = feature_tables(scaled.shape[-2])
    first = jnp.einsum("rk,...kt->...rt", left, scaled, precision=exact_mode) + left_one
    second = jnp.einsum("rk,...kt->...rt", right, scaled, precision=exact_mode) + right_one
    return first * second * weight


def block_output(q_feat, k_feat, head_values, doc_ids, carry_mask, state_in, normer_in):
    length = doc_ids.shape[0]
    causal = jnp.arange(length)[:, None] >= jnp.arange(length)[None, :]
    allowed = (causal & (doc_ids[:, None] == doc_ids[None, :])).astype(jnp.float32)
    scores = jnp.einsum("hft,hfs->hts", q_feat, k_feat, precision=split_mode) * allowed[None, :, :]
    numerator = jnp.einsum("hts,shd->thd", scores, head_values, precision=split_mode)
    numerator = numerator + carry_mask[:, None, None] * jnp.einsum(
        "hft,hfd->thd", q_feat, state_in, precision=split_mode
    )
    denominator = jnp.sum(scores, axis=2).T + carry_mask[:, None] * jnp.einsum(
        "hft,hf->th", q_feat, normer_in, precision=split_mode
    )
    return numerator / denominator[:, :, None]


def packed_join(key_row):
    def join(earlier, later):
        empty_later = later[key_row : key_row + 1] == 0.0
        same_doc = earlier[key_row : key_row + 1] == later[key_row : key_row + 1]
        row = lax.broadcasted_iota(jnp.int32, later.shape, 0)
        addend = jnp.where(same_doc & (row < key_row), earlier, 0.0)
        return jnp.where(empty_later, earlier, later + addend)

    return join


def pack(state, normer, key, edge):
    lanes = state.shape[-1]
    state_rows = state.reshape(-1, lanes)
    normer_flat = normer.reshape(-1)
    normer_rows = -(-normer_flat.size // lanes)
    normer_part = jnp.pad(normer_flat, (0, normer_rows * lanes - normer_flat.size))
    key_part = jnp.broadcast_to(key, (1, lanes))
    edge_rows = -(-edge.size // lanes)
    edge_part = jnp.pad(edge, (0, edge_rows * lanes - edge.size)).reshape(edge_rows, lanes)
    rows = state_rows.shape[0] + normer_rows + 1 + edge_rows
    tail = -rows % 8
    return jnp.concatenate(
        [
            state_rows,
            normer_part.reshape(normer_rows, lanes),
            key_part,
            edge_part,
            jnp.zeros((tail, lanes), state.dtype),
        ]
    )


def unpack(packed, state_shape, normer_shape, edge_size):
    lanes = state_shape[-1]
    state_rows = int(np.prod(state_shape[:-1]))
    normer_size = int(np.prod(normer_shape))
    key_row = state_rows + -(-normer_size // lanes)
    state = packed[:state_rows].reshape(state_shape)
    normer = packed[state_rows:key_row].reshape(-1)[:normer_size].reshape(normer_shape)
    edge_rows = -(-edge_size // lanes)
    edge = packed[key_row + 1 : key_row + 1 + edge_rows].reshape(-1)[:edge_size]
    return state, normer, edge


def body(queries, keys, values, seg_ids, conv_weight, out_weight, out_grad):
    local_heads = queries.shape[0] // FD
    length = queries.shape[1]
    head_width = values.shape[1] // local_heads
    reach = -(-(MOST - 1) // length)
    head_count = lax.axis_size("head")
    blocks = lax.all_to_all(
        jnp.broadcast_to(out_grad[None], (head_count,) + out_grad.shape), "head", 0, 0
    )
    grad_attn = lax.dot_general(
        blocks,
        out_weight.reshape(out_weight.shape[0], head_count, out_grad.shape[1]),
        (((0, 2), (1, 2)), ((), ())),
        preferred_element_type=jnp.float32,
    )
    doc_ids = (seg_ids + 1).astype(jnp.float32)
    query_rows = queries.astype(jnp.float32)
    key_heads = keys.astype(jnp.float32).reshape(local_heads, FD, length)
    head_values = values.astype(jnp.float32).reshape(length, local_heads, head_width)
    taps = conv_weight.astype(jnp.float32)
    row_count = query_rows.shape[0]
    near, far = window_steps(reach, lax.axis_size("ctx"))
    raw = raw_pack(keys, values, doc_ids, queries[:, length - 2 :].reshape(-1))
    feature_count = 1 + 2 * FD + FD * (FD - 1) // 2
    state_shape = (local_heads, feature_count, head_width)
    normer_shape = (local_heads, feature_count)
    key_row = local_heads * feature_count + -(-local_heads * feature_count // head_width)
    out_rows = key_row + 2 + (-(key_row + 2) % 8)
    received = [shifted(raw, "ctx", step, False) for step in near]
    forward_piece = window_state(
        received + [raw],
        local_heads,
        FD,
        values.shape[1],
        out_rows,
    )
    key_late, forward_piece = lax.optimization_barrier((key_heads, forward_piece))
    k_feat, feature_pullback = jax.vjp(features, key_late)
    join = packed_join(key_row)
    packed = fold(join, [shifted(forward_piece, "ctx", step, False) for step in far])
    state_in, normer_in, _ = unpack(packed, state_shape, normer_shape, 1)
    previous = raw_unpack(received[-1], values.shape[1], row_count, 2 * row_count)
    before = (
        previous[2][length - 2 :],
        previous[3].astype(jnp.float32).reshape(row_count, 2),
        state_in,
        normer_in,
    )
    query_ext = jnp.concatenate([before[1], query_rows], axis=1)
    ids_before = jnp.concatenate([before[0], doc_ids])
    q_conv = taps[0][:, None] * query_rows
    for offset in (1, 2):
        same_doc = (ids_before[2 - offset : 2 - offset + length] == doc_ids).astype(jnp.float32)
        q_conv = (
            q_conv
            + taps[offset][:, None]
            * query_ext[:, 2 - offset : 2 - offset + length]
            * same_doc[None, :]
        )
    carry_mask = (doc_ids == before[0][1]).astype(jnp.float32)

    def local_forward(q_conv_in, k_feat_in, values_in, state_in, normer_in):
        q_feat = features(q_conv_in.reshape(local_heads, FD, length))
        result = block_output(
            q_feat, k_feat_in, values_in, doc_ids, carry_mask, state_in, normer_in
        )
        return result.reshape(length, local_heads * head_width)

    _, local_pullback = jax.vjp(local_forward, q_conv, k_feat, head_values, before[2], before[3])
    grad_qconv, grad_kfeat, grad_heads, grad_state, grad_normer = local_pullback(grad_attn)
    backward_piece = pack(
        grad_state,
        grad_normer,
        doc_ids[0],
        jnp.concatenate([doc_ids[:2], grad_qconv[:, :2].reshape(-1)]),
    )
    packed = entering(backward_piece, "ctx", packed_join(key_row), True, reach)
    state_out, normer_out, edge = unpack(packed, grad_state.shape, grad_normer.shape, 2 + 2 * row_count)
    after = (edge[:2], edge[2:].reshape(row_count, 2), state_out, normer_out)
    head_mask = (doc_ids == after[0][0]).astype(jnp.float32)
    flowing = (
        jnp.einsum("hfd,shd->hfs", after[2], head_values, precision=split_mode)
        + after[3][:, :, None]
    )
    grad_kfeat = grad_kfeat + flowing * head_mask[None, None, :]
    grad_heads = grad_heads + jnp.einsum(
        "hfs,hfd->shd", k_feat * head_mask[None, None, :], after[2], precision=split_mode
    )
    (grad_key_heads,) = feature_pullback(grad_kfeat)
    grad_ext = jnp.concatenate([grad_qconv, after[1]], axis=1)
    ids_after = jnp.concatenate([doc_ids, after[0]])
    grad_queries = taps[0][:, None] * grad_qconv
    for offset in (1, 2):
        same_doc = (ids_after[offset : offset + length] == doc_ids).astype(jnp.float32)
        grad_queries = (
            grad_queries
            + taps[offset][:, None] * grad_ext[:, offset : offset + length] * same_doc[None, :]
        )
    grad_keys = grad_key_heads.reshape(local_heads * FD, length)
    grad_values = grad_heads.reshape(length, local_heads * head_width)
    return (grad_queries, grad_keys, grad_values)


def solution(mesh):
    in_specs = (
        P("head", "ctx"),
        P("head", "ctx"),
        P("ctx", "head"),
        P("ctx"),
        P(None, "head"),
        P("head", None),
        P("ctx", "head"),
    )
    out_specs = (P("head", "ctx"), P("head", "ctx"), P("ctx", "head"))
    return jax.shard_map(body, mesh=mesh, in_specs=in_specs, out_specs=out_specs, check_vma=False)
```
